32 devices in a mesh: groups: 2 (over y), sec: 4 (over x, core), plane: 4 (over z).
Axes of the slice: x: 2, y: 2, z: 4, core: 2. Of those that a mesh axis runs over, the one named last changes fastest.
Arguments:
- tokens: bfloat16 [16, 512, 1024], P(('groups', 'sec'), 'plane'), parts along dimension 0, may hold values from -8 to 8
- counts: int32 [16], P('groups'), parts along dimension 0, may hold values from 128 to 512, as said below
- region_ids: int32 [16, 512], P(('groups', 'sec'), 'plane'), parts along dimension 0, may hold values from 0 to 31
- norm_gains: float32 [2, 1024], replicated, may hold values from 0.1 to 1.9
- cross_qkv: bfloat16 [1024, 3072], P('plane'), may hold values from -2 to 2
- cross_out: bfloat16 [1024, 1024], P('plane'), may hold values from -0.1875 to 0.1875
- plane_qkv: bfloat16 [1024, 3072], P('plane'), may hold values from -2 to 2
- plane_out: bfloat16 [1024, 1024], P('plane'), may hold values from -0.1875 to 0.1875
Outputs:
- encoded: bfloat16 [16, 512, 1024], P(('groups', 'sec'), 'plane'), parts along dimension 0
- pooled: float32 [64, 1024], P(('groups', 'sec', 'plane')), parts along dimension 0
The draws below stay inside these ranges and needn't reach their ends.
There are 2 independent parts, one for each index of `groups`. The reference program is written for one: setup_inputs(seed, part) draws one part's arguments, and reference() takes and returns one part's arrays. A program takes and returns all parts, laid end to end along the dimension named above; an argument that names none is the same for every part. Nothing has to cross between parts.
Inputs may be any that keep to these rules, and one draw needn't show every extreme that they name: `counts`: valid tissue tokens of each section; they are the first positions of the section.
All inputs are finite; a program needn't handle non-finite values.
Results may differ from the reference program's by a relative error of at most 0.009.
Values may be sent and summed in bfloat16 or wider, within the bound.
No kernel may reach another device: no remote copies, remote signals or barrier semaphores. Data moves between devices by JAX's collectives and lax.ppermute only.
A program may use at most 64 MiB of HBM per device.

```python
import math
import jax
import jax.numpy as jnp
from jax import lax

D = 1024
HEADS = 16
HEAD_DIM = 64
WINDOW = 128
SEC_DEV = 2
TOK_DEV = 128
SECTIONS = 8
SEC_TOKENS = 512
REGIONS = 32


def clipped_normal(key, shape, bound):
    return jnp.clip(jax.random.normal(key, shape, jnp.float32), -bound, bound)


def draw_tokens(key, part):
    key = jax.random.fold_in(key, 13)
    first_key = jax.random.fold_in(key, 0)
    shape = (SECTIONS, SEC_TOKENS, D)
    return clipped_normal(first_key, shape, 6.0).astype(jnp.bfloat16)


def projection_draw(key):
    first_key = jax.random.fold_in(key, 0)
    base = clipped_normal(first_key, (D, 3 * D), 4.0) / math.sqrt(D)
    column_scale = jnp.concatenate([jnp.full((2 * D,), 1.6, jnp.float32), jnp.ones((D,), jnp.float32)])
    weights = base * column_scale[None, :]
    return jnp.clip(weights, -2.0, 2.0)


def draw_cross_qkv(key, part):
    return projection_draw(jax.random.fold_in(key, 11)).astype(jnp.bfloat16)


def draw_plane_qkv(key, part):
    return projection_draw(jax.random.fold_in(key, 12)).astype(jnp.bfloat16)


def draw_counts(key, part):
    key = jax.random.fold_in(key, 14)
    first_key, second_key, third_key = jax.random.split(key, 3)
    base = SEC_TOKENS - jax.random.randint(first_key, (SECTIONS,), 0, SEC_TOKENS - TOK_DEV + 1)
    short_block = jax.random.randint(second_key, (), 0, SECTIONS // SEC_DEV)
    full_section = (short_block * SEC_DEV + SEC_DEV + jax.random.randint(third_key, (), 0, SECTIONS - SEC_DEV)) % SECTIONS
    section_index = jnp.arange(SECTIONS, dtype=jnp.int32)
    base = jnp.where(section_index // SEC_DEV == short_block, TOK_DEV, base)
    base = jnp.where(section_index == full_section, SEC_TOKENS, base)
    return base.astype(jnp.int32)


def draw_region_ids(key, part):
    key = jax.random.fold_in(key, 15)
    first_key, second_key, third_key, fourth_key, fifth_key = jax.random.split(key, 5)
    tiles = SEC_TOKENS // TOK_DEV
    offsets = jax.random.randint(first_key, (SECTIONS, 1), 0, TOK_DEV)
    positions = jnp.arange(SEC_TOKENS, dtype=jnp.int32)[None, :]
    tile_index = (positions + offsets) // TOK_DEV % tiles
    block_index = jnp.arange(SECTIONS, dtype=jnp.int32)[:, None] // SEC_DEV
    halves = jax.random.randint(second_key, (SECTIONS, SEC_TOKENS), 0, 2)
    cells = (block_index * tiles + tile_index) * 2 + halves
    mapping = jax.random.permutation(third_key, 2 * (SECTIONS // SEC_DEV) * tiles).astype(jnp.int32)
    local_label = mapping[cells]
    scattered_label = jax.random.randint(fifth_key, (SECTIONS, SEC_TOKENS), 0, REGIONS)
    pick_scattered = jax.random.randint(fourth_key, (SECTIONS, SEC_TOKENS), 0, 2)
    return jnp.where(pick_scattered == 1, scattered_label, local_label).astype(jnp.int32)


def block_scale(key, shape, pieces, smallest, largest):
    loudness = 1.0
    for dim, blocks in pieces:
        draws = jax.random.uniform(jax.random.fold_in(jax.random.fold_in(key, 6), dim), (blocks,), jnp.float32, smallest / len(pieces), largest / len(pieces))
        loudness = loudness * jnp.repeat(jnp.exp(draws), shape[dim] // blocks).reshape((-1,) + (1,) * (len(shape) - 1 - dim))
    return loudness


def bell_draw(key, shape, width, most, shards=(), kind=jnp.bfloat16):
    values = jax.random.normal(key, shape, jnp.float32) * width
    if len(shards) > 0:
        values = block_scale(key, shape, shards, -0.22, 0.18) * values
    return jnp.clip(values, min=-most, max=most).astype(kind)


def setup_inputs(seed: int = 0, part: int = 0) -> dict:
    streams_of = jax.random.split(jax.random.key(seed), 9)
    part_keys = jax.random.split(jax.random.fold_in(streams_of[8], part), 9)
    tokens = draw_tokens(jax.random.fold_in(jax.random.fold_in(streams_of[8], part), 71), part)
    counts = draw_counts(jax.random.fold_in(jax.random.fold_in(streams_of[8], part), 71), part)
    region_ids = draw_region_ids(jax.random.fold_in(jax.random.fold_in(streams_of[8], part), 71), part)
    norm_gains = jnp.clip(1.0 + 0.18 * jax.random.normal(streams_of[3], (2, D), jnp.float32), 0.1, 1.9)
    cross_qkv = draw_cross_qkv(jax.random.fold_in(streams_of[8], 71), part)
    cross_out = bell_draw(streams_of[5], (D, D), D ** -0.5, 0.1875, ((0, 4),))
    plane_qkv = draw_plane_qkv(jax.random.fold_in(streams_of[8], 71), part)
    plane_out = bell_draw(streams_of[7], (D, D), D ** -0.5, 0.1875, ((0, 4),))
    return {"tokens": tokens, "counts": counts, "region_ids": region_ids, "norm_gains": norm_gains, "cross_qkv": cross_qkv, "cross_out": cross_out, "plane_qkv": plane_qkv, "plane_out": plane_out}


negative_big = -1e+30

def rms_norm(values, gain):
    wide = values.astype(jnp.float32)
    scaled = wide * lax.rsqrt(lax.optimization_barrier(jnp.mean(wide * wide, axis=-1, keepdims=True)) + 1e-06) * gain
    return scaled.astype(jnp.bfloat16)

def masked_softmax(scores, allowed):
    shifted = jnp.where(allowed, scores, negative_big)
    top = lax.optimization_barrier(jnp.max(shifted, axis=-1, keepdims=True))
    expo = jnp.where(allowed, jnp.exp(shifted - top), 0.0)
    return (expo / lax.optimization_barrier(jnp.sum(expo, axis=-1, keepdims=True))).astype(jnp.bfloat16)

def reference(tokens, counts, region_ids, norm_gains, cross_qkv, cross_out, plane_qkv, plane_out):
    score_scale = 1.0 / math.sqrt(HEAD_DIM)
    positions = jnp.arange(SEC_TOKENS, dtype=jnp.int32)
    valid = positions[None, :] < counts[:, None]
    flat_tokens = tokens.reshape(SECTIONS * SEC_TOKENS, D)
    normed = rms_norm(flat_tokens, norm_gains[0])
    projected = jnp.dot(normed, cross_qkv, preferred_element_type=jnp.float32).astype(jnp.bfloat16)
    projected = projected.reshape(SECTIONS, SEC_TOKENS, 3 * D)
    windows = SEC_TOKENS // WINDOW
    zero_pair = jnp.zeros((1, SEC_TOKENS, 2 * D), jnp.bfloat16)
    padded_kv = jnp.concatenate([zero_pair, projected[:, :, D:], zero_pair], axis=0)
    padded_valid = jnp.concatenate([jnp.zeros((1, SEC_TOKENS), bool), valid, jnp.zeros((1, SEC_TOKENS), bool)], axis=0)
    itself = jnp.arange(3 * WINDOW)[None, :] == jnp.arange(WINDOW)[:, None] + WINDOW

    def cross_section(section):
        query = lax.dynamic_slice_in_dim(projected, section, 1, 0)[0, :, :D]
        query = query.reshape(windows, WINDOW, HEADS, HEAD_DIM).astype(jnp.float32)
        near = lax.dynamic_slice_in_dim(padded_kv, section, 3, 0).reshape(3, windows, WINDOW, 2, HEADS, HEAD_DIM)
        near = jnp.transpose(near, (1, 0, 2, 3, 4, 5)).reshape(windows, 3 * WINDOW, 2, HEADS, HEAD_DIM).astype(jnp.float32)
        near_valid = lax.dynamic_slice_in_dim(padded_valid, section, 3, 0).reshape(3, windows, WINDOW)
        near_valid = jnp.transpose(near_valid, (1, 0, 2)).reshape(windows, 3 * WINDOW)
        scores = jnp.einsum('nqhd,nkhd->nhqk', query, near[:, :, 0]) * score_scale
        allowed = near_valid[:, None, None, :] | itself[None, None]
        attention = masked_softmax(scores, allowed).astype(jnp.float32)
        context = jnp.einsum('nhqk,nkhd->nqhd', attention, near[:, :, 1])
        return context.astype(jnp.bfloat16).reshape(SEC_TOKENS, D)
    context = lax.map(cross_section, jnp.arange(SECTIONS, dtype=jnp.int32)).reshape(SECTIONS * SEC_TOKENS, D)
    after_cross = (flat_tokens.astype(jnp.float32) + jnp.dot(context, cross_out, preferred_element_type=jnp.float32)).astype(jnp.bfloat16)
    normed = rms_norm(after_cross, norm_gains[1])
    projected = jnp.dot(normed, plane_qkv, preferred_element_type=jnp.float32).astype(jnp.bfloat16)
    projected = projected.reshape(SECTIONS, SEC_TOKENS, 3, HEADS, HEAD_DIM)
    items = jnp.transpose(projected, (0, 3, 1, 2, 4)).reshape(SECTIONS * HEADS, SEC_TOKENS, 3, HEAD_DIM)
    item_valid = jnp.broadcast_to(valid[:, None, :], (SECTIONS, HEADS, SEC_TOKENS)).reshape(SECTIONS * HEADS, SEC_TOKENS)
    diagonal = positions[:, None] == positions[None, :]

    def plane_item(item_pair):
        packed, key_alive = item_pair
        scores = jnp.dot(packed[:, 0], packed[:, 1].T, preferred_element_type=jnp.float32) * score_scale
        attention = masked_softmax(scores, key_alive[None, :] | diagonal)
        return jnp.dot(attention, packed[:, 2], preferred_element_type=jnp.float32).astype(jnp.bfloat16)
    attended = lax.map(plane_item, (items, item_valid))
    context = jnp.transpose(attended.reshape(SECTIONS, HEADS, SEC_TOKENS, HEAD_DIM), (0, 2, 1, 3)).reshape(SECTIONS * SEC_TOKENS, D)
    encoded = (after_cross.astype(jnp.float32) + jnp.dot(context, plane_out, preferred_element_type=jnp.float32)).astype(jnp.bfloat16)
    labels = region_ids.reshape(-1)
    weight_live = valid.reshape(-1).astype(jnp.float32)
    region_sum = jax.ops.segment_sum(encoded.astype(jnp.float32) * weight_live[:, None], labels, num_segments=REGIONS)
    region_count = jax.ops.segment_sum(weight_live, labels, num_segments=REGIONS)
    pooled = region_sum / jnp.maximum(region_count, 1.0)[:, None]
    return (encoded.reshape(SECTIONS, SEC_TOKENS, D), pooled)
```

```python
import math

import jax
import jax.numpy as jnp
from jax import lax
from jax.sharding import PartitionSpec as P

HEADS = 16
HEAD_DIM = 64
WINDOW = 128


negative_big = -1e30


def shifted_2(value, axis, by):
    peers = lax.axis_size(axis)
    pairs = [(i, i + by) for i in range(peers) if 0 <= i + by < peers]
    return lax.ppermute(value, axis, pairs)


def rms_norm(values, gain):
    wide = values.astype(jnp.float32)
    scaled = wide * lax.rsqrt(jnp.mean(wide * wide, axis=-1, keepdims=True) + 1e-06) * gain
    return scaled.astype(jnp.bfloat16)


def masked_softmax(scores, allowed):
    shifted = jnp.where(allowed, scores, negative_big)
    top = jnp.max(shifted, axis=-1, keepdims=True)
    expo = jnp.where(allowed, jnp.exp(shifted - top), 0.0)
    return (expo / jnp.sum(expo, axis=-1, keepdims=True)).astype(jnp.bfloat16)


def fold_product(inputs, weight_piece):
    return jnp.dot(inputs, weight_piece, preferred_element_type=jnp.float32)


def gather_pieces(shard):
    groups = lax.axis_size("groups")
    sections = lax.axis_size("sec")
    pair = 2 if sections % 2 == 0 else 1
    width = shard.shape[1] // (groups * pair)
    g = lax.axis_index("groups")
    k = lax.axis_index("sec") % pair
    own = g * pair + k
    mine = lax.dynamic_slice_in_dim(shard, own * width, width, axis=1)
    first = lax.all_gather(mine, "plane", axis=0, tiled=True)
    by_group = [(own, first)]
    for step in range(1, groups):
        moved = [(i, (i + step) % groups) for i in range(groups)]
        source = lax.rem(g - step + groups, groups)
        by_group.append((source * pair + k, lax.ppermute(first, "groups", moved)))
    held = list(by_group)
    if pair == 2:
        swap = [(i, i ^ 1) for i in range(sections)]
        for piece, block in by_group:
            held.append((piece - k + (1 - k), lax.ppermute(block, "sec", swap)))
    return held, width


def project(inputs, pieces):
    held, width = pieces
    out = jnp.zeros((inputs.shape[0], width * len(held)), jnp.float32)
    for piece, block in held:
        part = jnp.dot(inputs, block, preferred_element_type=jnp.float32)
        out = lax.dynamic_update_slice_in_dim(out, part, piece * width, axis=1)
    return out


def attend_items(pieces):
    packed_all, flags_all = pieces
    seq_len = packed_all.shape[2]
    block_len = 512
    score_scale = 1.0 / math.sqrt(HEAD_DIM)
    key_index = jnp.arange(seq_len, dtype=jnp.int32)

    def one_item(item_pair):
        packed, key_flag = item_pair
        key_rows = packed[:, HEAD_DIM : 2 * HEAD_DIM]
        value_rows = packed[:, 2 * HEAD_DIM :]
        key_alive = key_flag > 0.5
        query_blocks = packed[:, :HEAD_DIM].reshape(seq_len // block_len, block_len, HEAD_DIM)
        block_starts = jnp.arange(seq_len // block_len, dtype=jnp.int32) * block_len

        def one_block(block_pair):
            query_rows, offset = block_pair
            scores = (
                jnp.einsum("qd,kd->qk", query_rows, key_rows, preferred_element_type=jnp.float32)
                * score_scale
            )
            own_index = offset + jnp.arange(block_len, dtype=jnp.int32)
            allowed = key_alive[None, :] | (key_index[None, :] == own_index[:, None])
            attention = masked_softmax(scores, allowed)
            return jnp.dot(attention, value_rows, preferred_element_type=jnp.float32).astype(
                jnp.bfloat16
            )

        return lax.map(one_block, (query_blocks, block_starts)).reshape(seq_len, HEAD_DIM)

    return lax.map(one_item, (packed_all[0], flags_all[0]))[None]


def body(tokens, counts, region_ids, norm_gains, cross_qkv, cross_out, plane_qkv, plane_out):
    sec_block, tok_block, model_width = tokens.shape
    plane_count = lax.axis_size("plane")
    regions = 2 * lax.axis_size("sec") * plane_count
    positions = lax.axis_index("plane") * tok_block + jnp.arange(tok_block, dtype=jnp.int32)
    padded_counts = jnp.concatenate(
        [jnp.zeros((1,), jnp.int32), counts, jnp.zeros((1,), jnp.int32)]
    )
    near_counts = lax.dynamic_slice_in_dim(
        padded_counts, lax.axis_index("sec") * sec_block, sec_block + 2
    )
    near_valid = positions[None, :] < near_counts[:, None]
    own_valid = near_valid[1 : sec_block + 1]
    score_scale = 1.0 / math.sqrt(HEAD_DIM)
    cross_qkv_pieces = gather_pieces(cross_qkv)
    cross_out_pieces = gather_pieces(cross_out)
    plane_qkv_pieces = gather_pieces(plane_qkv)
    plane_out_pieces = gather_pieces(plane_out)
    normed = rms_norm(tokens, norm_gains[0])
    inputs = normed.reshape(-1, model_width)
    result = project(inputs, cross_qkv_pieces)
    projected = result.astype(jnp.bfloat16).reshape(sec_block, tok_block, 3 * model_width)
    own_kv = projected[:, :, model_width:]
    from_below = shifted_2(own_kv[sec_block - 1], "sec", 1)
    from_above = shifted_2(own_kv[0], "sec", -1)
    near_kv = jnp.concatenate([from_below[None], own_kv, from_above[None]], axis=0)
    queries = projected[:, :, :model_width]
    windows = tok_block // WINDOW
    query_win = queries.reshape(sec_block, windows, WINDOW, HEADS, HEAD_DIM)
    pair_win = near_kv.reshape(sec_block + 2, windows, WINDOW, 2, HEADS, HEAD_DIM)
    stacked = jnp.concatenate(
        [pair_win[0:sec_block], pair_win[1 : sec_block + 1], pair_win[2 : sec_block + 2]], axis=2
    )
    valid_win = near_valid.reshape(sec_block + 2, windows, WINDOW)
    valid_three = jnp.concatenate(
        [valid_win[0:sec_block], valid_win[1 : sec_block + 1], valid_win[2 : sec_block + 2]], axis=2
    )
    itself = jnp.arange(3 * WINDOW)[None, :] == jnp.arange(WINDOW)[:, None] + WINDOW
    scores = (
        jnp.einsum(
            "snqhd,snkhd->snhqk", query_win, stacked[:, :, :, 0], preferred_element_type=jnp.float32
        )
        * score_scale
    )
    allowed = valid_three[:, :, None, None, :] | itself[None, None, None]
    attention = masked_softmax(scores, allowed)
    context = jnp.einsum(
        "snhqk,snkhd->snqhd", attention, stacked[:, :, :, 1], preferred_element_type=jnp.float32
    )
    context = context.astype(jnp.bfloat16).reshape(-1, model_width)
    result = project(context, cross_out_pieces)
    after_cross = (tokens.reshape(-1, model_width).astype(jnp.float32) + result).astype(
        jnp.bfloat16
    )
    normed = rms_norm(after_cross, norm_gains[1])
    result = project(normed, plane_qkv_pieces)
    projected = result.astype(jnp.bfloat16).reshape(sec_block, tok_block, 3, HEADS, HEAD_DIM)
    per_device = sec_block * HEADS // plane_count
    heads_first = jnp.transpose(projected, (0, 3, 1, 2, 4)).reshape(
        plane_count, per_device, tok_block, 3 * HEAD_DIM
    )
    key_flags = jnp.broadcast_to(own_valid[:, None, :], (sec_block, HEADS, tok_block)).astype(
        jnp.bfloat16
    )
    key_flags = key_flags.reshape(plane_count, per_device, tok_block)
    attended = attend_items(
        (
            lax.all_to_all(heads_first, "plane", split_axis=0, concat_axis=2, tiled=True),
            lax.all_to_all(key_flags, "plane", split_axis=0, concat_axis=2, tiled=True),
        )
    )
    returned = lax.all_to_all(attended, "plane", split_axis=2, concat_axis=0, tiled=True)
    context = jnp.transpose(
        returned.reshape(sec_block, HEADS, tok_block, HEAD_DIM), (0, 2, 1, 3)
    ).reshape(-1, model_width)
    result = project(context, plane_out_pieces)
    encoded = (after_cross.astype(jnp.float32) + result).astype(jnp.bfloat16)
    labels = region_ids.reshape(-1)
    member = (jnp.arange(regions, dtype=jnp.int32)[:, None] == labels[None, :]) & own_valid.reshape(
        -1
    )[None, :]
    region_sum = jnp.dot(member.astype(jnp.bfloat16), encoded, preferred_element_type=jnp.float32)
    region_count = jnp.sum(member.astype(jnp.float32), axis=1)
    totals, counted = (
        lax.psum_scatter(region_sum, ("sec", "plane"), scatter_dimension=0, tiled=True),
        lax.psum_scatter(region_count, ("sec", "plane"), scatter_dimension=0, tiled=True),
    )
    pooled = totals / jnp.maximum(counted, 1.0)[:, None]
    return (encoded.reshape(sec_block, tok_block, model_width), pooled)


def solution(mesh):
    in_specs = (
        P(("groups", "sec"), "plane", None),
        P("groups"),
        P(("groups", "sec"), "plane"),
        P(),
        P("plane", None),
        P("plane", None),
        P("plane", None),
        P("plane", None),
    )
    out_specs = (P(("groups", "sec"), "plane", None), P(("groups", "sec", "plane"), None))
    return jax.shard_map(body, mesh=mesh, in_specs=in_specs, out_specs=out_specs, check_vma=False)
```

```python
import math

import jax
import jax.numpy as jnp
from jax import lax
from jax.sharding import PartitionSpec as P

HEADS = 16
HEAD_DIM = 64
WINDOW = 128


negative_big = -1e30


def shifted_2(value, axis, by):
    peers = lax.axis_size(axis)
    pairs = [(i, i + by) for i in range(peers) if 0 <= i + by < peers]
    return lax.ppermute(value, axis, pairs)


def rms_norm(values, gain):
    wide = values.astype(jnp.float32)
    scaled = wide * lax.rsqrt(jnp.mean(wide * wide, axis=-1, keepdims=True) + 1e-06) * gain
    return scaled.astype(jnp.bfloat16)


def masked_softmax(scores, allowed):
    shifted = jnp.where(allowed, scores, negative_big)
    top = jnp.max(shifted, axis=-1, keepdims=True)
    expo = jnp.where(allowed, jnp.exp(shifted - top), 0.0)
    return (expo / jnp.sum(expo, axis=-1, keepdims=True)).astype(jnp.bfloat16)


def fold_product(inputs, weight_piece):
    return jnp.dot(inputs, weight_piece, preferred_element_type=jnp.float32)


def gather_pieces(shards):
    groups = lax.axis_size("groups")
    sections = lax.axis_size("sec")
    pair = 2 if sections % 2 == 0 else 1
    count = groups * pair
    widths = [shard.shape[1] // count for shard in shards]
    g = lax.axis_index("groups")
    k = lax.axis_index("sec") % pair
    own = g * pair + k
    mine = jnp.concatenate(
        [
            lax.dynamic_slice_in_dim(shard, own * width, width, axis=1)
            for shard, width in zip(shards, widths)
        ],
        axis=1,
    )
    first = lax.all_gather(mine, "plane", axis=0, tiled=True)
    by_group = [(own, first)]
    for step in range(1, groups):
        moved = [(i, (i + step) % groups) for i in range(groups)]
        source = lax.rem(g - step + groups, groups)
        by_group.append((source * pair + k, lax.ppermute(first, "groups", moved)))
    held = list(by_group)
    if pair == 2:
        swap = [(i, i ^ 1) for i in range(sections)]
        for piece, block in by_group:
            held.append((piece - k + (1 - k), lax.ppermute(block, "sec", swap)))
    results = []
    offset = 0
    for width in widths:
        results.append(([(piece, block[:, offset : offset + width]) for piece, block in held], width))
        offset += width
    return results


def project(inputs, pieces):
    held, width = pieces
    out = jnp.zeros((inputs.shape[0], width * len(held)), jnp.float32)
    for piece, block in held:
        part = jnp.dot(inputs, block, preferred_element_type=jnp.float32)
        out = lax.dynamic_update_slice_in_dim(out, part, piece * width, axis=1)
    return out


def attend_items(pieces):
    packed_all, flags_all = pieces
    seq_len = packed_all.shape[2]
    block_len = 512
    score_scale = 1.0 / math.sqrt(HEAD_DIM)
    key_index = jnp.arange(seq_len, dtype=jnp.int32)

    def one_item(item_pair):
        packed, key_flag = item_pair
        key_rows = packed[:, HEAD_DIM : 2 * HEAD_DIM]
        value_rows = packed[:, 2 * HEAD_DIM :]
        key_alive = key_flag > 0.5
        query_blocks = packed[:, :HEAD_DIM].reshape(seq_len // block_len, block_len, HEAD_DIM)
        block_starts = jnp.arange(seq_len // block_len, dtype=jnp.int32) * block_len

        def one_block(block_pair):
            query_rows, offset = block_pair
            scores = (
                jnp.einsum("qd,kd->qk", query_rows, key_rows, preferred_element_type=jnp.float32)
                * score_scale
            )
            own_index = offset + jnp.arange(block_len, dtype=jnp.int32)
            allowed = key_alive[None, :] | (key_index[None, :] == own_index[:, None])
            attention = masked_softmax(scores, allowed)
            return jnp.dot(attention, value_rows, preferred_element_type=jnp.float32).astype(
                jnp.bfloat16
            )

        return lax.map(one_block, (query_blocks, block_starts)).reshape(seq_len, HEAD_DIM)

    return lax.map(one_item, (packed_all[0], flags_all[0]))[None]


def body(tokens, counts, region_ids, norm_gains, cross_qkv, cross_out, plane_qkv, plane_out):
    sec_block, tok_block, model_width = tokens.shape
    plane_count = lax.axis_size("plane")
    regions = 2 * lax.axis_size("sec") * plane_count
    positions = lax.axis_index("plane") * tok_block + jnp.arange(tok_block, dtype=jnp.int32)
    padded_counts = jnp.concatenate(
        [jnp.zeros((1,), jnp.int32), counts, jnp.zeros((1,), jnp.int32)]
    )
    near_counts = lax.dynamic_slice_in_dim(
        padded_counts, lax.axis_index("sec") * sec_block, sec_block + 2
    )
    near_valid = positions[None, :] < near_counts[:, None]
    own_valid = near_valid[1 : sec_block + 1]
    score_scale = 1.0 / math.sqrt(HEAD_DIM)
    (cross_qkv_pieces,) = gather_pieces([cross_qkv])
    (plane_qkv_pieces,) = gather_pieces([plane_qkv])
    cross_out_pieces, plane_out_pieces = gather_pieces([cross_out, plane_out])
    normed = rms_norm(tokens, norm_gains[0])
    inputs = normed.reshape(-1, model_width)
    result = project(inputs, cross_qkv_pieces)
    projected = result.astype(jnp.bfloat16).reshape(sec_block, tok_block, 3 * model_width)
    own_kv = projected[:, :, model_width:]
    from_below = shifted_2(own_kv[sec_block - 1], "sec", 1)
    from_above = shifted_2(own_kv[0], "sec", -1)
    near_kv = jnp.concatenate([from_below[None], own_kv, from_above[None]], axis=0)
    queries = projected[:, :, :model_width]
    windows = tok_block // WINDOW
    query_win = queries.reshape(sec_block, windows, WINDOW, HEADS, HEAD_DIM)
    pair_win = near_kv.reshape(sec_block + 2, windows, WINDOW, 2, HEADS, HEAD_DIM)
    stacked = jnp.concatenate(
        [pair_win[0:sec_block], pair_win[1 : sec_block + 1], pair_win[2 : sec_block + 2]], axis=2
    )
    valid_win = near_valid.reshape(sec_block + 2, windows, WINDOW)
    valid_three = jnp.concatenate(
        [valid_win[0:sec_block], valid_win[1 : sec_block + 1], valid_win[2 : sec_block + 2]], axis=2
    )
    itself = jnp.arange(3 * WINDOW)[None, :] == jnp.arange(WINDOW)[:, None] + WINDOW
    scores = (
        jnp.einsum(
            "snqhd,snkhd->snhqk", query_win, stacked[:, :, :, 0], preferred_element_type=jnp.float32
        )
        * score_scale
    )
    allowed = valid_three[:, :, None, None, :] | itself[None, None, None]
    attention = masked_softmax(scores, allowed)
    context = jnp.einsum(
        "snhqk,snkhd->snqhd", attention, stacked[:, :, :, 1], preferred_element_type=jnp.float32
    )
    context = context.astype(jnp.bfloat16).reshape(-1, model_width)
    result = project(context, cross_out_pieces)
    after_cross = (tokens.reshape(-1, model_width).astype(jnp.float32) + result).astype(
        jnp.bfloat16
    )
    normed = rms_norm(after_cross, norm_gains[1])
    result = project(normed, plane_qkv_pieces)
    projected = result.astype(jnp.bfloat16).reshape(sec_block, tok_block, 3, HEADS, HEAD_DIM)
    per_device = sec_block * HEADS // plane_count
    heads_first = jnp.transpose(projected, (0, 3, 1, 2, 4)).reshape(
        plane_count, per_device, tok_block, 3 * HEAD_DIM
    )
    key_flags = jnp.broadcast_to(own_valid[:, None, :], (sec_block, HEADS, tok_block)).astype(
        jnp.bfloat16
    )
    key_flags = key_flags.reshape(plane_count, per_device, tok_block)
    attended = attend_items(
        (
            lax.all_to_all(heads_first, "plane", split_axis=0, concat_axis=2, tiled=True),
            lax.all_to_all(key_flags, "plane", split_axis=0, concat_axis=2, tiled=True),
        )
    )
    returned = lax.all_to_all(attended, "plane", split_axis=2, concat_axis=0, tiled=True)
    context = jnp.transpose(
        returned.reshape(sec_block, HEADS, tok_block, HEAD_DIM), (0, 2, 1, 3)
    ).reshape(-1, model_width)
    result = project(context, plane_out_pieces)
    encoded = (after_cross.astype(jnp.float32) + result).astype(jnp.bfloat16)
    labels = region_ids.reshape(-1)
    member = (jnp.arange(regions, dtype=jnp.int32)[:, None] == labels[None, :]) & own_valid.reshape(
        -1
    )[None, :]
    extended = jnp.concatenate([encoded, jnp.ones((encoded.shape[0], 128), jnp.bfloat16)], axis=1)
    partial = jnp.dot(member.astype(jnp.bfloat16), extended, preferred_element_type=jnp.float32)
    sections = lax.axis_size("sec")
    width = partial.shape[1]
    partial = partial.reshape(sections, plane_count, 2, width)
    me_plane = lax.axis_index("plane")
    gathered = lax.dynamic_index_in_dim(partial, me_plane, axis=1, keepdims=False)
    for step in range(1, plane_count):
        moved = [(i, (i + step) % plane_count) for i in range(plane_count)]
        target = lax.rem(me_plane + step, plane_count)
        block = lax.dynamic_index_in_dim(partial, target, axis=1, keepdims=False)
        gathered = gathered + lax.ppermute(block, "plane", moved)
    me_sec = lax.axis_index("sec")
    totals = lax.dynamic_index_in_dim(gathered, me_sec, axis=0, keepdims=False)
    for step in range(1, sections):
        moved = [(i, (i + step) % sections) for i in range(sections)]
        target = lax.rem(me_sec + step, sections)
        block = lax.dynamic_index_in_dim(gathered, target, axis=0, keepdims=False)
        totals = totals + lax.ppermute(block, "sec", moved)
    counted = totals[:, model_width]
    pooled = totals[:, :model_width] / jnp.maximum(counted, 1.0)[:, None]
    return (encoded.reshape(sec_block, tok_block, model_width), pooled)


def solution(mesh):
    in_specs = (
        P(("groups", "sec"), "plane", None),
        P("groups"),
        P(("groups", "sec"), "plane"),
        P(),
        P("plane", None),
        P("plane", None),
        P("plane", None),
        P("plane", None),
    )
    out_specs = (P(("groups", "sec"), "plane", None), P(("groups", "sec", "plane"), None))
    return jax.shard_map(body, mesh=mesh, in_specs=in_specs, out_specs=out_specs, check_vma=False)
```

```python
import math

import jax
import jax.numpy as jnp
from jax import lax
from jax.sharding import PartitionSpec as P

HEADS = 16
HEAD_DIM = 64
WINDOW = 128


negative_big = -1e30


def shifted_2(value, axis, by):
    peers = lax.axis_size(axis)
    pairs = [(i, i + by) for i in range(peers) if 0 <= i + by < peers]
    return lax.ppermute(value, axis, pairs)


def rms_norm(values, gain):
    wide = values.astype(jnp.float32)
    scaled = wide * lax.rsqrt(jnp.mean(wide * wide, axis=-1, keepdims=True) + 1e-06) * gain
    return scaled.astype(jnp.bfloat16)


def masked_softmax(scores, allowed):
    shifted = jnp.where(allowed, scores, negative_big)
    top = jnp.max(shifted, axis=-1, keepdims=True)
    expo = jnp.where(allowed, jnp.exp(shifted - top), 0.0)
    return (expo / jnp.sum(expo, axis=-1, keepdims=True)).astype(jnp.bfloat16)


def fold_product(inputs, weight_piece):
    return jnp.dot(inputs, weight_piece, preferred_element_type=jnp.float32)


def replica_levels():
    levels = []
    if lax.axis_size("groups") % 2 == 0:
        levels.append(("groups", lax.axis_size("groups"), 1))
    if lax.axis_size("sec") % 4 == 0:
        levels.append(("sec", lax.axis_size("sec"), 2))
    if lax.axis_size("sec") % 2 == 0:
        levels.append(("sec", lax.axis_size("sec"), 1))
    return levels


def rotate_rows(values, axis):
    plane_count = lax.axis_size("plane")
    block = values.shape[axis] // plane_count
    start = (lax.axis_index("plane") + 1) * block
    doubled = jnp.concatenate([values, values], axis=axis)
    return lax.dynamic_slice_in_dim(doubled, start, (plane_count - 1) * block, axis=axis)


def gather_pieces(shards):
    levels = replica_levels()
    count = 2 ** len(levels)
    widths = [shard.shape[1] // count for shard in shards]
    own = 0
    for bit, (axis, _, flip) in enumerate(levels):
        own = own + ((lax.axis_index(axis) // flip) % 2) * (2 ** bit)
    mine = jnp.concatenate(
        [
            lax.dynamic_slice_in_dim(shard, own * width, width, axis=1)
            for shard, width in zip(shards, widths)
        ],
        axis=1,
    )
    gathered = lax.all_gather(mine, "plane", axis=0, tiled=True)
    held = [(own, rotate_rows(gathered, 0))]
    for bit, (axis, size, flip) in enumerate(levels):
        swap = [(i, i ^ flip) for i in range(size)]
        held = held + [
            (piece + (1 - 2 * ((piece // 2 ** bit) % 2)) * 2 ** bit, lax.ppermute(block, axis, swap))
            for piece, block in held
        ]
    results = []
    offset = 0
    for shard, width in zip(shards, widths):
        results.append((shard, [(piece, block[:, offset : offset + width]) for piece, block in held], width))
        offset += width
    return results


def project(inputs, pieces):
    shard, held, width = pieces
    rows = shard.shape[0]
    local_inputs = lax.dynamic_slice_in_dim(inputs, lax.axis_index("plane") * rows, rows, axis=1)
    local = jnp.dot(local_inputs, shard, preferred_element_type=jnp.float32)
    remote_inputs = rotate_rows(inputs, 1)
    remote = jnp.zeros_like(local)
    for piece, block in held:
        part = jnp.dot(remote_inputs, block, preferred_element_type=jnp.float32)
        remote = lax.dynamic_update_slice_in_dim(remote, part, piece * width, axis=1)
    return local + remote


def attend_items(pieces):
    packed_all, flags_all = pieces
    seq_len = packed_all.shape[2]
    block_len = 512
    score_scale = 1.0 / math.sqrt(HEAD_DIM)
    key_index = jnp.arange(seq_len, dtype=jnp.int32)

    def one_item(item_pair):
        packed, key_flag = item_pair
        key_rows = packed[:, HEAD_DIM : 2 * HEAD_DIM]
        value_rows = packed[:, 2 * HEAD_DIM :]
        key_alive = key_flag > 0.5
        query_blocks = packed[:, :HEAD_DIM].reshape(seq_len // block_len, block_len, HEAD_DIM)
        block_starts = jnp.arange(seq_len // block_len, dtype=jnp.int32) * block_len

        def one_block(block_pair):
            query_rows, offset = block_pair
            scores = (
                jnp.einsum("qd,kd->qk", query_rows, key_rows, preferred_element_type=jnp.float32)
                * score_scale
            )
            own_index = offset + jnp.arange(block_len, dtype=jnp.int32)
            allowed = key_alive[None, :] | (key_index[None, :] == own_index[:, None])
            attention = masked_softmax(scores, allowed)
            return jnp.dot(attention, value_rows, preferred_element_type=jnp.float32).astype(
                jnp.bfloat16
            )

        return lax.map(one_block, (query_blocks, block_starts)).reshape(seq_len, HEAD_DIM)

    return lax.map(one_item, (packed_all[0], flags_all[0]))[None]


def body(tokens, counts, region_ids, norm_gains, cross_qkv, cross_out, plane_qkv, plane_out):
    sec_block, tok_block, model_width = tokens.shape
    plane_count = lax.axis_size("plane")
    regions = 2 * lax.axis_size("sec") * plane_count
    positions = lax.axis_index("plane") * tok_block + jnp.arange(tok_block, dtype=jnp.int32)
    padded_counts = jnp.concatenate(
        [jnp.zeros((1,), jnp.int32), counts, jnp.zeros((1,), jnp.int32)]
    )
    near_counts = lax.dynamic_slice_in_dim(
        padded_counts, lax.axis_index("sec") * sec_block, sec_block + 2
    )
    near_valid = positions[None, :] < near_counts[:, None]
    own_valid = near_valid[1 : sec_block + 1]
    score_scale = 1.0 / math.sqrt(HEAD_DIM)
    cross_qkv_pieces, cross_out_pieces = gather_pieces([cross_qkv, cross_out])
    plane_qkv_pieces, plane_out_pieces = gather_pieces([plane_qkv, plane_out])
    normed = rms_norm(tokens, norm_gains[0])
    inputs = normed.reshape(-1, model_width)
    result = project(inputs, cross_qkv_pieces)
    projected = result.astype(jnp.bfloat16).reshape(sec_block, tok_block, 3 * model_width)
    own_kv = projected[:, :, model_width:]
    from_below = shifted_2(own_kv[sec_block - 1], "sec", 1)
    from_above = shifted_2(own_kv[0], "sec", -1)
    near_kv = jnp.concatenate([from_below[None], own_kv, from_above[None]], axis=0)
    queries = projected[:, :, :model_width]
    windows = tok_block // WINDOW
    query_win = queries.reshape(sec_block, windows, WINDOW, HEADS, HEAD_DIM)
    pair_win = near_kv.reshape(sec_block + 2, windows, WINDOW, 2, HEADS, HEAD_DIM)
    stacked = jnp.concatenate(
        [pair_win[0:sec_block], pair_win[1 : sec_block + 1], pair_win[2 : sec_block + 2]], axis=2
    )
    valid_win = near_valid.reshape(sec_block + 2, windows, WINDOW)
    valid_three = jnp.concatenate(
        [valid_win[0:sec_block], valid_win[1 : sec_block + 1], valid_win[2 : sec_block + 2]], axis=2
    )
    itself = jnp.arange(3 * WINDOW)[None, :] == jnp.arange(WINDOW)[:, None] + WINDOW
    scores = (
        jnp.einsum(
            "snqhd,snkhd->snhqk", query_win, stacked[:, :, :, 0], preferred_element_type=jnp.float32
        )
        * score_scale
    )
    allowed = valid_three[:, :, None, None, :] | itself[None, None, None]
    attention = masked_softmax(scores, allowed)
    context = jnp.einsum(
        "snhqk,snkhd->snqhd", attention, stacked[:, :, :, 1], preferred_element_type=jnp.float32
    )
    context = context.astype(jnp.bfloat16).reshape(-1, model_width)
    result = project(context, cross_out_pieces)
    after_cross = (tokens.reshape(-1, model_width).astype(jnp.float32) + result).astype(
        jnp.bfloat16
    )
    normed = rms_norm(after_cross, norm_gains[1])
    result = project(normed, plane_qkv_pieces)
    projected = result.astype(jnp.bfloat16).reshape(sec_block, tok_block, 3, HEADS, HEAD_DIM)
    per_device = sec_block * HEADS // plane_count
    heads_first = jnp.transpose(projected, (0, 3, 1, 2, 4)).reshape(
        plane_count, per_device, tok_block, 3 * HEAD_DIM
    )
    key_flags = jnp.broadcast_to(own_valid[:, None, :], (sec_block, HEADS, tok_block)).astype(
        jnp.bfloat16
    )
    key_flags = key_flags.reshape(plane_count, per_device, tok_block)
    attended = attend_items(
        (
            lax.all_to_all(heads_first, "plane", split_axis=0, concat_axis=2, tiled=True),
            lax.all_to_all(key_flags, "plane", split_axis=0, concat_axis=2, tiled=True),
        )
    )
    returned = lax.all_to_all(attended, "plane", split_axis=2, concat_axis=0, tiled=True)
    context = jnp.transpose(
        returned.reshape(sec_block, HEADS, tok_block, HEAD_DIM), (0, 2, 1, 3)
    ).reshape(-1, model_width)
    result = project(context, plane_out_pieces)
    encoded = (after_cross.astype(jnp.float32) + result).astype(jnp.bfloat16)
    labels = region_ids.reshape(-1)
    member = (jnp.arange(regions, dtype=jnp.int32)[:, None] == labels[None, :]) & own_valid.reshape(
        -1
    )[None, :]
    extended = jnp.concatenate([encoded, jnp.ones((encoded.shape[0], 128), jnp.bfloat16)], axis=1)
    partial = jnp.dot(member.astype(jnp.bfloat16), extended, preferred_element_type=jnp.float32)
    sections = lax.axis_size("sec")
    width = partial.shape[1]
    partial = partial.reshape(sections, plane_count, 2, width)
    me_plane = lax.axis_index("plane")
    gathered = lax.dynamic_index_in_dim(partial, me_plane, axis=1, keepdims=False)
    for step in range(1, plane_count):
        moved = [(i, (i + step) % plane_count) for i in range(plane_count)]
        target = lax.rem(me_plane + step, plane_count)
        block = lax.dynamic_index_in_dim(partial, target, axis=1, keepdims=False)
        gathered = gathered + lax.ppermute(block, "plane", moved)
    me_sec = lax.axis_index("sec")
    totals = lax.dynamic_index_in_dim(gathered, me_sec, axis=0, keepdims=False)
    for step in range(1, sections):
        moved = [(i, (i + step) % sections) for i in range(sections)]
        target = lax.rem(me_sec + step, sections)
        block = lax.dynamic_index_in_dim(gathered, target, axis=0, keepdims=False)
        totals = totals + lax.ppermute(block, "sec", moved)
    counted = totals[:, model_width]
    pooled = totals[:, :model_width] / jnp.maximum(counted, 1.0)[:, None]
    return (encoded.reshape(sec_block, tok_block, model_width), pooled)


def solution(mesh):
    in_specs = (
        P(("groups", "sec"), "plane", None),
        P("groups"),
        P(("groups", "sec"), "plane"),
        P(),
        P("plane", None),
        P("plane", None),
        P("plane", None),
        P("plane", None),
    )
    out_specs = (P(("groups", "sec"), "plane", None), P(("groups", "sec", "plane"), None))
    return jax.shard_map(body, mesh=mesh, in_specs=in_specs, out_specs=out_specs, check_vma=False)
```

```python
import math

import jax
import jax.numpy as jnp
from jax import lax
from jax.sharding import PartitionSpec as P

HEADS = 16
HEAD_DIM = 64
WINDOW = 128


negative_big = -1e30


def shifted_2(value, axis, by):
    peers = lax.axis_size(axis)
    pairs = [(i, i + by) for i in range(peers) if 0 <= i + by < peers]
    return lax.ppermute(value, axis, pairs)


def rms_norm(values, gain):
    wide = values.astype(jnp.float32)
    scaled = wide * lax.rsqrt(jnp.mean(wide * wide, axis=-1, keepdims=True) + 1e-06) * gain
    return scaled.astype(jnp.bfloat16)


def masked_softmax(scores, allowed):
    shifted = jnp.where(allowed, scores, negative_big)
    top = jnp.max(shifted, axis=-1, keepdims=True)
    expo = jnp.where(allowed, jnp.exp(shifted - top), 0.0)
    return (expo / jnp.sum(expo, axis=-1, keepdims=True)).astype(jnp.bfloat16)


def fold_product(inputs, weight_piece):
    return jnp.dot(inputs, weight_piece, preferred_element_type=jnp.float32)


def replica_levels():
    levels = []
    if lax.axis_size("groups") % 2 == 0:
        levels.append(("groups", lax.axis_size("groups"), 1))
    if lax.axis_size("sec") % 4 == 0:
        levels.append(("sec", lax.axis_size("sec"), 2))
    if lax.axis_size("sec") % 2 == 0:
        levels.append(("sec", lax.axis_size("sec"), 1))
    return levels


def rotate_rows(values, axis):
    plane_count = lax.axis_size("plane")
    block = values.shape[axis] // plane_count
    start = (lax.axis_index("plane") + 1) * block
    doubled = jnp.concatenate([values, values], axis=axis)
    return lax.dynamic_slice_in_dim(doubled, start, (plane_count - 1) * block, axis=axis)


def gather_pieces(shards):
    levels = replica_levels()
    count = 2 ** len(levels)
    widths = [shard.shape[1] // count for shard in shards]
    own = 0
    for bit, (axis, _, flip) in enumerate(levels):
        own = own + ((lax.axis_index(axis) // flip) % 2) * (2 ** bit)
    mine = jnp.concatenate(
        [
            lax.dynamic_slice_in_dim(shard, own * width, width, axis=1)
            for shard, width in zip(shards, widths)
        ],
        axis=1,
    )
    gathered = lax.all_gather(mine, "plane", axis=0, tiled=True)
    held = [(own, rotate_rows(gathered, 0))]
    for bit, (axis, size, flip) in enumerate(levels):
        swap = [(i, i ^ flip) for i in range(size)]
        held = held + [
            (piece + (1 - 2 * ((piece // 2 ** bit) % 2)) * 2 ** bit, lax.ppermute(block, axis, swap))
            for piece, block in held
        ]
    results = []
    offset = 0
    for shard, width in zip(shards, widths):
        results.append((shard, [(piece, block[:, offset : offset + width]) for piece, block in held], width))
        offset += width
    return results


def assemble(pieces):
    shard, held, width = pieces
    remote = jnp.zeros((held[0][1].shape[0], width * len(held)), shard.dtype)
    for piece, block in held:
        remote = lax.dynamic_update_slice_in_dim(remote, block, piece * width, axis=1)
    return shard, remote


def project(inputs, weights):
    shard, remote = weights
    rows = shard.shape[0]
    local_inputs = lax.dynamic_slice_in_dim(inputs, lax.axis_index("plane") * rows, rows, axis=1)
    local = jnp.dot(local_inputs, shard, preferred_element_type=jnp.float32)
    remote_inputs = rotate_rows(inputs, 1)
    return local + jnp.dot(remote_inputs, remote, preferred_element_type=jnp.float32)


def attend_items(pieces):
    packed_all, flags_all = pieces
    packed = packed_all[0]
    items, seq_len = packed.shape[0], packed.shape[1]
    block_len = min(seq_len, 512)
    score_scale = 1.0 / math.sqrt(HEAD_DIM)
    key_index = jnp.arange(seq_len, dtype=jnp.int32)
    keys = packed[:, :, HEAD_DIM : 2 * HEAD_DIM]
    values = packed[:, :, 2 * HEAD_DIM :]
    key_alive = flags_all[0] > 0.5

    def one_block(block_pair):
        query_rows, offset = block_pair
        scores = (
            jnp.einsum("nqd,nkd->nqk", query_rows, keys, preferred_element_type=jnp.float32)
            * score_scale
        )
        own_index = offset + jnp.arange(block_len, dtype=jnp.int32)
        allowed = key_alive[:, None, :] | (key_index[None, None, :] == own_index[None, :, None])
        attention = masked_softmax(scores, allowed)
        return jnp.einsum(
            "nqk,nkd->nqd", attention, values, preferred_element_type=jnp.float32
        ).astype(jnp.bfloat16)

    blocks = seq_len // block_len
    queries = packed[:, :, :HEAD_DIM]
    if blocks == 1:
        return one_block((queries, jnp.int32(0)))[None]
    query_blocks = jnp.transpose(queries.reshape(items, blocks, block_len, HEAD_DIM), (1, 0, 2, 3))
    starts = jnp.arange(blocks, dtype=jnp.int32) * block_len
    context = lax.map(one_block, (query_blocks, starts))
    return jnp.transpose(context, (1, 0, 2, 3)).reshape(items, seq_len, HEAD_DIM)[None]


def body(tokens, counts, region_ids, norm_gains, cross_qkv, cross_out, plane_qkv, plane_out):
    sec_block, tok_block, model_width = tokens.shape
    plane_count = lax.axis_size("plane")
    regions = 2 * lax.axis_size("sec") * plane_count
    positions = lax.axis_index("plane") * tok_block + jnp.arange(tok_block, dtype=jnp.int32)
    padded_counts = jnp.concatenate(
        [jnp.zeros((1,), jnp.int32), counts, jnp.zeros((1,), jnp.int32)]
    )
    near_counts = lax.dynamic_slice_in_dim(
        padded_counts, lax.axis_index("sec") * sec_block, sec_block + 2
    )
    near_valid = positions[None, :] < near_counts[:, None]
    own_valid = near_valid[1 : sec_block + 1]
    score_scale = 1.0 / math.sqrt(HEAD_DIM)
    cross_qkv_pieces, cross_out_pieces = map(assemble, gather_pieces([cross_qkv, cross_out]))
    plane_qkv_pieces, plane_out_pieces = map(assemble, gather_pieces([plane_qkv, plane_out]))
    normed = rms_norm(tokens, norm_gains[0])
    inputs = normed.reshape(-1, model_width)
    result = project(inputs, cross_qkv_pieces)
    projected = result.astype(jnp.bfloat16).reshape(sec_block, tok_block, 3 * model_width)
    own_kv = projected[:, :, model_width:]
    from_below = shifted_2(own_kv[sec_block - 1], "sec", 1)
    from_above = shifted_2(own_kv[0], "sec", -1)
    near_kv = jnp.concatenate([from_below[None], own_kv, from_above[None]], axis=0)
    queries = projected[:, :, :model_width]
    windows = tok_block // WINDOW
    query_win = queries.reshape(sec_block, windows, WINDOW, HEADS, HEAD_DIM)
    pair_win = near_kv.reshape(sec_block + 2, windows, WINDOW, 2, HEADS, HEAD_DIM)
    stacked = jnp.concatenate(
        [pair_win[0:sec_block], pair_win[1 : sec_block + 1], pair_win[2 : sec_block + 2]], axis=2
    )
    valid_win = near_valid.reshape(sec_block + 2, windows, WINDOW)
    valid_three = jnp.concatenate(
        [valid_win[0:sec_block], valid_win[1 : sec_block + 1], valid_win[2 : sec_block + 2]], axis=2
    )
    itself = jnp.arange(3 * WINDOW)[None, :] == jnp.arange(WINDOW)[:, None] + WINDOW
    scores = (
        jnp.einsum(
            "snqhd,snkhd->snhqk", query_win, stacked[:, :, :, 0], preferred_element_type=jnp.float32
        )
        * score_scale
    )
    allowed = valid_three[:, :, None, None, :] | itself[None, None, None]
    attention = masked_softmax(scores, allowed)
    context = jnp.einsum(
        "snhqk,snkhd->snqhd", attention, stacked[:, :, :, 1], preferred_element_type=jnp.float32
    )
    context = context.astype(jnp.bfloat16).reshape(-1, model_width)
    result = project(context, cross_out_pieces)
    after_cross = (tokens.reshape(-1, model_width).astype(jnp.float32) + result).astype(
        jnp.bfloat16
    )
    normed = rms_norm(after_cross, norm_gains[1])
    result = project(normed, plane_qkv_pieces)
    projected = result.astype(jnp.bfloat16).reshape(sec_block, tok_block, 3, HEADS, HEAD_DIM)
    per_device = sec_block * HEADS // plane_count
    heads_first = jnp.transpose(projected, (0, 3, 1, 2, 4)).reshape(
        plane_count, per_device, tok_block, 3 * HEAD_DIM
    )
    key_flags = jnp.broadcast_to(own_valid[:, None, :], (sec_block, HEADS, tok_block)).astype(
        jnp.bfloat16
    )
    key_flags = key_flags.reshape(plane_count, per_device, tok_block)
    attended = attend_items(
        (
            lax.all_to_all(heads_first, "plane", split_axis=0, concat_axis=2, tiled=True),
            lax.all_to_all(key_flags, "plane", split_axis=0, concat_axis=2, tiled=True),
        )
    )
    returned = lax.all_to_all(attended, "plane", split_axis=2, concat_axis=0, tiled=True)
    context = jnp.transpose(
        returned.reshape(sec_block, HEADS, tok_block, HEAD_DIM), (0, 2, 1, 3)
    ).reshape(-1, model_width)
    result = project(context, plane_out_pieces)
    encoded = (after_cross.astype(jnp.float32) + result).astype(jnp.bfloat16)
    labels = region_ids.reshape(-1)
    member = (jnp.arange(regions, dtype=jnp.int32)[:, None] == labels[None, :]) & own_valid.reshape(
        -1
    )[None, :]
    extended = jnp.concatenate([encoded, jnp.ones((encoded.shape[0], 128), jnp.bfloat16)], axis=1)
    partial = jnp.dot(member.astype(jnp.bfloat16), extended, preferred_element_type=jnp.float32)
    sections = lax.axis_size("sec")
    width = partial.shape[1]
    partial = partial.reshape(sections, plane_count, 2, width)
    me_plane = lax.axis_index("plane")
    gathered = lax.dynamic_index_in_dim(partial, me_plane, axis=1, keepdims=False)
    for step in range(1, plane_count):
        moved = [(i, (i + step) % plane_count) for i in range(plane_count)]
        target = lax.rem(me_plane + step, plane_count)
        block = lax.dynamic_index_in_dim(partial, target, axis=1, keepdims=False)
        gathered = gathered + lax.ppermute(block, "plane", moved)
    me_sec = lax.axis_index("sec")
    totals = lax.dynamic_index_in_dim(gathered, me_sec, axis=0, keepdims=False)
    for step in range(1, sections):
        moved = [(i, (i + step) % sections) for i in range(sections)]
        target = lax.rem(me_sec + step, sections)
        block = lax.dynamic_index_in_dim(gathered, target, axis=0, keepdims=False)
        totals = totals + lax.ppermute(block, "sec", moved)
    counted = totals[:, model_width]
    pooled = totals[:, :model_width] / jnp.maximum(counted, 1.0)[:, None]
    return (encoded.reshape(sec_block, tok_block, model_width), pooled)


def solution(mesh):
    in_specs = (
        P(("groups", "sec"), "plane", None),
        P("groups"),
        P(("groups", "sec"), "plane"),
        P(),
        P("plane", None),
        P("plane", None),
        P("plane", None),
        P("plane", None),
    )
    out_specs = (P(("groups", "sec"), "plane", None), P(("groups", "sec", "plane"), None))
    return jax.shard_map(body, mesh=mesh, in_specs=in_specs, out_specs=out_specs, check_vma=False)
```

```python
import math

import jax
import jax.numpy as jnp
from jax import lax
from jax.sharding import PartitionSpec as P

HEADS = 16
HEAD_DIM = 64
WINDOW = 128


negative_big = -1e30


def shifted_2(value, axis, by):
    peers = lax.axis_size(axis)
    pairs = [(i, i + by) for i in range(peers) if 0 <= i + by < peers]
    return lax.ppermute(value, axis, pairs)


def rms_norm(values, gain):
    wide = values.astype(jnp.float32)
    scaled = wide * lax.rsqrt(jnp.mean(wide * wide, axis=-1, keepdims=True) + 1e-06) * gain
    return scaled.astype(jnp.bfloat16)


def masked_softmax(scores, allowed):
    shifted = jnp.where(allowed, scores, negative_big)
    top = jnp.max(shifted, axis=-1, keepdims=True)
    expo = jnp.where(allowed, jnp.exp(shifted - top), 0.0)
    return (expo / jnp.sum(expo, axis=-1, keepdims=True)).astype(jnp.bfloat16)


def fold_product(inputs, weight_piece):
    return jnp.dot(inputs, weight_piece, preferred_element_type=jnp.float32)


def replica_levels():
    levels = []
    if lax.axis_size("groups") % 2 == 0:
        levels.append(("groups", lax.axis_size("groups"), 1))
    if lax.axis_size("sec") % 4 == 0:
        levels.append(("sec", lax.axis_size("sec"), 2))
    if lax.axis_size("sec") % 2 == 0:
        levels.append(("sec", lax.axis_size("sec"), 1))
    return levels


def rotate_rows(values, axis):
    plane_count = lax.axis_size("plane")
    block = values.shape[axis] // plane_count
    start = (lax.axis_index("plane") + 1) * block
    doubled = jnp.concatenate([values, values], axis=axis)
    return lax.dynamic_slice_in_dim(doubled, start, (plane_count - 1) * block, axis=axis)


def gather_pieces(shards):
    levels = replica_levels()
    count = 2 ** len(levels)
    widths = [shard.shape[1] // count for shard in shards]
    own = 0
    for bit, (axis, _, flip) in enumerate(levels):
        own = own + ((lax.axis_index(axis) // flip) % 2) * (2 ** bit)
    mine = jnp.concatenate(
        [
            lax.dynamic_slice_in_dim(shard, own * width, width, axis=1)
            for shard, width in zip(shards, widths)
        ],
        axis=1,
    )
    gathered = lax.all_gather(mine, "plane", axis=0, tiled=True)
    held = [(own, rotate_rows(gathered, 0))]
    direct = levels[:-1] if len(levels) > 1 else []
    if direct:
        axes = tuple(dict.fromkeys(axis for axis, _, _ in direct))
        sizes = {axis: lax.axis_size(axis) for axis in axes}
        total = 1
        for axis in axes:
            total *= sizes[axis]
        first_block = held[0][1]
        for mask in range(1, 2 ** len(direct)):
            pairs = []
            for linear in range(total):
                coords = {}
                rest = linear
                for axis in reversed(axes):
                    coords[axis] = rest % sizes[axis]
                    rest //= sizes[axis]
                for bit, (axis, _, flip) in enumerate(direct):
                    if mask & (1 << bit):
                        coords[axis] = coords[axis] ^ flip
                target = 0
                for axis in axes:
                    target = target * sizes[axis] + coords[axis]
                pairs.append((linear, target))
            held.append((lax.bitwise_xor(own, mask), lax.ppermute(first_block, axes, pairs)))
    for bit in range(len(direct), len(levels)):
        axis, size, flip = levels[bit]
        swap = [(i, i ^ flip) for i in range(size)]
        held = held + [
            (lax.bitwise_xor(piece, 2 ** bit), lax.ppermute(block, axis, swap))
            for piece, block in held
        ]
    results = []
    offset = 0
    for shard, width in zip(shards, widths):
        results.append((shard, [(piece, block[:, offset : offset + width]) for piece, block in held], width))
        offset += width
    return results


def project(inputs, pieces):
    shard, held, width = pieces
    rows = shard.shape[0]
    local_inputs = lax.dynamic_slice_in_dim(inputs, lax.axis_index("plane") * rows, rows, axis=1)
    local = jnp.dot(local_inputs, shard, preferred_element_type=jnp.float32)
    remote_inputs = rotate_rows(inputs, 1)
    remote = jnp.zeros_like(local)
    for piece, block in held:
        part = jnp.dot(remote_inputs, block, preferred_element_type=jnp.float32)
        remote = lax.dynamic_update_slice_in_dim(remote, part, piece * width, axis=1)
    return local + remote


def attend_items(pieces):
    packed_all, flags_all = pieces
    seq_len = packed_all.shape[2]
    block_len = 512
    score_scale = 1.0 / math.sqrt(HEAD_DIM)
    key_index = jnp.arange(seq_len, dtype=jnp.int32)

    def one_item(item_pair):
        packed, key_flag = item_pair
        key_rows = packed[:, HEAD_DIM : 2 * HEAD_DIM]
        value_rows = packed[:, 2 * HEAD_DIM :]
        key_alive = key_flag > 0.5
        query_blocks = packed[:, :HEAD_DIM].reshape(seq_len // block_len, block_len, HEAD_DIM)
        block_starts = jnp.arange(seq_len // block_len, dtype=jnp.int32) * block_len

        def one_block(block_pair):
            query_rows, offset = block_pair
            scores = (
                jnp.einsum("qd,kd->qk", query_rows, key_rows, preferred_element_type=jnp.float32)
                * score_scale
            )
            own_index = offset + jnp.arange(block_len, dtype=jnp.int32)
            allowed = key_alive[None, :] | (key_index[None, :] == own_index[:, None])
            attention = masked_softmax(scores, allowed)
            return jnp.dot(attention, value_rows, preferred_element_type=jnp.float32).astype(
                jnp.bfloat16
            )

        return lax.map(one_block, (query_blocks, block_starts)).reshape(seq_len, HEAD_DIM)

    return lax.map(one_item, (packed_all[0], flags_all[0]))[None]


def body(tokens, counts, region_ids, norm_gains, cross_qkv, cross_out, plane_qkv, plane_out):
    sec_block, tok_block, model_width = tokens.shape
    plane_count = lax.axis_size("plane")
    regions = 2 * lax.axis_size("sec") * plane_count
    positions = lax.axis_index("plane") * tok_block + jnp.arange(tok_block, dtype=jnp.int32)
    padded_counts = jnp.concatenate(
        [jnp.zeros((1,), jnp.int32), counts, jnp.zeros((1,), jnp.int32)]
    )
    near_counts = lax.dynamic_slice_in_dim(
        padded_counts, lax.axis_index("sec") * sec_block, sec_block + 2
    )
    near_valid = positions[None, :] < near_counts[:, None]
    own_valid = near_valid[1 : sec_block + 1]
    score_scale = 1.0 / math.sqrt(HEAD_DIM)
    cross_qkv_pieces, cross_out_pieces = gather_pieces([cross_qkv, cross_out])
    plane_qkv_pieces, plane_out_pieces = gather_pieces([plane_qkv, plane_out])
    normed = rms_norm(tokens, norm_gains[0])
    inputs = normed.reshape(-1, model_width)
    result = project(inputs, cross_qkv_pieces)
    projected = result.astype(jnp.bfloat16).reshape(sec_block, tok_block, 3 * model_width)
    own_kv = projected[:, :, model_width:]
    from_below = shifted_2(own_kv[sec_block - 1], "sec", 1)
    from_above = shifted_2(own_kv[0], "sec", -1)
    near_kv = jnp.concatenate([from_below[None], own_kv, from_above[None]], axis=0)
    queries = projected[:, :, :model_width]
    windows = tok_block // WINDOW
    query_win = queries.reshape(sec_block, windows, WINDOW, HEADS, HEAD_DIM)
    pair_win = near_kv.reshape(sec_block + 2, windows, WINDOW, 2, HEADS, HEAD_DIM)
    stacked = jnp.concatenate(
        [pair_win[0:sec_block], pair_win[1 : sec_block + 1], pair_win[2 : sec_block + 2]], axis=2
    )
    valid_win = near_valid.reshape(sec_block + 2, windows, WINDOW)
    valid_three = jnp.concatenate(
        [valid_win[0:sec_block], valid_win[1 : sec_block + 1], valid_win[2 : sec_block + 2]], axis=2
    )
    itself = jnp.arange(3 * WINDOW)[None, :] == jnp.arange(WINDOW)[:, None] + WINDOW
    scores = (
        jnp.einsum(
            "snqhd,snkhd->snhqk", query_win, stacked[:, :, :, 0], preferred_element_type=jnp.float32
        )
        * score_scale
    )
    allowed = valid_three[:, :, None, None, :] | itself[None, None, None]
    attention = masked_softmax(scores, allowed)
    context = jnp.einsum(
        "snhqk,snkhd->snqhd", attention, stacked[:, :, :, 1], preferred_element_type=jnp.float32
    )
    context = context.astype(jnp.bfloat16).reshape(-1, model_width)
    result = project(context, cross_out_pieces)
    after_cross = (tokens.reshape(-1, model_width).astype(jnp.float32) + result).astype(
        jnp.bfloat16
    )
    normed = rms_norm(after_cross, norm_gains[1])
    result = project(normed, plane_qkv_pieces)
    projected = result.astype(jnp.bfloat16).reshape(sec_block, tok_block, 3, HEADS, HEAD_DIM)
    per_device = sec_block * HEADS // plane_count
    heads_first = jnp.transpose(projected, (0, 3, 1, 2, 4)).reshape(
        plane_count, per_device, tok_block, 3 * HEAD_DIM
    )
    key_flags = jnp.broadcast_to(own_valid[:, None, :], (sec_block, HEADS, tok_block)).astype(
        jnp.bfloat16
    )
    key_flags = key_flags.reshape(plane_count, per_device, tok_block)
    attended = attend_items(
        (
            lax.all_to_all(heads_first, "plane", split_axis=0, concat_axis=2, tiled=True),
            lax.all_to_all(key_flags, "plane", split_axis=0, concat_axis=2, tiled=True),
        )
    )
    returned = lax.all_to_all(attended, "plane", split_axis=2, concat_axis=0, tiled=True)
    context = jnp.transpose(
        returned.reshape(sec_block, HEADS, tok_block, HEAD_DIM), (0, 2, 1, 3)
    ).reshape(-1, model_width)
    result = project(context, plane_out_pieces)
    encoded = (after_cross.astype(jnp.float32) + result).astype(jnp.bfloat16)
    labels = region_ids.reshape(-1)
    member = (jnp.arange(regions, dtype=jnp.int32)[:, None] == labels[None, :]) & own_valid.reshape(
        -1
    )[None, :]
    extended = jnp.concatenate([encoded, jnp.ones((encoded.shape[0], 128), jnp.bfloat16)], axis=1)
    partial = jnp.dot(member.astype(jnp.bfloat16), extended, preferred_element_type=jnp.float32)
    sections = lax.axis_size("sec")
    width = partial.shape[1]
    partial = partial.reshape(sections, plane_count, 2, width)
    me_plane = lax.axis_index("plane")
    gathered = lax.dynamic_index_in_dim(partial, me_plane, axis=1, keepdims=False)
    for step in range(1, plane_count):
        moved = [(i, (i + step) % plane_count) for i in range(plane_count)]
        target = lax.rem(me_plane + step, plane_count)
        block = lax.dynamic_index_in_dim(partial, target, axis=1, keepdims=False)
        gathered = gathered + lax.ppermute(block, "plane", moved)
    me_sec = lax.axis_index("sec")
    totals = lax.dynamic_index_in_dim(gathered, me_sec, axis=0, keepdims=False)
    for step in range(1, sections):
        moved = [(i, (i + step) % sections) for i in range(sections)]
        target = lax.rem(me_sec + step, sections)
        block = lax.dynamic_index_in_dim(gathered, target, axis=0, keepdims=False)
        totals = totals + lax.ppermute(block, "sec", moved)
    counted = totals[:, model_width]
    pooled = totals[:, :model_width] / jnp.maximum(counted, 1.0)[:, None]
    return (encoded.reshape(sec_block, tok_block, model_width), pooled)


def solution(mesh):
    in_specs = (
        P(("groups", "sec"), "plane", None),
        P("groups"),
        P(("groups", "sec"), "plane"),
        P(),
        P("plane", None),
        P("plane", None),
        P("plane", None),
        P("plane", None),
    )
    out_specs = (P(("groups", "sec"), "plane", None), P(("groups", "sec", "plane"), None))
    return jax.shard_map(body, mesh=mesh, in_specs=in_specs, out_specs=out_specs, check_vma=False)
```

```python
import math

import jax
import jax.numpy as jnp
from jax import lax
from jax.sharding import PartitionSpec as P

HEADS = 16
HEAD_DIM = 64
WINDOW = 128


negative_big = -1e30


def shifted_2(value, axis, by):
    peers = lax.axis_size(axis)
    pairs = [(i, i + by) for i in range(peers) if 0 <= i + by < peers]
    return lax.ppermute(value, axis, pairs)


def rms_norm(values, gain):
    wide = values.astype(jnp.float32)
    scaled = wide * lax.rsqrt(jnp.mean(wide * wide, axis=-1, keepdims=True) + 1e-06) * gain
    return scaled.astype(jnp.bfloat16)


def masked_softmax(scores, allowed):
    shifted = jnp.where(allowed, scores, negative_big)
    top = jnp.max(shifted, axis=-1, keepdims=True)
    expo = jnp.where(allowed, jnp.exp(shifted - top), 0.0)
    return (expo / jnp.sum(expo, axis=-1, keepdims=True)).astype(jnp.bfloat16)


def fold_product(inputs, weight_piece):
    return jnp.dot(inputs, weight_piece, preferred_element_type=jnp.float32)


def replica_levels():
    levels = []
    if lax.axis_size("groups") % 2 == 0:
        levels.append(("groups", lax.axis_size("groups"), 1))
    if lax.axis_size("sec") % 4 == 0:
        levels.append(("sec", lax.axis_size("sec"), 2))
    if lax.axis_size("sec") % 2 == 0:
        levels.append(("sec", lax.axis_size("sec"), 1))
    return levels


def rotate_rows(values, axis):
    plane_count = lax.axis_size("plane")
    block = values.shape[axis] // plane_count
    start = (lax.axis_index("plane") + 1) * block
    doubled = jnp.concatenate([values, values], axis=axis)
    return lax.dynamic_slice_in_dim(doubled, start, (plane_count - 1) * block, axis=axis)


def gather_pieces(shards):
    levels = replica_levels()
    count = 2 ** len(levels)
    widths = [shard.shape[1] // count for shard in shards]
    own = 0
    for bit, (axis, _, flip) in enumerate(levels):
        own = own + ((lax.axis_index(axis) // flip) % 2) * (2 ** bit)
    mine = jnp.concatenate(
        [
            lax.dynamic_slice_in_dim(shard, own * width, width, axis=1)
            for shard, width in zip(shards, widths)
        ],
        axis=1,
    )
    gathered = lax.all_gather(mine, "plane", axis=0, tiled=True)
    held = [(own, rotate_rows(gathered, 0))]
    for bit, (axis, size, flip) in enumerate(levels):
        swap = [(i, i ^ flip) for i in range(size)]
        held = held + [
            (piece + (1 - 2 * ((piece // 2 ** bit) % 2)) * 2 ** bit, lax.ppermute(block, axis, swap))
            for piece, block in held
        ]
    results = []
    offset = 0
    for shard, width in zip(shards, widths):
        results.append((shard, [(piece, block[:, offset : offset + width]) for piece, block in held], width))
        offset += width
    return results


def project(inputs, pieces):
    shard, held, width = pieces
    rows = shard.shape[0]
    local_inputs = lax.dynamic_slice_in_dim(inputs, lax.axis_index("plane") * rows, rows, axis=1)
    local = jnp.dot(local_inputs, shard, preferred_element_type=jnp.float32)
    remote_inputs = rotate_rows(inputs, 1)
    remote = jnp.zeros_like(local)
    for piece, block in held:
        part = jnp.dot(remote_inputs, block, preferred_element_type=jnp.float32)
        remote = lax.dynamic_update_slice_in_dim(remote, part, piece * width, axis=1)
    return local + remote


def attend_items(pieces):
    packed_all, flags_all = pieces
    seq_len = packed_all.shape[2]
    block_len = 512
    score_scale = 1.0 / math.sqrt(HEAD_DIM)
    key_index = jnp.arange(seq_len, dtype=jnp.int32)

    def one_item(item_pair):
        packed, key_flag = item_pair
        key_rows = packed[:, HEAD_DIM : 2 * HEAD_DIM]
        value_rows = packed[:, 2 * HEAD_DIM :]
        key_alive = key_flag > 0.5
        query_blocks = packed[:, :HEAD_DIM].reshape(seq_len // block_len, block_len, HEAD_DIM)
        block_starts = jnp.arange(seq_len // block_len, dtype=jnp.int32) * block_len

        def one_block(block_pair):
            query_rows, offset = block_pair
            scores = (
                jnp.einsum("qd,kd->qk", query_rows, key_rows, preferred_element_type=jnp.float32)
                * score_scale
            )
            own_index = offset + jnp.arange(block_len, dtype=jnp.int32)
            allowed = key_alive[None, :] | (key_index[None, :] == own_index[:, None])
            attention = masked_softmax(scores, allowed)
            return jnp.dot(attention, value_rows, preferred_element_type=jnp.float32).astype(
                jnp.bfloat16
            )

        return lax.map(one_block, (query_blocks, block_starts)).reshape(seq_len, HEAD_DIM)

    return lax.map(one_item, (packed_all[0], flags_all[0]))[None]


def attend_by_section(projected, counts, plane_count):
    sec_block, tok_block = projected.shape[0], projected.shape[1]
    share = HEADS // plane_count
    seq_len = plane_count * tok_block
    score_scale = 1.0 / math.sqrt(HEAD_DIM)
    key_index = jnp.arange(seq_len, dtype=jnp.int32)
    contexts = []
    for local in range(sec_block):
        section = lax.axis_index("sec") * sec_block + local
        key_alive = key_index < lax.dynamic_index_in_dim(counts, section, keepdims=False)
        outgoing = jnp.transpose(
            projected[local].reshape(tok_block, 3, plane_count, share, HEAD_DIM), (2, 3, 0, 1, 4)
        ).reshape(plane_count, share, tok_block, 3 * HEAD_DIM)
        packed = lax.all_to_all(outgoing, "plane", split_axis=0, concat_axis=2, tiled=True)[0]
        queries = packed[:, :, :HEAD_DIM]
        keys = packed[:, :, HEAD_DIM : 2 * HEAD_DIM]
        values = packed[:, :, 2 * HEAD_DIM :]
        scores = (
            jnp.einsum("nqd,nkd->nqk", queries, keys, preferred_element_type=jnp.float32)
            * score_scale
        )
        allowed = key_alive[None, None, :] | (key_index[None, None, :] == key_index[None, :, None])
        attention = masked_softmax(scores, allowed)
        context = jnp.einsum(
            "nqk,nkd->nqd", attention, values, preferred_element_type=jnp.float32
        ).astype(jnp.bfloat16)
        homeward = jnp.transpose(
            context.reshape(share, plane_count, tok_block, HEAD_DIM), (1, 0, 2, 3)
        )
        returned = lax.all_to_all(homeward, "plane", split_axis=0, concat_axis=1, tiled=True)[0]
        contexts.append(jnp.transpose(returned, (1, 0, 2)).reshape(tok_block, HEADS * HEAD_DIM))
    return jnp.concatenate(contexts, axis=0)


def body(tokens, counts, region_ids, norm_gains, cross_qkv, cross_out, plane_qkv, plane_out):
    sec_block, tok_block, model_width = tokens.shape
    plane_count = lax.axis_size("plane")
    regions = 2 * lax.axis_size("sec") * plane_count
    positions = lax.axis_index("plane") * tok_block + jnp.arange(tok_block, dtype=jnp.int32)
    padded_counts = jnp.concatenate(
        [jnp.zeros((1,), jnp.int32), counts, jnp.zeros((1,), jnp.int32)]
    )
    near_counts = lax.dynamic_slice_in_dim(
        padded_counts, lax.axis_index("sec") * sec_block, sec_block + 2
    )
    near_valid = positions[None, :] < near_counts[:, None]
    own_valid = near_valid[1 : sec_block + 1]
    score_scale = 1.0 / math.sqrt(HEAD_DIM)
    cross_qkv_pieces, cross_out_pieces = gather_pieces([cross_qkv, cross_out])
    plane_qkv_pieces, plane_out_pieces = gather_pieces([plane_qkv, plane_out])
    normed = rms_norm(tokens, norm_gains[0])
    inputs = normed.reshape(-1, model_width)
    result = project(inputs, cross_qkv_pieces)
    projected = result.astype(jnp.bfloat16).reshape(sec_block, tok_block, 3 * model_width)
    own_kv = projected[:, :, model_width:]
    from_below = shifted_2(own_kv[sec_block - 1], "sec", 1)
    from_above = shifted_2(own_kv[0], "sec", -1)
    near_kv = jnp.concatenate([from_below[None], own_kv, from_above[None]], axis=0)
    queries = projected[:, :, :model_width]
    windows = tok_block // WINDOW
    query_win = queries.reshape(sec_block, windows, WINDOW, HEADS, HEAD_DIM)
    pair_win = near_kv.reshape(sec_block + 2, windows, WINDOW, 2, HEADS, HEAD_DIM)
    stacked = jnp.concatenate(
        [pair_win[0:sec_block], pair_win[1 : sec_block + 1], pair_win[2 : sec_block + 2]], axis=2
    )
    valid_win = near_valid.reshape(sec_block + 2, windows, WINDOW)
    valid_three = jnp.concatenate(
        [valid_win[0:sec_block], valid_win[1 : sec_block + 1], valid_win[2 : sec_block + 2]], axis=2
    )
    itself = jnp.arange(3 * WINDOW)[None, :] == jnp.arange(WINDOW)[:, None] + WINDOW
    scores = (
        jnp.einsum(
            "snqhd,snkhd->snhqk", query_win, stacked[:, :, :, 0], preferred_element_type=jnp.float32
        )
        * score_scale
    )
    allowed = valid_three[:, :, None, None, :] | itself[None, None, None]
    attention = masked_softmax(scores, allowed)
    context = jnp.einsum(
        "snhqk,snkhd->snqhd", attention, stacked[:, :, :, 1], preferred_element_type=jnp.float32
    )
    context = context.astype(jnp.bfloat16).reshape(-1, model_width)
    result = project(context, cross_out_pieces)
    after_cross = (tokens.reshape(-1, model_width).astype(jnp.float32) + result).astype(
        jnp.bfloat16
    )
    normed = rms_norm(after_cross, norm_gains[1])
    result = project(normed, plane_qkv_pieces)
    projected = result.astype(jnp.bfloat16).reshape(sec_block, tok_block, 3, HEADS, HEAD_DIM)
    if HEADS % plane_count == 0:
        context = attend_by_section(projected, counts, plane_count)
    else:
        per_device = sec_block * HEADS // plane_count
        heads_first = jnp.transpose(projected, (0, 3, 1, 2, 4)).reshape(
            plane_count, per_device, tok_block, 3 * HEAD_DIM
        )
        key_flags = jnp.broadcast_to(own_valid[:, None, :], (sec_block, HEADS, tok_block)).astype(
            jnp.bfloat16
        )
        key_flags = key_flags.reshape(plane_count, per_device, tok_block)
        attended = attend_items(
            (
                lax.all_to_all(heads_first, "plane", split_axis=0, concat_axis=2, tiled=True),
                lax.all_to_all(key_flags, "plane", split_axis=0, concat_axis=2, tiled=True),
            )
        )
        returned = lax.all_to_all(attended, "plane", split_axis=2, concat_axis=0, tiled=True)
        context = jnp.transpose(
            returned.reshape(sec_block, HEADS, tok_block, HEAD_DIM), (0, 2, 1, 3)
        ).reshape(-1, model_width)
    result = project(context, plane_out_pieces)
    encoded = (after_cross.astype(jnp.float32) + result).astype(jnp.bfloat16)
    labels = region_ids.reshape(-1)
    member = (jnp.arange(regions, dtype=jnp.int32)[:, None] == labels[None, :]) & own_valid.reshape(
        -1
    )[None, :]
    extended = jnp.concatenate([encoded, jnp.ones((encoded.shape[0], 128), jnp.bfloat16)], axis=1)
    partial = jnp.dot(member.astype(jnp.bfloat16), extended, preferred_element_type=jnp.float32)
    sections = lax.axis_size("sec")
    width = partial.shape[1]
    partial = partial.reshape(sections, plane_count, 2, width)
    me_plane = lax.axis_index("plane")
    gathered = lax.dynamic_index_in_dim(partial, me_plane, axis=1, keepdims=False)
    for step in range(1, plane_count):
        moved = [(i, (i + step) % plane_count) for i in range(plane_count)]
        target = lax.rem(me_plane + step, plane_count)
        block = lax.dynamic_index_in_dim(partial, target, axis=1, keepdims=False)
        gathered = gathered + lax.ppermute(block, "plane", moved)
    me_sec = lax.axis_index("sec")
    totals = lax.dynamic_index_in_dim(gathered, me_sec, axis=0, keepdims=False)
    for step in range(1, sections):
        moved = [(i, (i + step) % sections) for i in range(sections)]
        target = lax.rem(me_sec + step, sections)
        block = lax.dynamic_index_in_dim(gathered, target, axis=0, keepdims=False)
        totals = totals + lax.ppermute(block, "sec", moved)
    counted = totals[:, model_width]
    pooled = totals[:, :model_width] / jnp.maximum(counted, 1.0)[:, None]
    return (encoded.reshape(sec_block, tok_block, model_width), pooled)


def solution(mesh):
    in_specs = (
        P(("groups", "sec"), "plane", None),
        P("groups"),
        P(("groups", "sec"), "plane"),
        P(),
        P("plane", None),
        P("plane", None),
        P("plane", None),
        P("plane", None),
    )
    out_specs = (P(("groups", "sec"), "plane", None), P(("groups", "sec", "plane"), None))
    return jax.shard_map(body, mesh=mesh, in_specs=in_specs, out_specs=out_specs, check_vma=False)
```

```python
import math

import jax
import jax.numpy as jnp
from jax import lax
from jax.sharding import PartitionSpec as P

HEADS = 16
HEAD_DIM = 64
WINDOW = 128


negative_big = -1e30


def shifted_2(value, axis, by):
    peers = lax.axis_size(axis)
    pairs = [(i, i + by) for i in range(peers) if 0 <= i + by < peers]
    return lax.ppermute(value, axis, pairs)


def rms_norm(values, gain):
    wide = values.astype(jnp.float32)
    scaled = wide * lax.rsqrt(jnp.mean(wide * wide, axis=-1, keepdims=True) + 1e-06) * gain
    return scaled.astype(jnp.bfloat16)


def masked_softmax(scores, allowed):
    shifted = jnp.where(allowed, scores, negative_big)
    top = jnp.max(shifted, axis=-1, keepdims=True)
    expo = jnp.where(allowed, jnp.exp(shifted - top), 0.0)
    return (expo / jnp.sum(expo, axis=-1, keepdims=True)).astype(jnp.bfloat16)


def fold_product(inputs, weight_piece):
    return jnp.dot(inputs, weight_piece, preferred_element_type=jnp.float32)


def replica_levels():
    levels = []
    if lax.axis_size("groups") % 2 == 0:
        levels.append(("groups", lax.axis_size("groups"), 1))
    if lax.axis_size("sec") % 4 == 0:
        levels.append(("sec", lax.axis_size("sec"), 2))
    if lax.axis_size("sec") % 2 == 0:
        levels.append(("sec", lax.axis_size("sec"), 1))
    return levels


def rotate_rows(values, axis):
    plane_count = lax.axis_size("plane")
    block = values.shape[axis] // plane_count
    start = (lax.axis_index("plane") + 1) * block
    doubled = jnp.concatenate([values, values], axis=axis)
    return lax.dynamic_slice_in_dim(doubled, start, (plane_count - 1) * block, axis=axis)


def gather_pieces(shards):
    levels = replica_levels()
    count = 2 ** len(levels)
    widths = [shard.shape[1] // count for shard in shards]
    own = 0
    for bit, (axis, _, flip) in enumerate(levels):
        own = own + ((lax.axis_index(axis) // flip) % 2) * (2 ** bit)
    mine = jnp.concatenate(
        [
            lax.dynamic_slice_in_dim(shard, own * width, width, axis=1)
            for shard, width in zip(shards, widths)
        ],
        axis=1,
    )
    gathered = lax.all_gather(mine, "plane", axis=0, tiled=True)
    held = [(own, rotate_rows(gathered, 0))]
    for bit, (axis, size, flip) in enumerate(levels):
        swap = [(i, i ^ flip) for i in range(size)]
        held = held + [
            (piece + (1 - 2 * ((piece // 2 ** bit) % 2)) * 2 ** bit, lax.ppermute(block, axis, swap))
            for piece, block in held
        ]
    results = []
    offset = 0
    for shard, width in zip(shards, widths):
        results.append((shard, [(piece, block[:, offset : offset + width]) for piece, block in held], width))
        offset += width
    return results


def project(inputs, pieces):
    shard, held, width = pieces
    rows = shard.shape[0]
    local_inputs = lax.dynamic_slice_in_dim(inputs, lax.axis_index("plane") * rows, rows, axis=1)
    local = jnp.dot(local_inputs, shard, preferred_element_type=jnp.float32)
    remote_inputs = rotate_rows(inputs, 1)
    remote = jnp.zeros_like(local)
    for piece, block in held:
        part = jnp.dot(remote_inputs, block, preferred_element_type=jnp.float32)
        remote = lax.dynamic_update_slice_in_dim(remote, part, piece * width, axis=1)
    return local + remote


def assemble(pieces):
    shard, held, width = pieces
    remote = jnp.zeros((held[0][1].shape[0], width * len(held)), shard.dtype)
    for piece, block in held:
        remote = lax.dynamic_update_slice_in_dim(remote, block, piece * width, axis=1)
    return shard, remote


def project_whole(inputs, weights):
    shard, remote = weights
    rows = shard.shape[0]
    local_inputs = lax.dynamic_slice_in_dim(inputs, lax.axis_index("plane") * rows, rows, axis=1)
    local = jnp.dot(local_inputs, shard, preferred_element_type=jnp.float32)
    return local + jnp.dot(rotate_rows(inputs, 1), remote, preferred_element_type=jnp.float32)


def attend_items(pieces):
    packed_all, flags_all = pieces
    seq_len = packed_all.shape[2]
    block_len = 512
    score_scale = 1.0 / math.sqrt(HEAD_DIM)
    key_index = jnp.arange(seq_len, dtype=jnp.int32)

    def one_item(item_pair):
        packed, key_flag = item_pair
        key_rows = packed[:, HEAD_DIM : 2 * HEAD_DIM]
        value_rows = packed[:, 2 * HEAD_DIM :]
        key_alive = key_flag > 0.5
        query_blocks = packed[:, :HEAD_DIM].reshape(seq_len // block_len, block_len, HEAD_DIM)
        block_starts = jnp.arange(seq_len // block_len, dtype=jnp.int32) * block_len

        def one_block(block_pair):
            query_rows, offset = block_pair
            scores = (
                jnp.einsum("qd,kd->qk", query_rows, key_rows, preferred_element_type=jnp.float32)
                * score_scale
            )
            own_index = offset + jnp.arange(block_len, dtype=jnp.int32)
            allowed = key_alive[None, :] | (key_index[None, :] == own_index[:, None])
            attention = masked_softmax(scores, allowed)
            return jnp.dot(attention, value_rows, preferred_element_type=jnp.float32).astype(
                jnp.bfloat16
            )

        return lax.map(one_block, (query_blocks, block_starts)).reshape(seq_len, HEAD_DIM)

    return lax.map(one_item, (packed_all[0], flags_all[0]))[None]


def attend_by_section(projected, counts, plane_count):
    sec_block, tok_block = projected.shape[0], projected.shape[1]
    share = HEADS // plane_count
    seq_len = plane_count * tok_block
    score_scale = 1.0 / math.sqrt(HEAD_DIM)
    key_index = jnp.arange(seq_len, dtype=jnp.int32)
    contexts = []
    for local in range(sec_block):
        section = lax.axis_index("sec") * sec_block + local
        key_alive = key_index < lax.dynamic_index_in_dim(counts, section, keepdims=False)
        outgoing = jnp.transpose(
            projected[local].reshape(tok_block, 3, plane_count, share, HEAD_DIM), (2, 3, 0, 1, 4)
        ).reshape(plane_count, share, tok_block, 3 * HEAD_DIM)
        packed = lax.all_to_all(outgoing, "plane", split_axis=0, concat_axis=2, tiled=True)[0]
        queries = packed[:, :, :HEAD_DIM]
        keys = packed[:, :, HEAD_DIM : 2 * HEAD_DIM]
        values = packed[:, :, 2 * HEAD_DIM :]
        scores = (
            jnp.einsum("nqd,nkd->nqk", queries, keys, preferred_element_type=jnp.float32)
            * score_scale
        )
        allowed = key_alive[None, None, :] | (key_index[None, None, :] == key_index[None, :, None])
        attention = masked_softmax(scores, allowed)
        context = jnp.einsum(
            "nqk,nkd->nqd", attention, values, preferred_element_type=jnp.float32
        ).astype(jnp.bfloat16)
        homeward = jnp.transpose(
            context.reshape(share, plane_count, tok_block, HEAD_DIM), (1, 0, 2, 3)
        )
        returned = lax.all_to_all(homeward, "plane", split_axis=0, concat_axis=1, tiled=True)[0]
        contexts.append(jnp.transpose(returned, (1, 0, 2)).reshape(tok_block, HEADS * HEAD_DIM))
    return contexts


def body(tokens, counts, region_ids, norm_gains, cross_qkv, cross_out, plane_qkv, plane_out):
    sec_block, tok_block, model_width = tokens.shape
    plane_count = lax.axis_size("plane")
    regions = 2 * lax.axis_size("sec") * plane_count
    positions = lax.axis_index("plane") * tok_block + jnp.arange(tok_block, dtype=jnp.int32)
    padded_counts = jnp.concatenate(
        [jnp.zeros((1,), jnp.int32), counts, jnp.zeros((1,), jnp.int32)]
    )
    near_counts = lax.dynamic_slice_in_dim(
        padded_counts, lax.axis_index("sec") * sec_block, sec_block + 2
    )
    near_valid = positions[None, :] < near_counts[:, None]
    own_valid = near_valid[1 : sec_block + 1]
    score_scale = 1.0 / math.sqrt(HEAD_DIM)
    cross_qkv_pieces, cross_out_pieces = gather_pieces([cross_qkv, cross_out])
    plane_qkv_pieces, plane_out_pieces = gather_pieces([plane_qkv, plane_out])
    cross_out_pieces = assemble(cross_out_pieces)
    plane_out_pieces = assemble(plane_out_pieces)
    normed = rms_norm(tokens, norm_gains[0])
    inputs = normed.reshape(-1, model_width)
    result = project(inputs, cross_qkv_pieces)
    projected = result.astype(jnp.bfloat16).reshape(sec_block, tok_block, 3 * model_width)
    own_kv = projected[:, :, model_width:]
    from_below = shifted_2(own_kv[sec_block - 1], "sec", 1)
    from_above = shifted_2(own_kv[0], "sec", -1)
    near_kv = jnp.concatenate([from_below[None], own_kv, from_above[None]], axis=0)
    queries = projected[:, :, :model_width]
    windows = tok_block // WINDOW
    query_win = queries.reshape(sec_block, windows, WINDOW, HEADS, HEAD_DIM)
    pair_win = near_kv.reshape(sec_block + 2, windows, WINDOW, 2, HEADS, HEAD_DIM)
    stacked = jnp.concatenate(
        [pair_win[0:sec_block], pair_win[1 : sec_block + 1], pair_win[2 : sec_block + 2]], axis=2
    )
    valid_win = near_valid.reshape(sec_block + 2, windows, WINDOW)
    valid_three = jnp.concatenate(
        [valid_win[0:sec_block], valid_win[1 : sec_block + 1], valid_win[2 : sec_block + 2]], axis=2
    )
    itself = jnp.arange(3 * WINDOW)[None, :] == jnp.arange(WINDOW)[:, None] + WINDOW
    scores = (
        jnp.einsum(
            "snqhd,snkhd->snhqk", query_win, stacked[:, :, :, 0], preferred_element_type=jnp.float32
        )
        * score_scale
    )
    allowed = valid_three[:, :, None, None, :] | itself[None, None, None]
    attention = masked_softmax(scores, allowed)
    context = jnp.einsum(
        "snhqk,snkhd->snqhd", attention, stacked[:, :, :, 1], preferred_element_type=jnp.float32
    )
    context = context.astype(jnp.bfloat16).reshape(-1, model_width)
    result = project_whole(context, cross_out_pieces)
    after_cross = (tokens.reshape(-1, model_width).astype(jnp.float32) + result).astype(
        jnp.bfloat16
    )
    normed = rms_norm(after_cross, norm_gains[1])
    result = project(normed, plane_qkv_pieces)
    projected = result.astype(jnp.bfloat16).reshape(sec_block, tok_block, 3, HEADS, HEAD_DIM)
    if HEADS % plane_count == 0:
        contexts = attend_by_section(projected, counts, plane_count)
    else:
        per_device = sec_block * HEADS // plane_count
        heads_first = jnp.transpose(projected, (0, 3, 1, 2, 4)).reshape(
            plane_count, per_device, tok_block, 3 * HEAD_DIM
        )
        key_flags = jnp.broadcast_to(own_valid[:, None, :], (sec_block, HEADS, tok_block)).astype(
            jnp.bfloat16
        )
        key_flags = key_flags.reshape(plane_count, per_device, tok_block)
        attended = attend_items(
            (
                lax.all_to_all(heads_first, "plane", split_axis=0, concat_axis=2, tiled=True),
                lax.all_to_all(key_flags, "plane", split_axis=0, concat_axis=2, tiled=True),
            )
        )
        returned = lax.all_to_all(attended, "plane", split_axis=2, concat_axis=0, tiled=True)
        contexts = [
            jnp.transpose(
                returned.reshape(sec_block, HEADS, tok_block, HEAD_DIM), (0, 2, 1, 3)
            ).reshape(-1, model_width)
        ]
    labels = region_ids.reshape(-1)
    member = (jnp.arange(regions, dtype=jnp.int32)[:, None] == labels[None, :]) & own_valid.reshape(
        -1
    )[None, :]
    member = member.astype(jnp.bfloat16)
    pieces_out = []
    partial = None
    row = 0
    for context in contexts:
        span = context.shape[0]
        result = project_whole(context, plane_out_pieces)
        piece = (after_cross[row : row + span].astype(jnp.float32) + result).astype(jnp.bfloat16)
        pieces_out.append(piece)
        extended = jnp.concatenate([piece, jnp.ones((span, 128), jnp.bfloat16)], axis=1)
        term = jnp.dot(member[:, row : row + span], extended, preferred_element_type=jnp.float32)
        partial = term if partial is None else partial + term
        row += span
    encoded = jnp.concatenate(pieces_out, axis=0)
    sections = lax.axis_size("sec")
    width = partial.shape[1]
    partial = partial.reshape(sections, plane_count, 2, width)
    me_plane = lax.axis_index("plane")
    gathered = lax.dynamic_index_in_dim(partial, me_plane, axis=1, keepdims=False)
    for step in range(1, plane_count):
        moved = [(i, (i + step) % plane_count) for i in range(plane_count)]
        target = lax.rem(me_plane + step, plane_count)
        block = lax.dynamic_index_in_dim(partial, target, axis=1, keepdims=False)
        gathered = gathered + lax.ppermute(block, "plane", moved)
    me_sec = lax.axis_index("sec")
    totals = lax.dynamic_index_in_dim(gathered, me_sec, axis=0, keepdims=False)
    for step in range(1, sections):
        moved = [(i, (i + step) % sections) for i in range(sections)]
        target = lax.rem(me_sec + step, sections)
        block = lax.dynamic_index_in_dim(gathered, target, axis=0, keepdims=False)
        totals = totals + lax.ppermute(block, "sec", moved)
    counted = totals[:, model_width]
    pooled = totals[:, :model_width] / jnp.maximum(counted, 1.0)[:, None]
    return (encoded.reshape(sec_block, tok_block, model_width), pooled)


def solution(mesh):
    in_specs = (
        P(("groups", "sec"), "plane", None),
        P("groups"),
        P(("groups", "sec"), "plane"),
        P(),
        P("plane", None),
        P("plane", None),
        P("plane", None),
        P("plane", None),
    )
    out_specs = (P(("groups", "sec"), "plane", None), P(("groups", "sec", "plane"), None))
    return jax.shard_map(body, mesh=mesh, in_specs=in_specs, out_specs=out_specs, check_vma=False)
```

```python
import math

import jax
import jax.numpy as jnp
from jax import lax
from jax.sharding import PartitionSpec as P

HEADS = 16
HEAD_DIM = 64
WINDOW = 128


negative_big = -1e30


def shifted_2(value, axis, by):
    peers = lax.axis_size(axis)
    pairs = [(i, i + by) for i in range(peers) if 0 <= i + by < peers]
    return lax.ppermute(value, axis, pairs)


def rms_norm(values, gain):
    wide = values.astype(jnp.float32)
    scaled = wide * lax.rsqrt(jnp.mean(wide * wide, axis=-1, keepdims=True) + 1e-06) * gain
    return scaled.astype(jnp.bfloat16)


def masked_softmax(scores, allowed):
    shifted = jnp.where(allowed, scores, negative_big)
    top = jnp.max(shifted, axis=-1, keepdims=True)
    expo = jnp.where(allowed, jnp.exp(shifted - top), 0.0)
    return (expo / jnp.sum(expo, axis=-1, keepdims=True)).astype(jnp.bfloat16)


def fold_product(inputs, weight_piece):
    return jnp.dot(inputs, weight_piece, preferred_element_type=jnp.float32)


def replica_levels():
    levels = []
    if lax.axis_size("groups") % 2 == 0:
        levels.append(("groups", lax.axis_size("groups"), 1))
    if lax.axis_size("sec") % 4 == 0:
        levels.append(("sec", lax.axis_size("sec"), 2))
    if lax.axis_size("sec") % 2 == 0:
        levels.append(("sec", lax.axis_size("sec"), 1))
    return levels


def rotate_rows(values, axis):
    plane_count = lax.axis_size("plane")
    block = values.shape[axis] // plane_count
    start = (lax.axis_index("plane") + 1) * block
    doubled = jnp.concatenate([values, values], axis=axis)
    return lax.dynamic_slice_in_dim(doubled, start, (plane_count - 1) * block, axis=axis)


def gather_pieces(shards, swap_first=False):
    levels = replica_levels()
    if swap_first and len(levels) == 3:
        levels = [levels[1], levels[0], levels[2]]
    count = 2 ** len(levels)
    widths = [shard.shape[1] // count for shard in shards]
    own = 0
    for bit, (axis, _, flip) in enumerate(levels):
        own = own + ((lax.axis_index(axis) // flip) % 2) * (2 ** bit)
    mine = jnp.concatenate(
        [
            lax.dynamic_slice_in_dim(shard, own * width, width, axis=1)
            for shard, width in zip(shards, widths)
        ],
        axis=1,
    )
    gathered = lax.all_gather(mine, "plane", axis=0, tiled=True)
    held = [(own, rotate_rows(gathered, 0))]
    for bit, (axis, size, flip) in enumerate(levels):
        swap = [(i, i ^ flip) for i in range(size)]
        held = held + [
            (piece + (1 - 2 * ((piece // 2 ** bit) % 2)) * 2 ** bit, lax.ppermute(block, axis, swap))
            for piece, block in held
        ]
    results = []
    offset = 0
    for shard, width in zip(shards, widths):
        results.append((shard, [(piece, block[:, offset : offset + width]) for piece, block in held], width))
        offset += width
    return results


def project(inputs, pieces):
    shard, held, width = pieces
    rows = shard.shape[0]
    local_inputs = lax.dynamic_slice_in_dim(inputs, lax.axis_index("plane") * rows, rows, axis=1)
    local = jnp.dot(local_inputs, shard, preferred_element_type=jnp.float32)
    remote_inputs = rotate_rows(inputs, 1)
    remote = jnp.zeros_like(local)
    for piece, block in held:
        part = jnp.dot(remote_inputs, block, preferred_element_type=jnp.float32)
        remote = lax.dynamic_update_slice_in_dim(remote, part, piece * width, axis=1)
    return local + remote


def assemble(pieces):
    shard, held, width = pieces
    remote = jnp.zeros((held[0][1].shape[0], width * len(held)), shard.dtype)
    for piece, block in held:
        remote = lax.dynamic_update_slice_in_dim(remote, block, piece * width, axis=1)
    return shard, remote


def project_whole(inputs, weights):
    shard, remote = weights
    rows = shard.shape[0]
    local_inputs = lax.dynamic_slice_in_dim(inputs, lax.axis_index("plane") * rows, rows, axis=1)
    local = jnp.dot(local_inputs, shard, preferred_element_type=jnp.float32)
    return local + jnp.dot(rotate_rows(inputs, 1), remote, preferred_element_type=jnp.float32)


def attend_items(pieces):
    packed_all, flags_all = pieces
    seq_len = packed_all.shape[2]
    block_len = 512
    score_scale = 1.0 / math.sqrt(HEAD_DIM)
    key_index = jnp.arange(seq_len, dtype=jnp.int32)

    def one_item(item_pair):
        packed, key_flag = item_pair
        key_rows = packed[:, HEAD_DIM : 2 * HEAD_DIM]
        value_rows = packed[:, 2 * HEAD_DIM :]
        key_alive = key_flag > 0.5
        query_blocks = packed[:, :HEAD_DIM].reshape(seq_len // block_len, block_len, HEAD_DIM)
        block_starts = jnp.arange(seq_len // block_len, dtype=jnp.int32) * block_len

        def one_block(block_pair):
            query_rows, offset = block_pair
            scores = (
                jnp.einsum("qd,kd->qk", query_rows, key_rows, preferred_element_type=jnp.float32)
                * score_scale
            )
            own_index = offset + jnp.arange(block_len, dtype=jnp.int32)
            allowed = key_alive[None, :] | (key_index[None, :] == own_index[:, None])
            attention = masked_softmax(scores, allowed)
            return jnp.dot(attention, value_rows, preferred_element_type=jnp.float32).astype(
                jnp.bfloat16
            )

        return lax.map(one_block, (query_blocks, block_starts)).reshape(seq_len, HEAD_DIM)

    return lax.map(one_item, (packed_all[0], flags_all[0]))[None]


def attend_by_section(projected, counts, plane_count):
    sec_block, tok_block = projected.shape[0], projected.shape[1]
    share = HEADS // plane_count
    seq_len = plane_count * tok_block
    score_scale = 1.0 / math.sqrt(HEAD_DIM)
    key_index = jnp.arange(seq_len, dtype=jnp.int32)
    contexts = []
    for local in range(sec_block):
        section = lax.axis_index("sec") * sec_block + local
        key_alive = key_index < lax.dynamic_index_in_dim(counts, section, keepdims=False)
        outgoing = jnp.transpose(
            projected[local].reshape(tok_block, 3, plane_count, share, HEAD_DIM), (2, 3, 0, 1, 4)
        ).reshape(plane_count, share, tok_block, 3 * HEAD_DIM)
        packed = lax.all_to_all(outgoing, "plane", split_axis=0, concat_axis=2, tiled=True)[0]
        queries = packed[:, :, :HEAD_DIM]
        keys = packed[:, :, HEAD_DIM : 2 * HEAD_DIM]
        values = packed[:, :, 2 * HEAD_DIM :]
        scores = (
            jnp.einsum("nqd,nkd->nqk", queries, keys, preferred_element_type=jnp.float32)
            * score_scale
        )
        allowed = key_alive[None, None, :] | (key_index[None, None, :] == key_index[None, :, None])
        attention = masked_softmax(scores, allowed)
        context = jnp.einsum(
            "nqk,nkd->nqd", attention, values, preferred_element_type=jnp.float32
        ).astype(jnp.bfloat16)
        homeward = jnp.transpose(
            context.reshape(share, plane_count, tok_block, HEAD_DIM), (1, 0, 2, 3)
        )
        returned = lax.all_to_all(homeward, "plane", split_axis=0, concat_axis=1, tiled=True)[0]
        contexts.append(jnp.transpose(returned, (1, 0, 2)).reshape(tok_block, HEADS * HEAD_DIM))
    return contexts


def body(tokens, counts, region_ids, norm_gains, cross_qkv, cross_out, plane_qkv, plane_out):
    sec_block, tok_block, model_width = tokens.shape
    plane_count = lax.axis_size("plane")
    regions = 2 * lax.axis_size("sec") * plane_count
    positions = lax.axis_index("plane") * tok_block + jnp.arange(tok_block, dtype=jnp.int32)
    padded_counts = jnp.concatenate(
        [jnp.zeros((1,), jnp.int32), counts, jnp.zeros((1,), jnp.int32)]
    )
    near_counts = lax.dynamic_slice_in_dim(
        padded_counts, lax.axis_index("sec") * sec_block, sec_block + 2
    )
    near_valid = positions[None, :] < near_counts[:, None]
    own_valid = near_valid[1 : sec_block + 1]
    score_scale = 1.0 / math.sqrt(HEAD_DIM)
    cross_qkv_pieces, cross_out_pieces = gather_pieces([cross_qkv, cross_out], swap_first=True)
    plane_qkv_pieces, plane_out_pieces = gather_pieces([plane_qkv, plane_out])
    cross_out_pieces = assemble(cross_out_pieces)
    plane_out_pieces = assemble(plane_out_pieces)
    normed = rms_norm(tokens, norm_gains[0])
    inputs = normed.reshape(-1, model_width)
    result = project(inputs, cross_qkv_pieces)
    projected = result.astype(jnp.bfloat16).reshape(sec_block, tok_block, 3 * model_width)
    own_kv = projected[:, :, model_width:]
    from_below = shifted_2(own_kv[sec_block - 1], "sec", 1)
    from_above = shifted_2(own_kv[0], "sec", -1)
    near_kv = jnp.concatenate([from_below[None], own_kv, from_above[None]], axis=0)
    queries = projected[:, :, :model_width]
    windows = tok_block // WINDOW
    query_win = queries.reshape(sec_block, windows, WINDOW, HEADS, HEAD_DIM)
    pair_win = near_kv.reshape(sec_block + 2, windows, WINDOW, 2, HEADS, HEAD_DIM)
    stacked = jnp.concatenate(
        [pair_win[0:sec_block], pair_win[1 : sec_block + 1], pair_win[2 : sec_block + 2]], axis=2
    )
    valid_win = near_valid.reshape(sec_block + 2, windows, WINDOW)
    valid_three = jnp.concatenate(
        [valid_win[0:sec_block], valid_win[1 : sec_block + 1], valid_win[2 : sec_block + 2]], axis=2
    )
    itself = jnp.arange(3 * WINDOW)[None, :] == jnp.arange(WINDOW)[:, None] + WINDOW
    scores = (
        jnp.einsum(
            "snqhd,snkhd->snhqk", query_win, stacked[:, :, :, 0], preferred_element_type=jnp.float32
        )
        * score_scale
    )
    allowed = valid_three[:, :, None, None, :] | itself[None, None, None]
    attention = masked_softmax(scores, allowed)
    context = jnp.einsum(
        "snhqk,snkhd->snqhd", attention, stacked[:, :, :, 1], preferred_element_type=jnp.float32
    )
    context = context.astype(jnp.bfloat16).reshape(-1, model_width)
    result = project_whole(context, cross_out_pieces)
    after_cross = (tokens.reshape(-1, model_width).astype(jnp.float32) + result).astype(
        jnp.bfloat16
    )
    normed = rms_norm(after_cross, norm_gains[1])
    result = project(normed, plane_qkv_pieces)
    projected = result.astype(jnp.bfloat16).reshape(sec_block, tok_block, 3, HEADS, HEAD_DIM)
    if HEADS % plane_count == 0:
        contexts = attend_by_section(projected, counts, plane_count)
    else:
        per_device = sec_block * HEADS // plane_count
        heads_first = jnp.transpose(projected, (0, 3, 1, 2, 4)).reshape(
            plane_count, per_device, tok_block, 3 * HEAD_DIM
        )
        key_flags = jnp.broadcast_to(own_valid[:, None, :], (sec_block, HEADS, tok_block)).astype(
            jnp.bfloat16
        )
        key_flags = key_flags.reshape(plane_count, per_device, tok_block)
        attended = attend_items(
            (
                lax.all_to_all(heads_first, "plane", split_axis=0, concat_axis=2, tiled=True),
                lax.all_to_all(key_flags, "plane", split_axis=0, concat_axis=2, tiled=True),
            )
        )
        returned = lax.all_to_all(attended, "plane", split_axis=2, concat_axis=0, tiled=True)
        contexts = [
            jnp.transpose(
                returned.reshape(sec_block, HEADS, tok_block, HEAD_DIM), (0, 2, 1, 3)
            ).reshape(-1, model_width)
        ]
    labels = region_ids.reshape(-1)
    member = (jnp.arange(regions, dtype=jnp.int32)[:, None] == labels[None, :]) & own_valid.reshape(
        -1
    )[None, :]
    member = member.astype(jnp.bfloat16)
    pieces_out = []
    partial = None
    row = 0
    for context in contexts:
        span = context.shape[0]
        result = project_whole(context, plane_out_pieces)
        piece = (after_cross[row : row + span].astype(jnp.float32) + result).astype(jnp.bfloat16)
        pieces_out.append(piece)
        extended = jnp.concatenate([piece, jnp.ones((span, 128), jnp.bfloat16)], axis=1)
        term = jnp.dot(member[:, row : row + span], extended, preferred_element_type=jnp.float32)
        partial = term if partial is None else partial + term
        row += span
    encoded = jnp.concatenate(pieces_out, axis=0)
    sections = lax.axis_size("sec")
    width = partial.shape[1]
    partial = partial.reshape(sections, plane_count, 2, width)
    me_plane = lax.axis_index("plane")
    gathered = lax.dynamic_index_in_dim(partial, me_plane, axis=1, keepdims=False)
    for step in range(1, plane_count):
        moved = [(i, (i + step) % plane_count) for i in range(plane_count)]
        target = lax.rem(me_plane + step, plane_count)
        block = lax.dynamic_index_in_dim(partial, target, axis=1, keepdims=False)
        gathered = gathered + lax.ppermute(block, "plane", moved)
    me_sec = lax.axis_index("sec")
    totals = lax.dynamic_index_in_dim(gathered, me_sec, axis=0, keepdims=False)
    for step in range(1, sections):
        moved = [(i, (i + step) % sections) for i in range(sections)]
        target = lax.rem(me_sec + step, sections)
        block = lax.dynamic_index_in_dim(gathered, target, axis=0, keepdims=False)
        totals = totals + lax.ppermute(block, "sec", moved)
    counted = totals[:, model_width]
    pooled = totals[:, :model_width] / jnp.maximum(counted, 1.0)[:, None]
    return (encoded.reshape(sec_block, tok_block, model_width), pooled)


def solution(mesh):
    in_specs = (
        P(("groups", "sec"), "plane", None),
        P("groups"),
        P(("groups", "sec"), "plane"),
        P(),
        P("plane", None),
        P("plane", None),
        P("plane", None),
        P("plane", None),
    )
    out_specs = (P(("groups", "sec"), "plane", None), P(("groups", "sec", "plane"), None))
    return jax.shard_map(body, mesh=mesh, in_specs=in_specs, out_specs=out_specs, check_vma=False)
```

```python
import math

import jax
import jax.numpy as jnp
from jax import lax
from jax.sharding import PartitionSpec as P

HEADS = 16
HEAD_DIM = 64
WINDOW = 128


negative_big = -1e30


def shifted_2(value, axis, by):
    peers = lax.axis_size(axis)
    pairs = [(i, i + by) for i in range(peers) if 0 <= i + by < peers]
    return lax.ppermute(value, axis, pairs)


def rms_norm(values, gain):
    wide = values.astype(jnp.float32)
    scaled = wide * lax.rsqrt(jnp.mean(wide * wide, axis=-1, keepdims=True) + 1e-06) * gain
    return scaled.astype(jnp.bfloat16)


def masked_softmax(scores, allowed):
    shifted = jnp.where(allowed, scores, negative_big)
    top = jnp.max(shifted, axis=-1, keepdims=True)
    expo = jnp.where(allowed, jnp.exp(shifted - top), 0.0)
    return (expo / jnp.sum(expo, axis=-1, keepdims=True)).astype(jnp.bfloat16)


def fold_product(inputs, weight_piece):
    return jnp.dot(inputs, weight_piece, preferred_element_type=jnp.float32)


def replica_levels():
    levels = []
    if lax.axis_size("groups") % 2 == 0:
        levels.append(("groups", lax.axis_size("groups"), 1))
    if lax.axis_size("sec") % 4 == 0:
        levels.append(("sec", lax.axis_size("sec"), 2))
    if lax.axis_size("sec") % 2 == 0:
        levels.append(("sec", lax.axis_size("sec"), 1))
    return levels


def rotate_rows(values, axis):
    plane_count = lax.axis_size("plane")
    block = values.shape[axis] // plane_count
    start = (lax.axis_index("plane") + 1) * block
    doubled = jnp.concatenate([values, values], axis=axis)
    return lax.dynamic_slice_in_dim(doubled, start, (plane_count - 1) * block, axis=axis)


def gather_pieces(shards, swap_first=False):
    levels = replica_levels()
    if swap_first and len(levels) == 3:
        levels = [levels[1], levels[0], levels[2]]
    count = 2 ** len(levels)
    widths = [shard.shape[1] // count for shard in shards]
    own = 0
    for bit, (axis, _, flip) in enumerate(levels):
        own = own + ((lax.axis_index(axis) // flip) % 2) * (2 ** bit)
    mine = jnp.concatenate(
        [
            lax.dynamic_slice_in_dim(shard, own * width, width, axis=1)
            for shard, width in zip(shards, widths)
        ],
        axis=1,
    )
    gathered = lax.all_gather(mine, "plane", axis=0, tiled=True)
    held = [([own], rotate_rows(gathered, 0)[None])]
    for bit, (axis, size, flip) in enumerate(levels):
        swap = [(i, i ^ flip) for i in range(size)]
        ids = [piece for group, _ in held for piece in group]
        stacked = held[0][1] if len(held) == 1 else jnp.concatenate([block for _, block in held], axis=0)
        moved = lax.ppermute(stacked, axis, swap)
        held = held + [([lax.bitwise_xor(piece, 2 ** bit) for piece in ids], moved)]
    results = []
    offset = 0
    for shard, width in zip(shards, widths):
        results.append(
            (shard, [(group, block[:, :, offset : offset + width]) for group, block in held], width)
        )
        offset += width
    return results


def project(inputs, pieces):
    shard, held, width = pieces
    rows = shard.shape[0]
    local_inputs = lax.dynamic_slice_in_dim(inputs, lax.axis_index("plane") * rows, rows, axis=1)
    local = jnp.dot(local_inputs, shard, preferred_element_type=jnp.float32)
    remote_inputs = rotate_rows(inputs, 1)
    remote = jnp.zeros_like(local)
    for group, block in held:
        parts = jnp.einsum("tk,nkc->ntc", remote_inputs, block, preferred_element_type=jnp.float32)
        for index, piece in enumerate(group):
            remote = lax.dynamic_update_slice_in_dim(remote, parts[index], piece * width, axis=1)
    return local + remote


def assemble(pieces):
    shard, held, width = pieces
    count = sum(len(group) for group, _ in held)
    remote = jnp.zeros((held[0][1].shape[1], width * count), shard.dtype)
    for group, block in held:
        for index, piece in enumerate(group):
            remote = lax.dynamic_update_slice_in_dim(remote, block[index], piece * width, axis=1)
    return shard, remote


def project_whole(inputs, weights):
    shard, remote = weights
    rows = shard.shape[0]
    local_inputs = lax.dynamic_slice_in_dim(inputs, lax.axis_index("plane") * rows, rows, axis=1)
    local = jnp.dot(local_inputs, shard, preferred_element_type=jnp.float32)
    return local + jnp.dot(rotate_rows(inputs, 1), remote, preferred_element_type=jnp.float32)


def attend_items(pieces):
    packed_all, flags_all = pieces
    seq_len = packed_all.shape[2]
    block_len = 512
    score_scale = 1.0 / math.sqrt(HEAD_DIM)
    key_index = jnp.arange(seq_len, dtype=jnp.int32)

    def one_item(item_pair):
        packed, key_flag = item_pair
        key_rows = packed[:, HEAD_DIM : 2 * HEAD_DIM]
        value_rows = packed[:, 2 * HEAD_DIM :]
        key_alive = key_flag > 0.5
        query_blocks = packed[:, :HEAD_DIM].reshape(seq_len // block_len, block_len, HEAD_DIM)
        block_starts = jnp.arange(seq_len // block_len, dtype=jnp.int32) * block_len

        def one_block(block_pair):
            query_rows, offset = block_pair
            scores = (
                jnp.einsum("qd,kd->qk", query_rows, key_rows, preferred_element_type=jnp.float32)
                * score_scale
            )
            own_index = offset + jnp.arange(block_len, dtype=jnp.int32)
            allowed = key_alive[None, :] | (key_index[None, :] == own_index[:, None])
            attention = masked_softmax(scores, allowed)
            return jnp.dot(attention, value_rows, preferred_element_type=jnp.float32).astype(
                jnp.bfloat16
            )

        return lax.map(one_block, (query_blocks, block_starts)).reshape(seq_len, HEAD_DIM)

    return lax.map(one_item, (packed_all[0], flags_all[0]))[None]


def attend_by_section(projected, counts, plane_count):
    sec_block, tok_block = projected.shape[0], projected.shape[1]
    share = HEADS // plane_count
    seq_len = plane_count * tok_block
    score_scale = 1.0 / math.sqrt(HEAD_DIM)
    key_index = jnp.arange(seq_len, dtype=jnp.int32)
    contexts = []
    for local in range(sec_block):
        section = lax.axis_index("sec") * sec_block + local
        key_alive = key_index < lax.dynamic_index_in_dim(counts, section, keepdims=False)
        outgoing = jnp.transpose(
            projected[local].reshape(tok_block, 3, plane_count, share, HEAD_DIM), (2, 3, 0, 1, 4)
        ).reshape(plane_count, share, tok_block, 3 * HEAD_DIM)
        packed = lax.all_to_all(outgoing, "plane", split_axis=0, concat_axis=2, tiled=True)[0]
        queries = packed[:, :, :HEAD_DIM]
        keys = packed[:, :, HEAD_DIM : 2 * HEAD_DIM]
        values = packed[:, :, 2 * HEAD_DIM :]
        scores = (
            jnp.einsum("nqd,nkd->nqk", queries, keys, preferred_element_type=jnp.float32)
            * score_scale
        )
        allowed = key_alive[None, None, :] | (key_index[None, None, :] == key_index[None, :, None])
        attention = masked_softmax(scores, allowed)
        context = jnp.einsum(
            "nqk,nkd->nqd", attention, values, preferred_element_type=jnp.float32
        ).astype(jnp.bfloat16)
        homeward = jnp.transpose(
            context.reshape(share, plane_count, tok_block, HEAD_DIM), (1, 0, 2, 3)
        )
        returned = lax.all_to_all(homeward, "plane", split_axis=0, concat_axis=1, tiled=True)[0]
        contexts.append(jnp.transpose(returned, (1, 0, 2)).reshape(tok_block, HEADS * HEAD_DIM))
    return contexts


def body(tokens, counts, region_ids, norm_gains, cross_qkv, cross_out, plane_qkv, plane_out):
    sec_block, tok_block, model_width = tokens.shape
    plane_count = lax.axis_size("plane")
    regions = 2 * lax.axis_size("sec") * plane_count
    positions = lax.axis_index("plane") * tok_block + jnp.arange(tok_block, dtype=jnp.int32)
    padded_counts = jnp.concatenate(
        [jnp.zeros((1,), jnp.int32), counts, jnp.zeros((1,), jnp.int32)]
    )
    near_counts = lax.dynamic_slice_in_dim(
        padded_counts, lax.axis_index("sec") * sec_block, sec_block + 2
    )
    near_valid = positions[None, :] < near_counts[:, None]
    own_valid = near_valid[1 : sec_block + 1]
    score_scale = 1.0 / math.sqrt(HEAD_DIM)
    cross_qkv_pieces, cross_out_pieces = gather_pieces([cross_qkv, cross_out], swap_first=True)
    plane_qkv_pieces, plane_out_pieces = gather_pieces([plane_qkv, plane_out])
    cross_out_pieces = assemble(cross_out_pieces)
    plane_out_pieces = assemble(plane_out_pieces)
    normed = rms_norm(tokens, norm_gains[0])
    inputs = normed.reshape(-1, model_width)
    result = project(inputs, cross_qkv_pieces)
    projected = result.astype(jnp.bfloat16).reshape(sec_block, tok_block, 3 * model_width)
    own_kv = projected[:, :, model_width:]
    from_below = shifted_2(own_kv[sec_block - 1], "sec", 1)
    from_above = shifted_2(own_kv[0], "sec", -1)
    near_kv = jnp.concatenate([from_below[None], own_kv, from_above[None]], axis=0)
    queries = projected[:, :, :model_width]
    windows = tok_block // WINDOW
    query_win = queries.reshape(sec_block, windows, WINDOW, HEADS, HEAD_DIM)
    pair_win = near_kv.reshape(sec_block + 2, windows, WINDOW, 2, HEADS, HEAD_DIM)
    stacked = jnp.concatenate(
        [pair_win[0:sec_block], pair_win[1 : sec_block + 1], pair_win[2 : sec_block + 2]], axis=2
    )
    valid_win = near_valid.reshape(sec_block + 2, windows, WINDOW)
    valid_three = jnp.concatenate(
        [valid_win[0:sec_block], valid_win[1 : sec_block + 1], valid_win[2 : sec_block + 2]], axis=2
    )
    itself = jnp.arange(3 * WINDOW)[None, :] == jnp.arange(WINDOW)[:, None] + WINDOW
    scores = (
        jnp.einsum(
            "snqhd,snkhd->snhqk", query_win, stacked[:, :, :, 0], preferred_element_type=jnp.float32
        )
        * score_scale
    )
    allowed = valid_three[:, :, None, None, :] | itself[None, None, None]
    attention = masked_softmax(scores, allowed)
    context = jnp.einsum(
        "snhqk,snkhd->snqhd", attention, stacked[:, :, :, 1], preferred_element_type=jnp.float32
    )
    context = context.astype(jnp.bfloat16).reshape(-1, model_width)
    result = project_whole(context, cross_out_pieces)
    after_cross = (tokens.reshape(-1, model_width).astype(jnp.float32) + result).astype(
        jnp.bfloat16
    )
    normed = rms_norm(after_cross, norm_gains[1])
    result = project(normed, plane_qkv_pieces)
    projected = result.astype(jnp.bfloat16).reshape(sec_block, tok_block, 3, HEADS, HEAD_DIM)
    if HEADS % plane_count == 0:
        contexts = attend_by_section(projected, counts, plane_count)
    else:
        per_device = sec_block * HEADS // plane_count
        heads_first = jnp.transpose(projected, (0, 3, 1, 2, 4)).reshape(
            plane_count, per_device, tok_block, 3 * HEAD_DIM
        )
        key_flags = jnp.broadcast_to(own_valid[:, None, :], (sec_block, HEADS, tok_block)).astype(
            jnp.bfloat16
        )
        key_flags = key_flags.reshape(plane_count, per_device, tok_block)
        attended = attend_items(
            (
                lax.all_to_all(heads_first, "plane", split_axis=0, concat_axis=2, tiled=True),
                lax.all_to_all(key_flags, "plane", split_axis=0, concat_axis=2, tiled=True),
            )
        )
        returned = lax.all_to_all(attended, "plane", split_axis=2, concat_axis=0, tiled=True)
        contexts = [
            jnp.transpose(
                returned.reshape(sec_block, HEADS, tok_block, HEAD_DIM), (0, 2, 1, 3)
            ).reshape(-1, model_width)
        ]
    labels = region_ids.reshape(-1)
    member = (jnp.arange(regions, dtype=jnp.int32)[:, None] == labels[None, :]) & own_valid.reshape(
        -1
    )[None, :]
    member = member.astype(jnp.bfloat16)
    pieces_out = []
    partial = None
    row = 0
    for context in contexts:
        span = context.shape[0]
        result = project_whole(context, plane_out_pieces)
        piece = (after_cross[row : row + span].astype(jnp.float32) + result).astype(jnp.bfloat16)
        pieces_out.append(piece)
        extended = jnp.concatenate([piece, jnp.ones((span, 128), jnp.bfloat16)], axis=1)
        term = jnp.dot(member[:, row : row + span], extended, preferred_element_type=jnp.float32)
        partial = term if partial is None else partial + term
        row += span
    encoded = jnp.concatenate(pieces_out, axis=0)
    sections = lax.axis_size("sec")
    width = partial.shape[1]
    partial = partial.reshape(sections, plane_count, 2, width)
    me_plane = lax.axis_index("plane")
    gathered = lax.dynamic_index_in_dim(partial, me_plane, axis=1, keepdims=False)
    for step in range(1, plane_count):
        moved = [(i, (i + step) % plane_count) for i in range(plane_count)]
        target = lax.rem(me_plane + step, plane_count)
        block = lax.dynamic_index_in_dim(partial, target, axis=1, keepdims=False)
        gathered = gathered + lax.ppermute(block, "plane", moved)
    me_sec = lax.axis_index("sec")
    totals = lax.dynamic_index_in_dim(gathered, me_sec, axis=0, keepdims=False)
    for step in range(1, sections):
        moved = [(i, (i + step) % sections) for i in range(sections)]
        target = lax.rem(me_sec + step, sections)
        block = lax.dynamic_index_in_dim(gathered, target, axis=0, keepdims=False)
        totals = totals + lax.ppermute(block, "sec", moved)
    counted = totals[:, model_width]
    pooled = totals[:, :model_width] / jnp.maximum(counted, 1.0)[:, None]
    return (encoded.reshape(sec_block, tok_block, model_width), pooled)


def solution(mesh):
    in_specs = (
        P(("groups", "sec"), "plane", None),
        P("groups"),
        P(("groups", "sec"), "plane"),
        P(),
        P("plane", None),
        P("plane", None),
        P("plane", None),
        P("plane", None),
    )
    out_specs = (P(("groups", "sec"), "plane", None), P(("groups", "sec", "plane"), None))
    return jax.shard_map(body, mesh=mesh, in_specs=in_specs, out_specs=out_specs, check_vma=False)
```

```python
import math

import jax
import jax.numpy as jnp
from jax import lax
from jax.sharding import PartitionSpec as P

HEADS = 16
HEAD_DIM = 64
WINDOW = 128


negative_big = -1e30


def shifted_2(value, axis, by):
    peers = lax.axis_size(axis)
    pairs = [(i, i + by) for i in range(peers) if 0 <= i + by < peers]
    return lax.ppermute(value, axis, pairs)


def rms_norm(values, gain):
    wide = values.astype(jnp.float32)
    scaled = wide * lax.rsqrt(jnp.mean(wide * wide, axis=-1, keepdims=True) + 1e-06) * gain
    return scaled.astype(jnp.bfloat16)


def masked_softmax(scores, allowed):
    shifted = jnp.where(allowed, scores, negative_big)
    top = jnp.max(shifted, axis=-1, keepdims=True)
    expo = jnp.where(allowed, jnp.exp(shifted - top), 0.0)
    return (expo / jnp.sum(expo, axis=-1, keepdims=True)).astype(jnp.bfloat16)


def fold_product(inputs, weight_piece):
    return jnp.dot(inputs, weight_piece, preferred_element_type=jnp.float32)


def replica_levels():
    levels = []
    if lax.axis_size("groups") % 2 == 0:
        levels.append(("groups", lax.axis_size("groups"), 1))
    if lax.axis_size("sec") % 4 == 0:
        levels.append(("sec", lax.axis_size("sec"), 2))
    if lax.axis_size("sec") % 2 == 0:
        levels.append(("sec", lax.axis_size("sec"), 1))
    return levels


def rotate_rows(values, axis):
    plane_count = lax.axis_size("plane")
    block = values.shape[axis] // plane_count
    start = (lax.axis_index("plane") + 1) * block
    doubled = jnp.concatenate([values, values], axis=axis)
    return lax.dynamic_slice_in_dim(doubled, start, (plane_count - 1) * block, axis=axis)


def gather_pieces(shards, swap_first=False):
    levels = replica_levels()
    if swap_first and len(levels) == 3:
        levels = [levels[1], levels[0], levels[2]]
    count = 2 ** len(levels)
    widths = [shard.shape[1] // count for shard in shards]
    own = 0
    for bit, (axis, _, flip) in enumerate(levels):
        own = own + ((lax.axis_index(axis) // flip) % 2) * (2 ** bit)
    mine = jnp.concatenate(
        [
            lax.dynamic_slice_in_dim(shard, own * width, width, axis=1)
            for shard, width in zip(shards, widths)
        ],
        axis=1,
    )
    gathered = lax.all_gather(mine, "plane", axis=0, tiled=True)
    held = [(own, rotate_rows(gathered, 0))]
    for bit, (axis, size, flip) in enumerate(levels):
        swap = [(i, i ^ flip) for i in range(size)]
        held = held + [
            (piece + (1 - 2 * ((piece // 2 ** bit) % 2)) * 2 ** bit, lax.ppermute(block, axis, swap))
            for piece, block in held
        ]
    results = []
    offset = 0
    for shard, width in zip(shards, widths):
        results.append((shard, [(piece, block[:, offset : offset + width]) for piece, block in held], width))
        offset += width
    return results


def project(inputs, pieces):
    shard, held, width = pieces
    rows = shard.shape[0]
    local_inputs = lax.dynamic_slice_in_dim(inputs, lax.axis_index("plane") * rows, rows, axis=1)
    local = jnp.dot(local_inputs, shard, preferred_element_type=jnp.float32)
    remote_inputs = rotate_rows(inputs, 1)
    remote = jnp.zeros_like(local)
    for piece, block in held:
        part = jnp.dot(remote_inputs, block, preferred_element_type=jnp.float32)
        remote = lax.dynamic_update_slice_in_dim(remote, part, piece * width, axis=1)
    return local + remote


def assemble(pieces):
    shard, held, width = pieces
    remote = jnp.zeros((held[0][1].shape[0], width * len(held)), shard.dtype)
    for piece, block in held:
        remote = lax.dynamic_update_slice_in_dim(remote, block, piece * width, axis=1)
    return shard, remote


def project_whole(inputs, weights):
    shard, remote = weights
    rows = shard.shape[0]
    local_inputs = lax.dynamic_slice_in_dim(inputs, lax.axis_index("plane") * rows, rows, axis=1)
    local = jnp.dot(local_inputs, shard, preferred_element_type=jnp.float32)
    return local + jnp.dot(rotate_rows(inputs, 1), remote, preferred_element_type=jnp.float32)


def attend_items(pieces):
    packed_all, flags_all = pieces
    seq_len = packed_all.shape[2]
    block_len = 512
    score_scale = 1.0 / math.sqrt(HEAD_DIM)
    key_index = jnp.arange(seq_len, dtype=jnp.int32)

    def one_item(item_pair):
        packed, key_flag = item_pair
        key_rows = packed[:, HEAD_DIM : 2 * HEAD_DIM]
        value_rows = packed[:, 2 * HEAD_DIM :]
        key_alive = key_flag > 0.5
        query_blocks = packed[:, :HEAD_DIM].reshape(seq_len // block_len, block_len, HEAD_DIM)
        block_starts = jnp.arange(seq_len // block_len, dtype=jnp.int32) * block_len

        def one_block(block_pair):
            query_rows, offset = block_pair
            scores = (
                jnp.einsum("qd,kd->qk", query_rows, key_rows, preferred_element_type=jnp.float32)
                * score_scale
            )
            own_index = offset + jnp.arange(block_len, dtype=jnp.int32)
            allowed = key_alive[None, :] | (key_index[None, :] == own_index[:, None])
            attention = masked_softmax(scores, allowed)
            return jnp.dot(attention, value_rows, preferred_element_type=jnp.float32).astype(
                jnp.bfloat16
            )

        return lax.map(one_block, (query_blocks, block_starts)).reshape(seq_len, HEAD_DIM)

    return lax.map(one_item, (packed_all[0], flags_all[0]))[None]


def attend_by_section(projected, counts, plane_count):
    sec_block, tok_block = projected.shape[0], projected.shape[1]
    share = HEADS // plane_count
    seq_len = plane_count * tok_block
    score_scale = 1.0 / math.sqrt(HEAD_DIM)
    key_index = jnp.arange(seq_len, dtype=jnp.int32)
    contexts = []
    for local in range(sec_block):
        section = lax.axis_index("sec") * sec_block + local
        key_alive = key_index < lax.dynamic_index_in_dim(counts, section, keepdims=False)
        outgoing = jnp.transpose(
            projected[local].reshape(tok_block, 3, plane_count, share, HEAD_DIM), (2, 3, 0, 1, 4)
        ).reshape(plane_count, share, tok_block, 3 * HEAD_DIM)
        packed = lax.all_to_all(outgoing, "plane", split_axis=0, concat_axis=2, tiled=True)[0]
        queries = packed[:, :, :HEAD_DIM]
        keys = packed[:, :, HEAD_DIM : 2 * HEAD_DIM]
        values = packed[:, :, 2 * HEAD_DIM :]
        scores = (
            jnp.einsum("nqd,nkd->nqk", queries, keys, preferred_element_type=jnp.float32)
            * score_scale
        )
        allowed = key_alive[None, None, :] | (key_index[None, None, :] == key_index[None, :, None])
        attention = masked_softmax(scores, allowed)
        context = jnp.einsum(
            "nqk,nkd->nqd", attention, values, preferred_element_type=jnp.float32
        ).astype(jnp.bfloat16)
        homeward = jnp.transpose(
            context.reshape(share, plane_count, tok_block, HEAD_DIM), (1, 0, 2, 3)
        )
        returned = lax.all_to_all(homeward, "plane", split_axis=0, concat_axis=1, tiled=True)[0]
        contexts.append(jnp.transpose(returned, (1, 0, 2)).reshape(tok_block, HEADS * HEAD_DIM))
    return contexts


def body(tokens, counts, region_ids, norm_gains, cross_qkv, cross_out, plane_qkv, plane_out):
    sec_block, tok_block, model_width = tokens.shape
    plane_count = lax.axis_size("plane")
    regions = 2 * lax.axis_size("sec") * plane_count
    positions = lax.axis_index("plane") * tok_block + jnp.arange(tok_block, dtype=jnp.int32)
    padded_counts = jnp.concatenate(
        [jnp.zeros((1,), jnp.int32), counts, jnp.zeros((1,), jnp.int32)]
    )
    near_counts = lax.dynamic_slice_in_dim(
        padded_counts, lax.axis_index("sec") * sec_block, sec_block + 2
    )
    near_valid = positions[None, :] < near_counts[:, None]
    own_valid = near_valid[1 : sec_block + 1]
    score_scale = 1.0 / math.sqrt(HEAD_DIM)
    cross_qkv_pieces, cross_out_pieces = gather_pieces([cross_qkv, cross_out], swap_first=True)
    plane_qkv_pieces, plane_out_pieces = gather_pieces([plane_qkv, plane_out], swap_first=True)
    cross_out_pieces = assemble(cross_out_pieces)
    plane_out_pieces = assemble(plane_out_pieces)
    normed = rms_norm(tokens, norm_gains[0])
    inputs = normed.reshape(-1, model_width)
    result = project(inputs, cross_qkv_pieces)
    projected = result.astype(jnp.bfloat16).reshape(sec_block, tok_block, 3 * model_width)
    own_kv = projected[:, :, model_width:]
    from_below = shifted_2(own_kv[sec_block - 1], "sec", 1)
    from_above = shifted_2(own_kv[0], "sec", -1)
    near_kv = jnp.concatenate([from_below[None], own_kv, from_above[None]], axis=0)
    queries = projected[:, :, :model_width]
    windows = tok_block // WINDOW
    query_win = queries.reshape(sec_block, windows, WINDOW, HEADS, HEAD_DIM)
    pair_win = near_kv.reshape(sec_block + 2, windows, WINDOW, 2, HEADS, HEAD_DIM)
    stacked = jnp.concatenate(
        [pair_win[0:sec_block], pair_win[1 : sec_block + 1], pair_win[2 : sec_block + 2]], axis=2
    )
    valid_win = near_valid.reshape(sec_block + 2, windows, WINDOW)
    valid_three = jnp.concatenate(
        [valid_win[0:sec_block], valid_win[1 : sec_block + 1], valid_win[2 : sec_block + 2]], axis=2
    )
    itself = jnp.arange(3 * WINDOW)[None, :] == jnp.arange(WINDOW)[:, None] + WINDOW
    scores = (
        jnp.einsum(
            "snqhd,snkhd->snhqk", query_win, stacked[:, :, :, 0], preferred_element_type=jnp.float32
        )
        * score_scale
    )
    allowed = valid_three[:, :, None, None, :] | itself[None, None, None]
    attention = masked_softmax(scores, allowed)
    context = jnp.einsum(
        "snhqk,snkhd->snqhd", attention, stacked[:, :, :, 1], preferred_element_type=jnp.float32
    )
    context = context.astype(jnp.bfloat16).reshape(-1, model_width)
    result = project_whole(context, cross_out_pieces)
    after_cross = (tokens.reshape(-1, model_width).astype(jnp.float32) + result).astype(
        jnp.bfloat16
    )
    normed = rms_norm(after_cross, norm_gains[1])
    result = project(normed, plane_qkv_pieces)
    projected = result.astype(jnp.bfloat16).reshape(sec_block, tok_block, 3, HEADS, HEAD_DIM)
    if HEADS % plane_count == 0:
        contexts = attend_by_section(projected, counts, plane_count)
    else:
        per_device = sec_block * HEADS // plane_count
        heads_first = jnp.transpose(projected, (0, 3, 1, 2, 4)).reshape(
            plane_count, per_device, tok_block, 3 * HEAD_DIM
        )
        key_flags = jnp.broadcast_to(own_valid[:, None, :], (sec_block, HEADS, tok_block)).astype(
            jnp.bfloat16
        )
        key_flags = key_flags.reshape(plane_count, per_device, tok_block)
        attended = attend_items(
            (
                lax.all_to_all(heads_first, "plane", split_axis=0, concat_axis=2, tiled=True),
                lax.all_to_all(key_flags, "plane", split_axis=0, concat_axis=2, tiled=True),
            )
        )
        returned = lax.all_to_all(attended, "plane", split_axis=2, concat_axis=0, tiled=True)
        contexts = [
            jnp.transpose(
                returned.reshape(sec_block, HEADS, tok_block, HEAD_DIM), (0, 2, 1, 3)
            ).reshape(-1, model_width)
        ]
    labels = region_ids.reshape(-1)
    member = (jnp.arange(regions, dtype=jnp.int32)[:, None] == labels[None, :]) & own_valid.reshape(
        -1
    )[None, :]
    member = member.astype(jnp.bfloat16)
    pieces_out = []
    partial = None
    row = 0
    for context in contexts:
        span = context.shape[0]
        result = project_whole(context, plane_out_pieces)
        piece = (after_cross[row : row + span].astype(jnp.float32) + result).astype(jnp.bfloat16)
        pieces_out.append(piece)
        extended = jnp.concatenate([piece, jnp.ones((span, 128), jnp.bfloat16)], axis=1)
        term = jnp.dot(member[:, row : row + span], extended, preferred_element_type=jnp.float32)
        partial = term if partial is None else partial + term
        row += span
    encoded = jnp.concatenate(pieces_out, axis=0)
    sections = lax.axis_size("sec")
    width = partial.shape[1]
    partial = partial.reshape(sections, plane_count, 2, width)
    me_plane = lax.axis_index("plane")
    gathered = lax.dynamic_index_in_dim(partial, me_plane, axis=1, keepdims=False)
    for step in range(1, plane_count):
        moved = [(i, (i + step) % plane_count) for i in range(plane_count)]
        target = lax.rem(me_plane + step, plane_count)
        block = lax.dynamic_index_in_dim(partial, target, axis=1, keepdims=False)
        gathered = gathered + lax.ppermute(block, "plane", moved)
    me_sec = lax.axis_index("sec")
    totals = lax.dynamic_index_in_dim(gathered, me_sec, axis=0, keepdims=False)
    for step in range(1, sections):
        moved = [(i, (i + step) % sections) for i in range(sections)]
        target = lax.rem(me_sec + step, sections)
        block = lax.dynamic_index_in_dim(gathered, target, axis=0, keepdims=False)
        totals = totals + lax.ppermute(block, "sec", moved)
    counted = totals[:, model_width]
    pooled = totals[:, :model_width] / jnp.maximum(counted, 1.0)[:, None]
    return (encoded.reshape(sec_block, tok_block, model_width), pooled)


def solution(mesh):
    in_specs = (
        P(("groups", "sec"), "plane", None),
        P("groups"),
        P(("groups", "sec"), "plane"),
        P(),
        P("plane", None),
        P("plane", None),
        P("plane", None),
        P("plane", None),
    )
    out_specs = (P(("groups", "sec"), "plane", None), P(("groups", "sec", "plane"), None))
    return jax.shard_map(body, mesh=mesh, in_specs=in_specs, out_specs=out_specs, check_vma=False)
```

```python
import math

import jax
import jax.numpy as jnp
from jax import lax
from jax.sharding import PartitionSpec as P

HEADS = 16
HEAD_DIM = 64
WINDOW = 128


negative_big = -1e30


def shifted_2(value, axis, by):
    peers = lax.axis_size(axis)
    pairs = [(i, i + by) for i in range(peers) if 0 <= i + by < peers]
    return lax.ppermute(value, axis, pairs)


def rms_norm(values, gain):
    wide = values.astype(jnp.float32)
    scaled = wide * lax.rsqrt(jnp.mean(wide * wide, axis=-1, keepdims=True) + 1e-06) * gain
    return scaled.astype(jnp.bfloat16)


def masked_softmax(scores, allowed):
    shifted = jnp.where(allowed, scores, negative_big)
    top = jnp.max(shifted, axis=-1, keepdims=True)
    expo = jnp.where(allowed, jnp.exp(shifted - top), 0.0)
    return (expo / jnp.sum(expo, axis=-1, keepdims=True)).astype(jnp.bfloat16)


def fold_product(inputs, weight_piece):
    return jnp.dot(inputs, weight_piece, preferred_element_type=jnp.float32)


def replica_levels():
    levels = []
    if lax.axis_size("groups") % 2 == 0:
        levels.append(("groups", lax.axis_size("groups"), 1))
    if lax.axis_size("sec") % 4 == 0:
        levels.append(("sec", lax.axis_size("sec"), 2))
    if lax.axis_size("sec") % 2 == 0:
        levels.append(("sec", lax.axis_size("sec"), 1))
    return levels


def rotate_rows(values, axis):
    plane_count = lax.axis_size("plane")
    block = values.shape[axis] // plane_count
    start = (lax.axis_index("plane") + 1) * block
    doubled = jnp.concatenate([values, values], axis=axis)
    return lax.dynamic_slice_in_dim(doubled, start, (plane_count - 1) * block, axis=axis)


def gather_pieces(shards, swap_first=False):
    levels = replica_levels()
    if swap_first and len(levels) == 3:
        levels = [levels[1], levels[0], levels[2]]
    count = 2 ** len(levels)
    widths = [shard.shape[1] // count for shard in shards]
    own = 0
    for bit, (axis, _, flip) in enumerate(levels):
        own = own + ((lax.axis_index(axis) // flip) % 2) * (2 ** bit)
    mine = jnp.concatenate(
        [
            lax.dynamic_slice_in_dim(shard, own * width, width, axis=1)
            for shard, width in zip(shards, widths)
        ],
        axis=1,
    )
    gathered = lax.all_gather(mine, "plane", axis=0, tiled=True)
    held = [(own, rotate_rows(gathered, 0))]
    for bit, (axis, size, flip) in enumerate(levels):
        swap = [(i, i ^ flip) for i in range(size)]
        held = held + [
            (piece + (1 - 2 * ((piece // 2 ** bit) % 2)) * 2 ** bit, lax.ppermute(block, axis, swap))
            for piece, block in held
        ]
    results = []
    offset = 0
    for shard, width in zip(shards, widths):
        results.append((shard, [(piece, block[:, offset : offset + width]) for piece, block in held], width))
        offset += width
    return results


def project(inputs, pieces):
    shard, held, width = pieces
    rows = shard.shape[0]
    local_inputs = lax.dynamic_slice_in_dim(inputs, lax.axis_index("plane") * rows, rows, axis=1)
    local = jnp.dot(local_inputs, shard, preferred_element_type=jnp.float32)
    remote_inputs = rotate_rows(inputs, 1)
    remote = jnp.zeros_like(local)
    for piece, block in held:
        part = jnp.dot(remote_inputs, block, preferred_element_type=jnp.float32)
        remote = lax.dynamic_update_slice_in_dim(remote, part, piece * width, axis=1)
    return local + remote


def assemble(pieces):
    shard, held, width = pieces
    remote = jnp.zeros((held[0][1].shape[0], width * len(held)), shard.dtype)
    for piece, block in held:
        remote = lax.dynamic_update_slice_in_dim(remote, block, piece * width, axis=1)
    return shard, remote


def project_whole(inputs, weights):
    shard, remote = weights
    rows = shard.shape[0]
    local_inputs = lax.dynamic_slice_in_dim(inputs, lax.axis_index("plane") * rows, rows, axis=1)
    local = jnp.dot(local_inputs, shard, preferred_element_type=jnp.float32)
    return local + jnp.dot(rotate_rows(inputs, 1), remote, preferred_element_type=jnp.float32)


def attend_items(pieces):
    packed_all, flags_all = pieces
    seq_len = packed_all.shape[2]
    block_len = 512
    score_scale = 1.0 / math.sqrt(HEAD_DIM)
    key_index = jnp.arange(seq_len, dtype=jnp.int32)

    def one_item(item_pair):
        packed, key_flag = item_pair
        key_rows = packed[:, HEAD_DIM : 2 * HEAD_DIM]
        value_rows = packed[:, 2 * HEAD_DIM :]
        key_alive = key_flag > 0.5
        query_blocks = packed[:, :HEAD_DIM].reshape(seq_len // block_len, block_len, HEAD_DIM)
        block_starts = jnp.arange(seq_len // block_len, dtype=jnp.int32) * block_len

        def one_block(block_pair):
            query_rows, offset = block_pair
            scores = (
                jnp.einsum("qd,kd->qk", query_rows, key_rows, preferred_element_type=jnp.float32)
                * score_scale
            )
            own_index = offset + jnp.arange(block_len, dtype=jnp.int32)
            allowed = key_alive[None, :] | (key_index[None, :] == own_index[:, None])
            attention = masked_softmax(scores, allowed)
            return jnp.dot(attention, value_rows, preferred_element_type=jnp.float32).astype(
                jnp.bfloat16
            )

        return lax.map(one_block, (query_blocks, block_starts)).reshape(seq_len, HEAD_DIM)

    return lax.map(one_item, (packed_all[0], flags_all[0]))[None]


def attend_by_section(projected, counts, plane_count):
    sec_block, tok_block = projected.shape[0], projected.shape[1]
    share = HEADS // plane_count
    seq_len = plane_count * tok_block
    score_scale = 1.0 / math.sqrt(HEAD_DIM)
    key_index = jnp.arange(seq_len, dtype=jnp.int32)
    contexts = []
    for local in range(sec_block):
        section = lax.axis_index("sec") * sec_block + local
        key_alive = key_index < lax.dynamic_index_in_dim(counts, section, keepdims=False)
        outgoing = jnp.transpose(
            projected[local].reshape(tok_block, 3, plane_count, share, HEAD_DIM), (2, 3, 0, 1, 4)
        ).reshape(plane_count, share, tok_block, 3 * HEAD_DIM)
        packed = lax.all_to_all(outgoing, "plane", split_axis=0, concat_axis=2, tiled=True)[0]
        queries = packed[:, :, :HEAD_DIM]
        keys = packed[:, :, HEAD_DIM : 2 * HEAD_DIM]
        values = packed[:, :, 2 * HEAD_DIM :]
        scores = (
            jnp.einsum("nqd,nkd->nqk", queries, keys, preferred_element_type=jnp.float32)
            * score_scale
        )
        allowed = key_alive[None, None, :] | (key_index[None, None, :] == key_index[None, :, None])
        attention = masked_softmax(scores, allowed)
        context = jnp.einsum(
            "nqk,nkd->nqd", attention, values, preferred_element_type=jnp.float32
        ).astype(jnp.bfloat16)
        homeward = jnp.transpose(
            context.reshape(share, plane_count, tok_block, HEAD_DIM), (1, 0, 2, 3)
        )
        returned = lax.all_to_all(homeward, "plane", split_axis=0, concat_axis=1, tiled=True)[0]
        contexts.append(jnp.transpose(returned, (1, 0, 2)).reshape(tok_block, HEADS * HEAD_DIM))
    return contexts


def body(tokens, counts, region_ids, norm_gains, cross_qkv, cross_out, plane_qkv, plane_out):
    sec_block, tok_block, model_width = tokens.shape
    plane_count = lax.axis_size("plane")
    regions = 2 * lax.axis_size("sec") * plane_count
    positions = lax.axis_index("plane") * tok_block + jnp.arange(tok_block, dtype=jnp.int32)
    padded_counts = jnp.concatenate(
        [jnp.zeros((1,), jnp.int32), counts, jnp.zeros((1,), jnp.int32)]
    )
    near_counts = lax.dynamic_slice_in_dim(
        padded_counts, lax.axis_index("sec") * sec_block, sec_block + 2
    )
    near_valid = positions[None, :] < near_counts[:, None]
    own_valid = near_valid[1 : sec_block + 1]
    score_scale = 1.0 / math.sqrt(HEAD_DIM)
    cross_qkv_pieces, cross_out_pieces, plane_out_pieces = gather_pieces(
        [cross_qkv, cross_out, plane_out], swap_first=True
    )
    (plane_qkv_pieces,) = gather_pieces([plane_qkv], swap_first=True)
    cross_out_pieces = assemble(cross_out_pieces)
    plane_out_pieces = assemble(plane_out_pieces)
    normed = rms_norm(tokens, norm_gains[0])
    inputs = normed.reshape(-1, model_width)
    result = project(inputs, cross_qkv_pieces)
    projected = result.astype(jnp.bfloat16).reshape(sec_block, tok_block, 3 * model_width)
    own_kv = projected[:, :, model_width:]
    from_below = shifted_2(own_kv[sec_block - 1], "sec", 1)
    from_above = shifted_2(own_kv[0], "sec", -1)
    near_kv = jnp.concatenate([from_below[None], own_kv, from_above[None]], axis=0)
    queries = projected[:, :, :model_width]
    windows = tok_block // WINDOW
    query_win = queries.reshape(sec_block, windows, WINDOW, HEADS, HEAD_DIM)
    pair_win = near_kv.reshape(sec_block + 2, windows, WINDOW, 2, HEADS, HEAD_DIM)
    stacked = jnp.concatenate(
        [pair_win[0:sec_block], pair_win[1 : sec_block + 1], pair_win[2 : sec_block + 2]], axis=2
    )
    valid_win = near_valid.reshape(sec_block + 2, windows, WINDOW)
    valid_three = jnp.concatenate(
        [valid_win[0:sec_block], valid_win[1 : sec_block + 1], valid_win[2 : sec_block + 2]], axis=2
    )
    itself = jnp.arange(3 * WINDOW)[None, :] == jnp.arange(WINDOW)[:, None] + WINDOW
    scores = (
        jnp.einsum(
            "snqhd,snkhd->snhqk", query_win, stacked[:, :, :, 0], preferred_element_type=jnp.float32
        )
        * score_scale
    )
    allowed = valid_three[:, :, None, None, :] | itself[None, None, None]
    attention = masked_softmax(scores, allowed)
    context = jnp.einsum(
        "snhqk,snkhd->snqhd", attention, stacked[:, :, :, 1], preferred_element_type=jnp.float32
    )
    context = context.astype(jnp.bfloat16).reshape(-1, model_width)
    result = project_whole(context, cross_out_pieces)
    after_cross = (tokens.reshape(-1, model_width).astype(jnp.float32) + result).astype(
        jnp.bfloat16
    )
    normed = rms_norm(after_cross, norm_gains[1])
    result = project(normed, plane_qkv_pieces)
    projected = result.astype(jnp.bfloat16).reshape(sec_block, tok_block, 3, HEADS, HEAD_DIM)
    if HEADS % plane_count == 0:
        contexts = attend_by_section(projected, counts, plane_count)
    else:
        per_device = sec_block * HEADS // plane_count
        heads_first = jnp.transpose(projected, (0, 3, 1, 2, 4)).reshape(
            plane_count, per_device, tok_block, 3 * HEAD_DIM
        )
        key_flags = jnp.broadcast_to(own_valid[:, None, :], (sec_block, HEADS, tok_block)).astype(
            jnp.bfloat16
        )
        key_flags = key_flags.reshape(plane_count, per_device, tok_block)
        attended = attend_items(
            (
                lax.all_to_all(heads_first, "plane", split_axis=0, concat_axis=2, tiled=True),
                lax.all_to_all(key_flags, "plane", split_axis=0, concat_axis=2, tiled=True),
            )
        )
        returned = lax.all_to_all(attended, "plane", split_axis=2, concat_axis=0, tiled=True)
        contexts = [
            jnp.transpose(
                returned.reshape(sec_block, HEADS, tok_block, HEAD_DIM), (0, 2, 1, 3)
            ).reshape(-1, model_width)
        ]
    labels = region_ids.reshape(-1)
    member = (jnp.arange(regions, dtype=jnp.int32)[:, None] == labels[None, :]) & own_valid.reshape(
        -1
    )[None, :]
    member = member.astype(jnp.bfloat16)
    pieces_out = []
    partial = None
    row = 0
    for context in contexts:
        span = context.shape[0]
        result = project_whole(context, plane_out_pieces)
        piece = (after_cross[row : row + span].astype(jnp.float32) + result).astype(jnp.bfloat16)
        pieces_out.append(piece)
        extended = jnp.concatenate([piece, jnp.ones((span, 128), jnp.bfloat16)], axis=1)
        term = jnp.dot(member[:, row : row + span], extended, preferred_element_type=jnp.float32)
        partial = term if partial is None else partial + term
        row += span
    encoded = jnp.concatenate(pieces_out, axis=0)
    sections = lax.axis_size("sec")
    width = partial.shape[1]
    partial = partial.reshape(sections, plane_count, 2, width)
    me_plane = lax.axis_index("plane")
    gathered = lax.dynamic_index_in_dim(partial, me_plane, axis=1, keepdims=False)
    for step in range(1, plane_count):
        moved = [(i, (i + step) % plane_count) for i in range(plane_count)]
        target = lax.rem(me_plane + step, plane_count)
        block = lax.dynamic_index_in_dim(partial, target, axis=1, keepdims=False)
        gathered = gathered + lax.ppermute(block, "plane", moved)
    me_sec = lax.axis_index("sec")
    totals = lax.dynamic_index_in_dim(gathered, me_sec, axis=0, keepdims=False)
    for step in range(1, sections):
        moved = [(i, (i + step) % sections) for i in range(sections)]
        target = lax.rem(me_sec + step, sections)
        block = lax.dynamic_index_in_dim(gathered, target, axis=0, keepdims=False)
        totals = totals + lax.ppermute(block, "sec", moved)
    counted = totals[:, model_width]
    pooled = totals[:, :model_width] / jnp.maximum(counted, 1.0)[:, None]
    return (encoded.reshape(sec_block, tok_block, model_width), pooled)


def solution(mesh):
    in_specs = (
        P(("groups", "sec"), "plane", None),
        P("groups"),
        P(("groups", "sec"), "plane"),
        P(),
        P("plane", None),
        P("plane", None),
        P("plane", None),
        P("plane", None),
    )
    out_specs = (P(("groups", "sec"), "plane", None), P(("groups", "sec", "plane"), None))
    return jax.shard_map(body, mesh=mesh, in_specs=in_specs, out_specs=out_specs, check_vma=False)
```

```python
import math

import jax
import jax.numpy as jnp
from jax import lax
from jax.sharding import PartitionSpec as P

HEADS = 16
HEAD_DIM = 64
WINDOW = 128


negative_big = -1e30


def shifted_2(value, axis, by):
    peers = lax.axis_size(axis)
    pairs = [(i, i + by) for i in range(peers) if 0 <= i + by < peers]
    return lax.ppermute(value, axis, pairs)


def rms_norm(values, gain):
    wide = values.astype(jnp.float32)
    scaled = wide * lax.rsqrt(jnp.mean(wide * wide, axis=-1, keepdims=True) + 1e-06) * gain
    return scaled.astype(jnp.bfloat16)


def masked_softmax(scores, allowed):
    shifted = jnp.where(allowed, scores, negative_big)
    top = jnp.max(shifted, axis=-1, keepdims=True)
    expo = jnp.where(allowed, jnp.exp(shifted - top), 0.0)
    return (expo / jnp.sum(expo, axis=-1, keepdims=True)).astype(jnp.bfloat16)


def fold_product(inputs, weight_piece):
    return jnp.dot(inputs, weight_piece, preferred_element_type=jnp.float32)


def replica_levels():
    levels = []
    if lax.axis_size("groups") % 2 == 0:
        levels.append(("groups", lax.axis_size("groups"), 1))
    if lax.axis_size("sec") % 4 == 0:
        levels.append(("sec", lax.axis_size("sec"), 2))
    if lax.axis_size("sec") % 2 == 0:
        levels.append(("sec", lax.axis_size("sec"), 1))
    return levels


def rotate_rows(values, axis):
    plane_count = lax.axis_size("plane")
    block = values.shape[axis] // plane_count
    start = (lax.axis_index("plane") + 1) * block
    doubled = jnp.concatenate([values, values], axis=axis)
    return lax.dynamic_slice_in_dim(doubled, start, (plane_count - 1) * block, axis=axis)


def gather_pieces(shards, swap_first=False, skip_middle=False):
    levels = replica_levels()
    if skip_middle and len(levels) == 3:
        levels = [levels[0], levels[2]]
    elif swap_first and len(levels) == 3:
        levels = [levels[1], levels[0], levels[2]]
    count = 2 ** len(levels)
    widths = [shard.shape[1] // count for shard in shards]
    own = 0
    for bit, (axis, _, flip) in enumerate(levels):
        own = own + ((lax.axis_index(axis) // flip) % 2) * (2 ** bit)
    mine = jnp.concatenate(
        [
            lax.dynamic_slice_in_dim(shard, own * width, width, axis=1)
            for shard, width in zip(shards, widths)
        ],
        axis=1,
    )
    gathered = lax.all_gather(mine, "plane", axis=0, tiled=True)
    held = [(own, rotate_rows(gathered, 0))]
    for bit, (axis, size, flip) in enumerate(levels):
        swap = [(i, i ^ flip) for i in range(size)]
        held = held + [
            (piece + (1 - 2 * ((piece // 2 ** bit) % 2)) * 2 ** bit, lax.ppermute(block, axis, swap))
            for piece, block in held
        ]
    results = []
    offset = 0
    for shard, width in zip(shards, widths):
        results.append((shard, [(piece, block[:, offset : offset + width]) for piece, block in held], width))
        offset += width
    return results


def project(inputs, pieces):
    shard, held, width = pieces
    rows = shard.shape[0]
    local_inputs = lax.dynamic_slice_in_dim(inputs, lax.axis_index("plane") * rows, rows, axis=1)
    local = jnp.dot(local_inputs, shard, preferred_element_type=jnp.float32)
    remote_inputs = rotate_rows(inputs, 1)
    remote = jnp.zeros_like(local)
    for piece, block in held:
        part = jnp.dot(remote_inputs, block, preferred_element_type=jnp.float32)
        remote = lax.dynamic_update_slice_in_dim(remote, part, piece * width, axis=1)
    return local + remote


def assemble(pieces):
    shard, held, width = pieces
    remote = jnp.zeros((held[0][1].shape[0], width * len(held)), shard.dtype)
    for piece, block in held:
        remote = lax.dynamic_update_slice_in_dim(remote, block, piece * width, axis=1)
    return shard, remote


def project_whole(inputs, weights):
    shard, remote = weights
    rows = shard.shape[0]
    local_inputs = lax.dynamic_slice_in_dim(inputs, lax.axis_index("plane") * rows, rows, axis=1)
    local = jnp.dot(local_inputs, shard, preferred_element_type=jnp.float32)
    return local + jnp.dot(rotate_rows(inputs, 1), remote, preferred_element_type=jnp.float32)


def attend_items(pieces):
    packed_all, flags_all = pieces
    seq_len = packed_all.shape[2]
    block_len = 512
    score_scale = 1.0 / math.sqrt(HEAD_DIM)
    key_index = jnp.arange(seq_len, dtype=jnp.int32)

    def one_item(item_pair):
        packed, key_flag = item_pair
        key_rows = packed[:, HEAD_DIM : 2 * HEAD_DIM]
        value_rows = packed[:, 2 * HEAD_DIM :]
        key_alive = key_flag > 0.5
        query_blocks = packed[:, :HEAD_DIM].reshape(seq_len // block_len, block_len, HEAD_DIM)
        block_starts = jnp.arange(seq_len // block_len, dtype=jnp.int32) * block_len

        def one_block(block_pair):
            query_rows, offset = block_pair
            scores = (
                jnp.einsum("qd,kd->qk", query_rows, key_rows, preferred_element_type=jnp.float32)
                * score_scale
            )
            own_index = offset + jnp.arange(block_len, dtype=jnp.int32)
            allowed = key_alive[None, :] | (key_index[None, :] == own_index[:, None])
            attention = masked_softmax(scores, allowed)
            return jnp.dot(attention, value_rows, preferred_element_type=jnp.float32).astype(
                jnp.bfloat16
            )

        return lax.map(one_block, (query_blocks, block_starts)).reshape(seq_len, HEAD_DIM)

    return lax.map(one_item, (packed_all[0], flags_all[0]))[None]


def attend_by_section(projected, counts, plane_count):
    sec_block, tok_block = projected.shape[0], projected.shape[1]
    share = HEADS // plane_count
    seq_len = plane_count * tok_block
    score_scale = 1.0 / math.sqrt(HEAD_DIM)
    key_index = jnp.arange(seq_len, dtype=jnp.int32)
    contexts = []
    for local in range(sec_block):
        section = lax.axis_index("sec") * sec_block + local
        key_alive = key_index < lax.dynamic_index_in_dim(counts, section, keepdims=False)
        outgoing = jnp.transpose(
            projected[local].reshape(tok_block, 3, plane_count, share, HEAD_DIM), (2, 3, 0, 1, 4)
        ).reshape(plane_count, share, tok_block, 3 * HEAD_DIM)
        packed = lax.all_to_all(outgoing, "plane", split_axis=0, concat_axis=2, tiled=True)[0]
        queries = packed[:, :, :HEAD_DIM]
        keys = packed[:, :, HEAD_DIM : 2 * HEAD_DIM]
        values = packed[:, :, 2 * HEAD_DIM :]
        scores = (
            jnp.einsum("nqd,nkd->nqk", queries, keys, preferred_element_type=jnp.float32)
            * score_scale
        )
        allowed = key_alive[None, None, :] | (key_index[None, None, :] == key_index[None, :, None])
        attention = masked_softmax(scores, allowed)
        context = jnp.einsum(
            "nqk,nkd->nqd", attention, values, preferred_element_type=jnp.float32
        ).astype(jnp.bfloat16)
        homeward = jnp.transpose(
            context.reshape(share, plane_count, tok_block, HEAD_DIM), (1, 0, 2, 3)
        )
        returned = lax.all_to_all(homeward, "plane", split_axis=0, concat_axis=1, tiled=True)[0]
        contexts.append(jnp.transpose(returned, (1, 0, 2)).reshape(tok_block, HEADS * HEAD_DIM))
    return contexts


def body(tokens, counts, region_ids, norm_gains, cross_qkv, cross_out, plane_qkv, plane_out):
    sec_block, tok_block, model_width = tokens.shape
    plane_count = lax.axis_size("plane")
    regions = 2 * lax.axis_size("sec") * plane_count
    positions = lax.axis_index("plane") * tok_block + jnp.arange(tok_block, dtype=jnp.int32)
    padded_counts = jnp.concatenate(
        [jnp.zeros((1,), jnp.int32), counts, jnp.zeros((1,), jnp.int32)]
    )
    near_counts = lax.dynamic_slice_in_dim(
        padded_counts, lax.axis_index("sec") * sec_block, sec_block + 2
    )
    near_valid = positions[None, :] < near_counts[:, None]
    own_valid = near_valid[1 : sec_block + 1]
    score_scale = 1.0 / math.sqrt(HEAD_DIM)
    cross_qkv_pieces, cross_out_pieces = gather_pieces([cross_qkv, cross_out], swap_first=True)
    plane_qkv_pieces, plane_out_pieces = gather_pieces([plane_qkv, plane_out], skip_middle=True)
    cross_out_pieces = assemble(cross_out_pieces)
    plane_out_pieces = assemble(plane_out_pieces)
    normed = rms_norm(tokens, norm_gains[0])
    inputs = normed.reshape(-1, model_width)
    result = project(inputs, cross_qkv_pieces)
    projected = result.astype(jnp.bfloat16).reshape(sec_block, tok_block, 3 * model_width)
    own_kv = projected[:, :, model_width:]
    from_below = shifted_2(own_kv[sec_block - 1], "sec", 1)
    from_above = shifted_2(own_kv[0], "sec", -1)
    near_kv = jnp.concatenate([from_below[None], own_kv, from_above[None]], axis=0)
    queries = projected[:, :, :model_width]
    windows = tok_block // WINDOW
    query_win = queries.reshape(sec_block, windows, WINDOW, HEADS, HEAD_DIM)
    pair_win = near_kv.reshape(sec_block + 2, windows, WINDOW, 2, HEADS, HEAD_DIM)
    stacked = jnp.concatenate(
        [pair_win[0:sec_block], pair_win[1 : sec_block + 1], pair_win[2 : sec_block + 2]], axis=2
    )
    valid_win = near_valid.reshape(sec_block + 2, windows, WINDOW)
    valid_three = jnp.concatenate(
        [valid_win[0:sec_block], valid_win[1 : sec_block + 1], valid_win[2 : sec_block + 2]], axis=2
    )
    itself = jnp.arange(3 * WINDOW)[None, :] == jnp.arange(WINDOW)[:, None] + WINDOW
    scores = (
        jnp.einsum(
            "snqhd,snkhd->snhqk", query_win, stacked[:, :, :, 0], preferred_element_type=jnp.float32
        )
        * score_scale
    )
    allowed = valid_three[:, :, None, None, :] | itself[None, None, None]
    attention = masked_softmax(scores, allowed)
    context = jnp.einsum(
        "snhqk,snkhd->snqhd", attention, stacked[:, :, :, 1], preferred_element_type=jnp.float32
    )
    context = context.astype(jnp.bfloat16).reshape(-1, model_width)
    result = project_whole(context, cross_out_pieces)
    after_cross = (tokens.reshape(-1, model_width).astype(jnp.float32) + result).astype(
        jnp.bfloat16
    )
    normed = rms_norm(after_cross, norm_gains[1])
    result = project(normed, plane_qkv_pieces)
    projected = result.astype(jnp.bfloat16).reshape(sec_block, tok_block, 3, HEADS, HEAD_DIM)
    if HEADS % plane_count == 0:
        contexts = attend_by_section(projected, counts, plane_count)
    else:
        per_device = sec_block * HEADS // plane_count
        heads_first = jnp.transpose(projected, (0, 3, 1, 2, 4)).reshape(
            plane_count, per_device, tok_block, 3 * HEAD_DIM
        )
        key_flags = jnp.broadcast_to(own_valid[:, None, :], (sec_block, HEADS, tok_block)).astype(
            jnp.bfloat16
        )
        key_flags = key_flags.reshape(plane_count, per_device, tok_block)
        attended = attend_items(
            (
                lax.all_to_all(heads_first, "plane", split_axis=0, concat_axis=2, tiled=True),
                lax.all_to_all(key_flags, "plane", split_axis=0, concat_axis=2, tiled=True),
            )
        )
        returned = lax.all_to_all(attended, "plane", split_axis=2, concat_axis=0, tiled=True)
        contexts = [
            jnp.transpose(
                returned.reshape(sec_block, HEADS, tok_block, HEAD_DIM), (0, 2, 1, 3)
            ).reshape(-1, model_width)
        ]
    labels = region_ids.reshape(-1)
    member = (jnp.arange(regions, dtype=jnp.int32)[:, None] == labels[None, :]) & own_valid.reshape(
        -1
    )[None, :]
    member = member.astype(jnp.bfloat16)
    pieces_out = []
    partial = None
    row = 0
    for context in contexts:
        span = context.shape[0]
        result = project_whole(context, plane_out_pieces)
        piece = (after_cross[row : row + span].astype(jnp.float32) + result).astype(jnp.bfloat16)
        pieces_out.append(piece)
        extended = jnp.concatenate([piece, jnp.ones((span, 128), jnp.bfloat16)], axis=1)
        term = jnp.dot(member[:, row : row + span], extended, preferred_element_type=jnp.float32)
        partial = term if partial is None else partial + term
        row += span
    encoded = jnp.concatenate(pieces_out, axis=0)
    sections = lax.axis_size("sec")
    width = partial.shape[1]
    partial = partial.reshape(sections, plane_count, 2, width)
    me_plane = lax.axis_index("plane")
    gathered = lax.dynamic_index_in_dim(partial, me_plane, axis=1, keepdims=False)
    for step in range(1, plane_count):
        moved = [(i, (i + step) % plane_count) for i in range(plane_count)]
        target = lax.rem(me_plane + step, plane_count)
        block = lax.dynamic_index_in_dim(partial, target, axis=1, keepdims=False)
        gathered = gathered + lax.ppermute(block, "plane", moved)
    me_sec = lax.axis_index("sec")
    totals = lax.dynamic_index_in_dim(gathered, me_sec, axis=0, keepdims=False)
    for step in range(1, sections):
        moved = [(i, (i + step) % sections) for i in range(sections)]
        target = lax.rem(me_sec + step, sections)
        block = lax.dynamic_index_in_dim(gathered, target, axis=0, keepdims=False)
        totals = totals + lax.ppermute(block, "sec", moved)
    counted = totals[:, model_width]
    pooled = totals[:, :model_width] / jnp.maximum(counted, 1.0)[:, None]
    return (encoded.reshape(sec_block, tok_block, model_width), pooled)


def solution(mesh):
    in_specs = (
        P(("groups", "sec"), "plane", None),
        P("groups"),
        P(("groups", "sec"), "plane"),
        P(),
        P("plane", None),
        P("plane", None),
        P("plane", None),
        P("plane", None),
    )
    out_specs = (P(("groups", "sec"), "plane", None), P(("groups", "sec", "plane"), None))
    return jax.shard_map(body, mesh=mesh, in_specs=in_specs, out_specs=out_specs, check_vma=False)
```

```python
import math

import jax
import jax.numpy as jnp
from jax import lax
from jax.sharding import PartitionSpec as P

HEADS = 16
HEAD_DIM = 64
WINDOW = 128


negative_big = -1e30


def shifted_2(value, axis, by):
    peers = lax.axis_size(axis)
    pairs = [(i, i + by) for i in range(peers) if 0 <= i + by < peers]
    return lax.ppermute(value, axis, pairs)


def rms_norm(values, gain):
    wide = values.astype(jnp.float32)
    scaled = wide * lax.rsqrt(jnp.mean(wide * wide, axis=-1, keepdims=True) + 1e-06) * gain
    return scaled.astype(jnp.bfloat16)


def masked_softmax(scores, allowed):
    shifted = jnp.where(allowed, scores, negative_big)
    top = jnp.max(shifted, axis=-1, keepdims=True)
    expo = jnp.where(allowed, jnp.exp(shifted - top), 0.0)
    return (expo / jnp.sum(expo, axis=-1, keepdims=True)).astype(jnp.bfloat16)


def fold_product(inputs, weight_piece):
    return jnp.dot(inputs, weight_piece, preferred_element_type=jnp.float32)


def replica_levels():
    levels = []
    if lax.axis_size("groups") % 2 == 0:
        levels.append(("groups", lax.axis_size("groups"), 1))
    if lax.axis_size("sec") % 4 == 0:
        levels.append(("sec", lax.axis_size("sec"), 2))
    if lax.axis_size("sec") % 2 == 0:
        levels.append(("sec", lax.axis_size("sec"), 1))
    return levels


def rotate_rows(values, axis):
    plane_count = lax.axis_size("plane")
    block = values.shape[axis] // plane_count
    start = (lax.axis_index("plane") + 1) * block
    doubled = jnp.concatenate([values, values], axis=axis)
    return lax.dynamic_slice_in_dim(doubled, start, (plane_count - 1) * block, axis=axis)


def gather_pieces(shards, swap_first=False, skip_middle=False):
    levels = replica_levels()
    if skip_middle and len(levels) == 3:
        levels = [levels[0], levels[2]]
    elif swap_first and len(levels) == 3:
        levels = [levels[1], levels[0], levels[2]]
    count = 2 ** len(levels)
    widths = [shard.shape[1] // count for shard in shards]
    own = 0
    for bit, (axis, _, flip) in enumerate(levels):
        own = own + ((lax.axis_index(axis) // flip) % 2) * (2 ** bit)
    mine = jnp.concatenate(
        [
            lax.dynamic_slice_in_dim(shard, own * width, width, axis=1)
            for shard, width in zip(shards, widths)
        ],
        axis=1,
    )
    gathered = lax.all_gather(mine, "plane", axis=0, tiled=True)
    held = [(own, rotate_rows(gathered, 0))]
    for bit, (axis, size, flip) in enumerate(levels):
        swap = [(i, i ^ flip) for i in range(size)]
        held = held + [
            (piece + (1 - 2 * ((piece // 2 ** bit) % 2)) * 2 ** bit, lax.ppermute(block, axis, swap))
            for piece, block in held
        ]
    results = []
    offset = 0
    for shard, width in zip(shards, widths):
        results.append((shard, [(piece, block[:, offset : offset + width]) for piece, block in held], width))
        offset += width
    return results


def project(inputs, pieces):
    shard, held, width = pieces
    rows = shard.shape[0]
    local_inputs = lax.dynamic_slice_in_dim(inputs, lax.axis_index("plane") * rows, rows, axis=1)
    local = jnp.dot(local_inputs, shard, preferred_element_type=jnp.float32)
    remote_inputs = rotate_rows(inputs, 1)
    remote = jnp.zeros_like(local)
    for piece, block in held:
        part = jnp.dot(remote_inputs, block, preferred_element_type=jnp.float32)
        remote = lax.dynamic_update_slice_in_dim(remote, part, piece * width, axis=1)
    return local + remote


def assemble(pieces):
    shard, held, width = pieces
    remote = jnp.zeros((held[0][1].shape[0], width * len(held)), shard.dtype)
    for piece, block in held:
        remote = lax.dynamic_update_slice_in_dim(remote, block, piece * width, axis=1)
    return shard, remote


def project_whole(inputs, weights):
    shard, remote = weights
    rows = shard.shape[0]
    local_inputs = lax.dynamic_slice_in_dim(inputs, lax.axis_index("plane") * rows, rows, axis=1)
    local = jnp.dot(local_inputs, shard, preferred_element_type=jnp.float32)
    return local + jnp.dot(rotate_rows(inputs, 1), remote, preferred_element_type=jnp.float32)


def attend_items(pieces):
    packed_all, flags_all = pieces
    seq_len = packed_all.shape[2]
    block_len = 512
    score_scale = 1.0 / math.sqrt(HEAD_DIM)
    key_index = jnp.arange(seq_len, dtype=jnp.int32)

    def one_item(item_pair):
        packed, key_flag = item_pair
        key_rows = packed[:, HEAD_DIM : 2 * HEAD_DIM]
        value_rows = packed[:, 2 * HEAD_DIM :]
        key_alive = key_flag > 0.5
        query_blocks = packed[:, :HEAD_DIM].reshape(seq_len // block_len, block_len, HEAD_DIM)
        block_starts = jnp.arange(seq_len // block_len, dtype=jnp.int32) * block_len

        def one_block(block_pair):
            query_rows, offset = block_pair
            scores = (
                jnp.einsum("qd,kd->qk", query_rows, key_rows, preferred_element_type=jnp.float32)
                * score_scale
            )
            own_index = offset + jnp.arange(block_len, dtype=jnp.int32)
            allowed = key_alive[None, :] | (key_index[None, :] == own_index[:, None])
            attention = masked_softmax(scores, allowed)
            return jnp.dot(attention, value_rows, preferred_element_type=jnp.float32).astype(
                jnp.bfloat16
            )

        return lax.map(one_block, (query_blocks, block_starts)).reshape(seq_len, HEAD_DIM)

    return lax.map(one_item, (packed_all[0], flags_all[0]))[None]


def attend_by_section(projected, counts, plane_count):
    sec_block, tok_block = len(projected), projected[0].shape[0]
    share = HEADS // plane_count
    seq_len = plane_count * tok_block
    score_scale = 1.0 / math.sqrt(HEAD_DIM)
    key_index = jnp.arange(seq_len, dtype=jnp.int32)
    contexts = []
    for local in range(sec_block):
        section = lax.axis_index("sec") * sec_block + local
        key_alive = key_index < lax.dynamic_index_in_dim(counts, section, keepdims=False)
        outgoing = jnp.transpose(
            projected[local].reshape(tok_block, 3, plane_count, share, HEAD_DIM), (2, 3, 0, 1, 4)
        ).reshape(plane_count, share, tok_block, 3 * HEAD_DIM)
        packed = lax.all_to_all(outgoing, "plane", split_axis=0, concat_axis=2, tiled=True)[0]
        queries = packed[:, :, :HEAD_DIM]
        keys = packed[:, :, HEAD_DIM : 2 * HEAD_DIM]
        values = packed[:, :, 2 * HEAD_DIM :]
        scores = (
            jnp.einsum("nqd,nkd->nqk", queries, keys, preferred_element_type=jnp.float32)
            * score_scale
        )
        allowed = key_alive[None, None, :] | (key_index[None, None, :] == key_index[None, :, None])
        attention = masked_softmax(scores, allowed)
        context = jnp.einsum(
            "nqk,nkd->nqd", attention, values, preferred_element_type=jnp.float32
        ).astype(jnp.bfloat16)
        homeward = jnp.transpose(
            context.reshape(share, plane_count, tok_block, HEAD_DIM), (1, 0, 2, 3)
        )
        returned = lax.all_to_all(homeward, "plane", split_axis=0, concat_axis=1, tiled=True)[0]
        contexts.append(jnp.transpose(returned, (1, 0, 2)).reshape(tok_block, HEADS * HEAD_DIM))
    return contexts


def body(tokens, counts, region_ids, norm_gains, cross_qkv, cross_out, plane_qkv, plane_out):
    sec_block, tok_block, model_width = tokens.shape
    plane_count = lax.axis_size("plane")
    regions = 2 * lax.axis_size("sec") * plane_count
    positions = lax.axis_index("plane") * tok_block + jnp.arange(tok_block, dtype=jnp.int32)
    padded_counts = jnp.concatenate(
        [jnp.zeros((1,), jnp.int32), counts, jnp.zeros((1,), jnp.int32)]
    )
    near_counts = lax.dynamic_slice_in_dim(
        padded_counts, lax.axis_index("sec") * sec_block, sec_block + 2
    )
    near_valid = positions[None, :] < near_counts[:, None]
    own_valid = near_valid[1 : sec_block + 1]
    score_scale = 1.0 / math.sqrt(HEAD_DIM)
    cross_qkv_pieces, cross_out_pieces = gather_pieces([cross_qkv, cross_out], swap_first=True)
    plane_qkv_pieces, plane_out_pieces = gather_pieces([plane_qkv, plane_out], skip_middle=True)
    cross_out_pieces = assemble(cross_out_pieces)
    plane_out_pieces = assemble(plane_out_pieces)
    normed = rms_norm(tokens, norm_gains[0])
    inputs = normed.reshape(-1, model_width)
    result = project(inputs, cross_qkv_pieces)
    projected = result.astype(jnp.bfloat16).reshape(sec_block, tok_block, 3 * model_width)
    own_kv = projected[:, :, model_width:]
    from_below = shifted_2(own_kv[sec_block - 1], "sec", 1)
    from_above = shifted_2(own_kv[0], "sec", -1)
    near_kv = jnp.concatenate([from_below[None], own_kv, from_above[None]], axis=0)
    queries = projected[:, :, :model_width]
    windows = tok_block // WINDOW
    query_win = queries.reshape(sec_block, windows, WINDOW, HEADS, HEAD_DIM)
    pair_win = near_kv.reshape(sec_block + 2, windows, WINDOW, 2, HEADS, HEAD_DIM)
    stacked = jnp.concatenate(
        [pair_win[0:sec_block], pair_win[1 : sec_block + 1], pair_win[2 : sec_block + 2]], axis=2
    )
    valid_win = near_valid.reshape(sec_block + 2, windows, WINDOW)
    valid_three = jnp.concatenate(
        [valid_win[0:sec_block], valid_win[1 : sec_block + 1], valid_win[2 : sec_block + 2]], axis=2
    )
    itself = jnp.arange(3 * WINDOW)[None, :] == jnp.arange(WINDOW)[:, None] + WINDOW
    scores = (
        jnp.einsum(
            "snqhd,snkhd->snhqk", query_win, stacked[:, :, :, 0], preferred_element_type=jnp.float32
        )
        * score_scale
    )
    allowed = valid_three[:, :, None, None, :] | itself[None, None, None]
    attention = masked_softmax(scores, allowed)
    context = jnp.einsum(
        "snhqk,snkhd->snqhd", attention, stacked[:, :, :, 1], preferred_element_type=jnp.float32
    )
    context = context.astype(jnp.bfloat16).reshape(-1, model_width)
    result = project_whole(context, cross_out_pieces)
    after_cross = (tokens.reshape(-1, model_width).astype(jnp.float32) + result).astype(
        jnp.bfloat16
    )
    normed = rms_norm(after_cross, norm_gains[1])
    if HEADS % plane_count == 0:
        projected = [
            project(normed[local * tok_block : (local + 1) * tok_block], plane_qkv_pieces)
            .astype(jnp.bfloat16)
            .reshape(tok_block, 3, HEADS, HEAD_DIM)
            for local in range(sec_block)
        ]
        contexts = attend_by_section(projected, counts, plane_count)
    else:
        result = project(normed, plane_qkv_pieces)
        projected = result.astype(jnp.bfloat16).reshape(sec_block, tok_block, 3, HEADS, HEAD_DIM)
        per_device = sec_block * HEADS // plane_count
        heads_first = jnp.transpose(projected, (0, 3, 1, 2, 4)).reshape(
            plane_count, per_device, tok_block, 3 * HEAD_DIM
        )
        key_flags = jnp.broadcast_to(own_valid[:, None, :], (sec_block, HEADS, tok_block)).astype(
            jnp.bfloat16
        )
        key_flags = key_flags.reshape(plane_count, per_device, tok_block)
        attended = attend_items(
            (
                lax.all_to_all(heads_first, "plane", split_axis=0, concat_axis=2, tiled=True),
                lax.all_to_all(key_flags, "plane", split_axis=0, concat_axis=2, tiled=True),
            )
        )
        returned = lax.all_to_all(attended, "plane", split_axis=2, concat_axis=0, tiled=True)
        contexts = [
            jnp.transpose(
                returned.reshape(sec_block, HEADS, tok_block, HEAD_DIM), (0, 2, 1, 3)
            ).reshape(-1, model_width)
        ]
    labels = region_ids.reshape(-1)
    member = (jnp.arange(regions, dtype=jnp.int32)[:, None] == labels[None, :]) & own_valid.reshape(
        -1
    )[None, :]
    member = member.astype(jnp.bfloat16)
    pieces_out = []
    partial = None
    row = 0
    for context in contexts:
        span = context.shape[0]
        result = project_whole(context, plane_out_pieces)
        piece = (after_cross[row : row + span].astype(jnp.float32) + result).astype(jnp.bfloat16)
        pieces_out.append(piece)
        extended = jnp.concatenate([piece, jnp.ones((span, 128), jnp.bfloat16)], axis=1)
        term = jnp.dot(member[:, row : row + span], extended, preferred_element_type=jnp.float32)
        partial = term if partial is None else partial + term
        row += span
    encoded = jnp.concatenate(pieces_out, axis=0)
    sections = lax.axis_size("sec")
    width = partial.shape[1]
    partial = partial.reshape(sections, plane_count, 2, width)
    me_plane = lax.axis_index("plane")
    gathered = lax.dynamic_index_in_dim(partial, me_plane, axis=1, keepdims=False)
    for step in range(1, plane_count):
        moved = [(i, (i + step) % plane_count) for i in range(plane_count)]
        target = lax.rem(me_plane + step, plane_count)
        block = lax.dynamic_index_in_dim(partial, target, axis=1, keepdims=False)
        gathered = gathered + lax.ppermute(block, "plane", moved)
    me_sec = lax.axis_index("sec")
    totals = lax.dynamic_index_in_dim(gathered, me_sec, axis=0, keepdims=False)
    for step in range(1, sections):
        moved = [(i, (i + step) % sections) for i in range(sections)]
        target = lax.rem(me_sec + step, sections)
        block = lax.dynamic_index_in_dim(gathered, target, axis=0, keepdims=False)
        totals = totals + lax.ppermute(block, "sec", moved)
    counted = totals[:, model_width]
    pooled = totals[:, :model_width] / jnp.maximum(counted, 1.0)[:, None]
    return (encoded.reshape(sec_block, tok_block, model_width), pooled)


def solution(mesh):
    in_specs = (
        P(("groups", "sec"), "plane", None),
        P("groups"),
        P(("groups", "sec"), "plane"),
        P(),
        P("plane", None),
        P("plane", None),
        P("plane", None),
        P("plane", None),
    )
    out_specs = (P(("groups", "sec"), "plane", None), P(("groups", "sec", "plane"), None))
    return jax.shard_map(body, mesh=mesh, in_specs=in_specs, out_specs=out_specs, check_vma=False)
```

```python
import math

import jax
import jax.numpy as jnp
from jax import lax
from jax.sharding import PartitionSpec as P

HEADS = 16
HEAD_DIM = 64
WINDOW = 128


negative_big = -1e30


def shifted_2(value, axis, by):
    peers = lax.axis_size(axis)
    pairs = [(i, i + by) for i in range(peers) if 0 <= i + by < peers]
    return lax.ppermute(value, axis, pairs)


def rms_norm(values, gain):
    wide = values.astype(jnp.float32)
    scaled = wide * lax.rsqrt(jnp.mean(wide * wide, axis=-1, keepdims=True) + 1e-06) * gain
    return scaled.astype(jnp.bfloat16)


def masked_softmax(scores, allowed):
    shifted = jnp.where(allowed, scores, negative_big)
    top = jnp.max(shifted, axis=-1, keepdims=True)
    expo = jnp.where(allowed, jnp.exp(shifted - top), 0.0)
    return (expo / jnp.sum(expo, axis=-1, keepdims=True)).astype(jnp.bfloat16)


def fold_product(inputs, weight_piece):
    return jnp.dot(inputs, weight_piece, preferred_element_type=jnp.float32)


def replica_levels():
    levels = []
    if lax.axis_size("groups") % 2 == 0:
        levels.append(("groups", lax.axis_size("groups"), 1))
    if lax.axis_size("sec") % 4 == 0:
        levels.append(("sec", lax.axis_size("sec"), 2))
    if lax.axis_size("sec") % 2 == 0:
        levels.append(("sec", lax.axis_size("sec"), 1))
    return levels


def rotate_rows(values, axis):
    plane_count = lax.axis_size("plane")
    block = values.shape[axis] // plane_count
    start = (lax.axis_index("plane") + 1) * block
    doubled = jnp.concatenate([values, values], axis=axis)
    return lax.dynamic_slice_in_dim(doubled, start, (plane_count - 1) * block, axis=axis)


def gather_pieces(shards, swap_first=False, skip_middle=False):
    levels = replica_levels()
    if skip_middle and len(levels) == 3:
        levels = [levels[0], levels[2]]
    elif swap_first and len(levels) == 3:
        levels = [levels[1], levels[0], levels[2]]
    count = 2 ** len(levels)
    widths = [shard.shape[1] // count for shard in shards]
    own = 0
    for bit, (axis, _, flip) in enumerate(levels):
        own = own + ((lax.axis_index(axis) // flip) % 2) * (2 ** bit)
    mine = jnp.concatenate(
        [
            lax.dynamic_slice_in_dim(shard, own * width, width, axis=1)
            for shard, width in zip(shards, widths)
        ],
        axis=1,
    )
    gathered = lax.all_gather(mine, "plane", axis=0, tiled=True)
    held = [(own, rotate_rows(gathered, 0))]
    for bit, (axis, size, flip) in enumerate(levels):
        swap = [(i, i ^ flip) for i in range(size)]
        held = held + [
            (piece + (1 - 2 * ((piece // 2 ** bit) % 2)) * 2 ** bit, lax.ppermute(block, axis, swap))
            for piece, block in held
        ]
    results = []
    offset = 0
    for shard, width in zip(shards, widths):
        results.append((shard, [(piece, block[:, offset : offset + width]) for piece, block in held], width))
        offset += width
    return results


def project(inputs, pieces):
    shard, held, width = pieces
    rows = shard.shape[0]
    local_inputs = lax.dynamic_slice_in_dim(inputs, lax.axis_index("plane") * rows, rows, axis=1)
    local = jnp.dot(local_inputs, shard, preferred_element_type=jnp.float32)
    remote_inputs = rotate_rows(inputs, 1)
    remote = jnp.zeros_like(local)
    for piece, block in held:
        part = jnp.dot(remote_inputs, block, preferred_element_type=jnp.float32)
        remote = lax.dynamic_update_slice_in_dim(remote, part, piece * width, axis=1)
    return local + remote


def assemble(pieces):
    shard, held, width = pieces
    remote = jnp.zeros((held[0][1].shape[0], width * len(held)), shard.dtype)
    for piece, block in held:
        remote = lax.dynamic_update_slice_in_dim(remote, block, piece * width, axis=1)
    return shard, remote


def project_whole(inputs, weights):
    shard, remote = weights
    rows = shard.shape[0]
    local_inputs = lax.dynamic_slice_in_dim(inputs, lax.axis_index("plane") * rows, rows, axis=1)
    local = jnp.dot(local_inputs, shard, preferred_element_type=jnp.float32)
    return local + jnp.dot(rotate_rows(inputs, 1), remote, preferred_element_type=jnp.float32)


def attend_items(pieces):
    packed_all, flags_all = pieces
    seq_len = packed_all.shape[2]
    block_len = 512
    score_scale = 1.0 / math.sqrt(HEAD_DIM)
    key_index = jnp.arange(seq_len, dtype=jnp.int32)

    def one_item(item_pair):
        packed, key_flag = item_pair
        key_rows = packed[:, HEAD_DIM : 2 * HEAD_DIM]
        value_rows = packed[:, 2 * HEAD_DIM :]
        key_alive = key_flag > 0.5
        query_blocks = packed[:, :HEAD_DIM].reshape(seq_len // block_len, block_len, HEAD_DIM)
        block_starts = jnp.arange(seq_len // block_len, dtype=jnp.int32) * block_len

        def one_block(block_pair):
            query_rows, offset = block_pair
            scores = (
                jnp.einsum("qd,kd->qk", query_rows, key_rows, preferred_element_type=jnp.float32)
                * score_scale
            )
            own_index = offset + jnp.arange(block_len, dtype=jnp.int32)
            allowed = key_alive[None, :] | (key_index[None, :] == own_index[:, None])
            attention = masked_softmax(scores, allowed)
            return jnp.dot(attention, value_rows, preferred_element_type=jnp.float32).astype(
                jnp.bfloat16
            )

        return lax.map(one_block, (query_blocks, block_starts)).reshape(seq_len, HEAD_DIM)

    return lax.map(one_item, (packed_all[0], flags_all[0]))[None]


def attend_by_section(projected, counts, plane_count):
    sec_block, tok_block = projected.shape[0], projected.shape[1]
    share = HEADS // plane_count
    seq_len = plane_count * tok_block
    score_scale = 1.0 / math.sqrt(HEAD_DIM)
    key_index = jnp.arange(seq_len, dtype=jnp.int32)
    contexts = []
    for local in range(sec_block):
        section = lax.axis_index("sec") * sec_block + local
        key_alive = key_index < lax.dynamic_index_in_dim(counts, section, keepdims=False)
        outgoing = jnp.transpose(
            projected[local].reshape(tok_block, 3, plane_count, share, HEAD_DIM), (2, 3, 0, 1, 4)
        ).reshape(plane_count, share, tok_block, 3 * HEAD_DIM)
        packed = lax.all_to_all(outgoing, "plane", split_axis=0, concat_axis=2, tiled=True)[0]
        queries = packed[:, :, :HEAD_DIM]
        keys = packed[:, :, HEAD_DIM : 2 * HEAD_DIM]
        values = packed[:, :, 2 * HEAD_DIM :]
        scores = (
            jnp.einsum("nqd,nkd->nqk", queries, keys, preferred_element_type=jnp.float32)
            * score_scale
        )
        allowed = key_alive[None, None, :] | (key_index[None, None, :] == key_index[None, :, None])
        attention = masked_softmax(scores, allowed)
        context = jnp.einsum(
            "nqk,nkd->nqd", attention, values, preferred_element_type=jnp.float32
        ).astype(jnp.bfloat16)
        homeward = jnp.transpose(
            context.reshape(share, plane_count, tok_block, HEAD_DIM), (1, 0, 2, 3)
        )
        returned = lax.all_to_all(homeward, "plane", split_axis=0, concat_axis=1, tiled=True)[0]
        contexts.append(jnp.transpose(returned, (1, 0, 2)).reshape(tok_block, HEADS * HEAD_DIM))
    return contexts


def body(tokens, counts, region_ids, norm_gains, cross_qkv, cross_out, plane_qkv, plane_out):
    sec_block, tok_block, model_width = tokens.shape
    plane_count = lax.axis_size("plane")
    regions = 2 * lax.axis_size("sec") * plane_count
    positions = lax.axis_index("plane") * tok_block + jnp.arange(tok_block, dtype=jnp.int32)
    padded_counts = jnp.concatenate(
        [jnp.zeros((1,), jnp.int32), counts, jnp.zeros((1,), jnp.int32)]
    )
    near_counts = lax.dynamic_slice_in_dim(
        padded_counts, lax.axis_index("sec") * sec_block, sec_block + 2
    )
    near_valid = positions[None, :] < near_counts[:, None]
    own_valid = near_valid[1 : sec_block + 1]
    score_scale = 1.0 / math.sqrt(HEAD_DIM)
    cross_qkv_pieces, cross_out_pieces = gather_pieces([cross_qkv, cross_out], swap_first=True)
    plane_qkv_pieces, plane_out_pieces = gather_pieces([plane_qkv, plane_out], skip_middle=True)
    cross_out_pieces = assemble(cross_out_pieces)
    plane_out_pieces = assemble(plane_out_pieces)
    normed = rms_norm(tokens, norm_gains[0])
    inputs = normed.reshape(-1, model_width)
    result = project(inputs, cross_qkv_pieces)
    projected = result.astype(jnp.bfloat16).reshape(sec_block, tok_block, 3 * model_width)
    own_kv = projected[:, :, model_width:]
    from_below = shifted_2(own_kv[sec_block - 1], "sec", 1)
    from_above = shifted_2(own_kv[0], "sec", -1)
    near_kv = jnp.concatenate([from_below[None], own_kv, from_above[None]], axis=0)
    queries = projected[:, :, :model_width]
    windows = tok_block // WINDOW
    query_win = queries.reshape(sec_block, windows, WINDOW, HEADS, HEAD_DIM)
    pair_win = near_kv.reshape(sec_block + 2, windows, WINDOW, 2, HEADS, HEAD_DIM)
    stacked = jnp.concatenate(
        [pair_win[0:sec_block], pair_win[1 : sec_block + 1], pair_win[2 : sec_block + 2]], axis=2
    )
    valid_win = near_valid.reshape(sec_block + 2, windows, WINDOW)
    valid_three = jnp.concatenate(
        [valid_win[0:sec_block], valid_win[1 : sec_block + 1], valid_win[2 : sec_block + 2]], axis=2
    )
    itself = jnp.arange(3 * WINDOW)[None, :] == jnp.arange(WINDOW)[:, None] + WINDOW
    scores = (
        jnp.einsum(
            "snqhd,snkhd->snhqk", query_win, stacked[:, :, :, 0], preferred_element_type=jnp.float32
        )
        * score_scale
    )
    allowed = valid_three[:, :, None, None, :] | itself[None, None, None]
    attention = masked_softmax(scores, allowed)
    context = jnp.einsum(
        "snhqk,snkhd->snqhd", attention, stacked[:, :, :, 1], preferred_element_type=jnp.float32
    )
    context = context.astype(jnp.bfloat16).reshape(-1, model_width)
    result = project_whole(context, cross_out_pieces)
    after_cross = (tokens.reshape(-1, model_width).astype(jnp.float32) + result).astype(
        jnp.bfloat16
    )
    normed = rms_norm(after_cross, norm_gains[1])
    result = project(normed, plane_qkv_pieces)
    projected = result.astype(jnp.bfloat16).reshape(sec_block, tok_block, 3, HEADS, HEAD_DIM)
    if HEADS % plane_count == 0:
        contexts = attend_by_section(projected, counts, plane_count)
    else:
        per_device = sec_block * HEADS // plane_count
        heads_first = jnp.transpose(projected, (0, 3, 1, 2, 4)).reshape(
            plane_count, per_device, tok_block, 3 * HEAD_DIM
        )
        key_flags = jnp.broadcast_to(own_valid[:, None, :], (sec_block, HEADS, tok_block)).astype(
            jnp.bfloat16
        )
        key_flags = key_flags.reshape(plane_count, per_device, tok_block)
        attended = attend_items(
            (
                lax.all_to_all(heads_first, "plane", split_axis=0, concat_axis=2, tiled=True),
                lax.all_to_all(key_flags, "plane", split_axis=0, concat_axis=2, tiled=True),
            )
        )
        returned = lax.all_to_all(attended, "plane", split_axis=2, concat_axis=0, tiled=True)
        contexts = [
            jnp.transpose(
                returned.reshape(sec_block, HEADS, tok_block, HEAD_DIM), (0, 2, 1, 3)
            ).reshape(-1, model_width)
        ]
    labels = region_ids.reshape(-1)
    member = (jnp.arange(regions, dtype=jnp.int32)[:, None] == labels[None, :]) & own_valid.reshape(
        -1
    )[None, :]
    member = member.astype(jnp.bfloat16)
    pieces_out = []
    partial = None
    row = 0
    for context in contexts:
        span = context.shape[0]
        result = project_whole(context, plane_out_pieces)
        piece = (after_cross[row : row + span].astype(jnp.float32) + result).astype(jnp.bfloat16)
        pieces_out.append(piece)
        extended = jnp.concatenate([piece, jnp.ones((span, 128), jnp.bfloat16)], axis=1)
        term = jnp.dot(member[:, row : row + span], extended, preferred_element_type=jnp.float32)
        partial = term if partial is None else partial + term
        row += span
    encoded = jnp.concatenate(pieces_out, axis=0)
    owners = lax.axis_size("sec") * plane_count
    arrived = lax.all_to_all(partial, ("sec", "plane"), split_axis=0, concat_axis=0, tiled=True)
    totals = jnp.sum(arrived.reshape(owners, 2, partial.shape[1]), axis=0)
    counted = totals[:, model_width]
    pooled = totals[:, :model_width] / jnp.maximum(counted, 1.0)[:, None]
    return (encoded.reshape(sec_block, tok_block, model_width), pooled)


def solution(mesh):
    in_specs = (
        P(("groups", "sec"), "plane", None),
        P("groups"),
        P(("groups", "sec"), "plane"),
        P(),
        P("plane", None),
        P("plane", None),
        P("plane", None),
        P("plane", None),
    )
    out_specs = (P(("groups", "sec"), "plane", None), P(("groups", "sec", "plane"), None))
    return jax.shard_map(body, mesh=mesh, in_specs=in_specs, out_specs=out_specs, check_vma=False)
```

```python
import math

import jax
import jax.numpy as jnp
from jax import lax
from jax.sharding import PartitionSpec as P

HEADS = 16
HEAD_DIM = 64
WINDOW = 128


negative_big = -1e30


def shifted_2(value, axis, by):
    peers = lax.axis_size(axis)
    pairs = [(i, i + by) for i in range(peers) if 0 <= i + by < peers]
    return lax.ppermute(value, axis, pairs)


def rms_norm(values, gain):
    wide = values.astype(jnp.float32)
    scaled = wide * lax.rsqrt(jnp.mean(wide * wide, axis=-1, keepdims=True) + 1e-06) * gain
    return scaled.astype(jnp.bfloat16)


def masked_softmax(scores, allowed):
    shifted = jnp.where(allowed, scores, negative_big)
    top = jnp.max(shifted, axis=-1, keepdims=True)
    expo = jnp.where(allowed, jnp.exp(shifted - top), 0.0)
    return (expo / jnp.sum(expo, axis=-1, keepdims=True)).astype(jnp.bfloat16)


def fold_product(inputs, weight_piece):
    return jnp.dot(inputs, weight_piece, preferred_element_type=jnp.float32)


def replica_levels():
    levels = []
    if lax.axis_size("groups") % 2 == 0:
        levels.append(("groups", lax.axis_size("groups"), 1))
    if lax.axis_size("sec") % 4 == 0:
        levels.append(("sec", lax.axis_size("sec"), 2))
    if lax.axis_size("sec") % 2 == 0:
        levels.append(("sec", lax.axis_size("sec"), 1))
    return levels


def rotate_rows(values, axis):
    plane_count = lax.axis_size("plane")
    block = values.shape[axis] // plane_count
    start = (lax.axis_index("plane") + 1) * block
    doubled = jnp.concatenate([values, values], axis=axis)
    return lax.dynamic_slice_in_dim(doubled, start, (plane_count - 1) * block, axis=axis)


def gather_pieces(shards, swap_first=False, skip_middle=False):
    levels = replica_levels()
    if skip_middle and len(levels) == 3:
        levels = [levels[0], levels[2]]
    elif swap_first and len(levels) == 3:
        levels = [levels[1], levels[0], levels[2]]
    count = 2 ** len(levels)
    widths = [shard.shape[1] // count for shard in shards]
    own = 0
    for bit, (axis, _, flip) in enumerate(levels):
        own = own + ((lax.axis_index(axis) // flip) % 2) * (2 ** bit)
    mine = jnp.concatenate(
        [
            lax.dynamic_slice_in_dim(shard, own * width, width, axis=1)
            for shard, width in zip(shards, widths)
        ],
        axis=1,
    )
    gathered = lax.all_gather(mine, "plane", axis=0, tiled=True)
    held = [(own, rotate_rows(gathered, 0))]
    for bit, (axis, size, flip) in enumerate(levels):
        swap = [(i, i ^ flip) for i in range(size)]
        held = held + [
            (piece + (1 - 2 * ((piece // 2 ** bit) % 2)) * 2 ** bit, lax.ppermute(block, axis, swap))
            for piece, block in held
        ]
    results = []
    offset = 0
    for shard, width in zip(shards, widths):
        results.append((shard, [(piece, block[:, offset : offset + width]) for piece, block in held], width))
        offset += width
    return results


def project(inputs, pieces):
    shard, held, width = pieces
    rows = shard.shape[0]
    local_inputs = lax.dynamic_slice_in_dim(inputs, lax.axis_index("plane") * rows, rows, axis=1)
    local = jnp.dot(local_inputs, shard, preferred_element_type=jnp.float32)
    remote_inputs = rotate_rows(inputs, 1)
    remote = jnp.zeros_like(local)
    for piece, block in held:
        part = jnp.dot(remote_inputs, block, preferred_element_type=jnp.float32)
        remote = lax.dynamic_update_slice_in_dim(remote, part, piece * width, axis=1)
    return local + remote


def assemble(pieces):
    shard, held, width = pieces
    remote = jnp.zeros((held[0][1].shape[0], width * len(held)), shard.dtype)
    for piece, block in held:
        remote = lax.dynamic_update_slice_in_dim(remote, block, piece * width, axis=1)
    return shard, remote


def project_whole(inputs, weights):
    shard, remote = weights
    rows = shard.shape[0]
    local_inputs = lax.dynamic_slice_in_dim(inputs, lax.axis_index("plane") * rows, rows, axis=1)
    local = jnp.dot(local_inputs, shard, preferred_element_type=jnp.float32)
    return local + jnp.dot(rotate_rows(inputs, 1), remote, preferred_element_type=jnp.float32)


def attend_items(pieces):
    packed_all, flags_all = pieces
    seq_len = packed_all.shape[2]
    block_len = 512
    score_scale = 1.0 / math.sqrt(HEAD_DIM)
    key_index = jnp.arange(seq_len, dtype=jnp.int32)

    def one_item(item_pair):
        packed, key_flag = item_pair
        key_rows = packed[:, HEAD_DIM : 2 * HEAD_DIM]
        value_rows = packed[:, 2 * HEAD_DIM :]
        key_alive = key_flag > 0.5
        query_blocks = packed[:, :HEAD_DIM].reshape(seq_len // block_len, block_len, HEAD_DIM)
        block_starts = jnp.arange(seq_len // block_len, dtype=jnp.int32) * block_len

        def one_block(block_pair):
            query_rows, offset = block_pair
            scores = (
                jnp.einsum("qd,kd->qk", query_rows, key_rows, preferred_element_type=jnp.float32)
                * score_scale
            )
            own_index = offset + jnp.arange(block_len, dtype=jnp.int32)
            allowed = key_alive[None, :] | (key_index[None, :] == own_index[:, None])
            attention = masked_softmax(scores, allowed)
            return jnp.dot(attention, value_rows, preferred_element_type=jnp.float32).astype(
                jnp.bfloat16
            )

        return lax.map(one_block, (query_blocks, block_starts)).reshape(seq_len, HEAD_DIM)

    return lax.map(one_item, (packed_all[0], flags_all[0]))[None]


def attend_by_section(projected, counts, plane_count):
    sec_block, tok_block = projected.shape[0], projected.shape[1]
    share = HEADS // plane_count
    seq_len = plane_count * tok_block
    score_scale = 1.0 / math.sqrt(HEAD_DIM)
    key_index = jnp.arange(seq_len, dtype=jnp.int32)
    contexts = []
    for local in range(sec_block):
        section = lax.axis_index("sec") * sec_block + local
        key_alive = key_index < lax.dynamic_index_in_dim(counts, section, keepdims=False)
        outgoing = jnp.transpose(
            projected[local].reshape(tok_block, 3, plane_count, share, HEAD_DIM), (2, 3, 0, 1, 4)
        ).reshape(plane_count, share, tok_block, 3 * HEAD_DIM)
        packed = lax.all_to_all(outgoing, "plane", split_axis=0, concat_axis=2, tiled=True)[0]
        queries = packed[:, :, :HEAD_DIM]
        keys = packed[:, :, HEAD_DIM : 2 * HEAD_DIM]
        values = packed[:, :, 2 * HEAD_DIM :]
        scores = (
            jnp.einsum("nqd,nkd->nqk", queries, keys, preferred_element_type=jnp.float32)
            * score_scale
        )
        allowed = key_alive[None, None, :] | (key_index[None, None, :] == key_index[None, :, None])
        attention = masked_softmax(scores, allowed)
        context = jnp.einsum(
            "nqk,nkd->nqd", attention, values, preferred_element_type=jnp.float32
        ).astype(jnp.bfloat16)
        homeward = jnp.transpose(
            context.reshape(share, plane_count, tok_block, HEAD_DIM), (1, 0, 2, 3)
        )
        returned = lax.all_to_all(homeward, "plane", split_axis=0, concat_axis=1, tiled=True)[0]
        contexts.append(jnp.transpose(returned, (1, 0, 2)).reshape(tok_block, HEADS * HEAD_DIM))
    return contexts


def body(tokens, counts, region_ids, norm_gains, cross_qkv, cross_out, plane_qkv, plane_out):
    sec_block, tok_block, model_width = tokens.shape
    plane_count = lax.axis_size("plane")
    regions = 2 * lax.axis_size("sec") * plane_count
    positions = lax.axis_index("plane") * tok_block + jnp.arange(tok_block, dtype=jnp.int32)
    padded_counts = jnp.concatenate(
        [jnp.zeros((1,), jnp.int32), counts, jnp.zeros((1,), jnp.int32)]
    )
    near_counts = lax.dynamic_slice_in_dim(
        padded_counts, lax.axis_index("sec") * sec_block, sec_block + 2
    )
    near_valid = positions[None, :] < near_counts[:, None]
    own_valid = near_valid[1 : sec_block + 1]
    score_scale = 1.0 / math.sqrt(HEAD_DIM)
    cross_qkv_pieces, cross_out_pieces = gather_pieces([cross_qkv, cross_out])
    plane_qkv_pieces, plane_out_pieces = gather_pieces([plane_qkv, plane_out], skip_middle=True)
    cross_out_pieces = assemble(cross_out_pieces)
    plane_out_pieces = assemble(plane_out_pieces)
    normed = rms_norm(tokens, norm_gains[0])
    inputs = normed.reshape(-1, model_width)
    result = project(inputs, cross_qkv_pieces)
    projected = result.astype(jnp.bfloat16).reshape(sec_block, tok_block, 3 * model_width)
    own_kv = projected[:, :, model_width:]
    from_below = shifted_2(own_kv[sec_block - 1], "sec", 1)
    from_above = shifted_2(own_kv[0], "sec", -1)
    near_kv = jnp.concatenate([from_below[None], own_kv, from_above[None]], axis=0)
    queries = projected[:, :, :model_width]
    windows = tok_block // WINDOW
    query_win = queries.reshape(sec_block, windows, WINDOW, HEADS, HEAD_DIM)
    pair_win = near_kv.reshape(sec_block + 2, windows, WINDOW, 2, HEADS, HEAD_DIM)
    stacked = jnp.concatenate(
        [pair_win[0:sec_block], pair_win[1 : sec_block + 1], pair_win[2 : sec_block + 2]], axis=2
    )
    valid_win = near_valid.reshape(sec_block + 2, windows, WINDOW)
    valid_three = jnp.concatenate(
        [valid_win[0:sec_block], valid_win[1 : sec_block + 1], valid_win[2 : sec_block + 2]], axis=2
    )
    itself = jnp.arange(3 * WINDOW)[None, :] == jnp.arange(WINDOW)[:, None] + WINDOW
    scores = (
        jnp.einsum(
            "snqhd,snkhd->snhqk", query_win, stacked[:, :, :, 0], preferred_element_type=jnp.float32
        )
        * score_scale
    )
    allowed = valid_three[:, :, None, None, :] | itself[None, None, None]
    attention = masked_softmax(scores, allowed)
    context = jnp.einsum(
        "snhqk,snkhd->snqhd", attention, stacked[:, :, :, 1], preferred_element_type=jnp.float32
    )
    context = context.astype(jnp.bfloat16).reshape(-1, model_width)
    result = project_whole(context, cross_out_pieces)
    after_cross = (tokens.reshape(-1, model_width).astype(jnp.float32) + result).astype(
        jnp.bfloat16
    )
    normed = rms_norm(after_cross, norm_gains[1])
    result = project(normed, plane_qkv_pieces)
    projected = result.astype(jnp.bfloat16).reshape(sec_block, tok_block, 3, HEADS, HEAD_DIM)
    if HEADS % plane_count == 0:
        contexts = attend_by_section(projected, counts, plane_count)
    else:
        per_device = sec_block * HEADS // plane_count
        heads_first = jnp.transpose(projected, (0, 3, 1, 2, 4)).reshape(
            plane_count, per_device, tok_block, 3 * HEAD_DIM
        )
        key_flags = jnp.broadcast_to(own_valid[:, None, :], (sec_block, HEADS, tok_block)).astype(
            jnp.bfloat16
        )
        key_flags = key_flags.reshape(plane_count, per_device, tok_block)
        attended = attend_items(
            (
                lax.all_to_all(heads_first, "plane", split_axis=0, concat_axis=2, tiled=True),
                lax.all_to_all(key_flags, "plane", split_axis=0, concat_axis=2, tiled=True),
            )
        )
        returned = lax.all_to_all(attended, "plane", split_axis=2, concat_axis=0, tiled=True)
        contexts = [
            jnp.transpose(
                returned.reshape(sec_block, HEADS, tok_block, HEAD_DIM), (0, 2, 1, 3)
            ).reshape(-1, model_width)
        ]
    labels = region_ids.reshape(-1)
    member = (jnp.arange(regions, dtype=jnp.int32)[:, None] == labels[None, :]) & own_valid.reshape(
        -1
    )[None, :]
    member = member.astype(jnp.bfloat16)
    pieces_out = []
    partial = None
    row = 0
    for context in contexts:
        span = context.shape[0]
        result = project_whole(context, plane_out_pieces)
        piece = (after_cross[row : row + span].astype(jnp.float32) + result).astype(jnp.bfloat16)
        pieces_out.append(piece)
        extended = jnp.concatenate([piece, jnp.ones((span, 128), jnp.bfloat16)], axis=1)
        term = jnp.dot(member[:, row : row + span], extended, preferred_element_type=jnp.float32)
        partial = term if partial is None else partial + term
        row += span
    encoded = jnp.concatenate(pieces_out, axis=0)
    sections = lax.axis_size("sec")
    width = partial.shape[1]
    partial = partial.reshape(sections, plane_count, 2, width)
    me_plane = lax.axis_index("plane")
    gathered = lax.dynamic_index_in_dim(partial, me_plane, axis=1, keepdims=False)
    for step in range(1, plane_count):
        moved = [(i, (i + step) % plane_count) for i in range(plane_count)]
        target = lax.rem(me_plane + step, plane_count)
        block = lax.dynamic_index_in_dim(partial, target, axis=1, keepdims=False)
        gathered = gathered + lax.ppermute(block, "plane", moved)
    me_sec = lax.axis_index("sec")
    totals = lax.dynamic_index_in_dim(gathered, me_sec, axis=0, keepdims=False)
    for step in range(1, sections):
        moved = [(i, (i + step) % sections) for i in range(sections)]
        target = lax.rem(me_sec + step, sections)
        block = lax.dynamic_index_in_dim(gathered, target, axis=0, keepdims=False)
        totals = totals + lax.ppermute(block, "sec", moved)
    counted = totals[:, model_width]
    pooled = totals[:, :model_width] / jnp.maximum(counted, 1.0)[:, None]
    return (encoded.reshape(sec_block, tok_block, model_width), pooled)


def solution(mesh):
    in_specs = (
        P(("groups", "sec"), "plane", None),
        P("groups"),
        P(("groups", "sec"), "plane"),
        P(),
        P("plane", None),
        P("plane", None),
        P("plane", None),
        P("plane", None),
    )
    out_specs = (P(("groups", "sec"), "plane", None), P(("groups", "sec", "plane"), None))
    return jax.shard_map(body, mesh=mesh, in_specs=in_specs, out_specs=out_specs, check_vma=False)
```

```python
import math

import jax
import jax.numpy as jnp
from jax import lax
from jax.sharding import PartitionSpec as P

HEADS = 16
HEAD_DIM = 64
WINDOW = 128


negative_big = -1e30


def shifted_2(value, axis, by):
    peers = lax.axis_size(axis)
    pairs = [(i, i + by) for i in range(peers) if 0 <= i + by < peers]
    return lax.ppermute(value, axis, pairs)


def rms_norm(values, gain):
    wide = values.astype(jnp.float32)
    scaled = wide * lax.rsqrt(jnp.mean(wide * wide, axis=-1, keepdims=True) + 1e-06) * gain
    return scaled.astype(jnp.bfloat16)


def masked_softmax(scores, allowed):
    shifted = jnp.where(allowed, scores, negative_big)
    top = jnp.max(shifted, axis=-1, keepdims=True)
    expo = jnp.where(allowed, jnp.exp(shifted - top), 0.0)
    return (expo / jnp.sum(expo, axis=-1, keepdims=True)).astype(jnp.bfloat16)


def fold_product(inputs, weight_piece):
    return jnp.dot(inputs, weight_piece, preferred_element_type=jnp.float32)


def replica_levels():
    levels = []
    if lax.axis_size("groups") % 2 == 0:
        levels.append(("groups", lax.axis_size("groups"), 1))
    if lax.axis_size("sec") % 4 == 0:
        levels.append(("sec", lax.axis_size("sec"), 2))
    if lax.axis_size("sec") % 2 == 0:
        levels.append(("sec", lax.axis_size("sec"), 1))
    return levels


def rotate_rows(values, axis):
    plane_count = lax.axis_size("plane")
    block = values.shape[axis] // plane_count
    start = (lax.axis_index("plane") + 1) * block
    doubled = jnp.concatenate([values, values], axis=axis)
    return lax.dynamic_slice_in_dim(doubled, start, (plane_count - 1) * block, axis=axis)


def gather_pieces(shards, swap_first=False, skip_middle=False, full_rows=False):
    levels = replica_levels()
    if skip_middle and len(levels) == 3:
        levels = [levels[0], levels[2]]
    elif swap_first and len(levels) == 3:
        levels = [levels[1], levels[0], levels[2]]
    count = 2 ** len(levels)
    widths = [shard.shape[1] // count for shard in shards]
    own = 0
    for bit, (axis, _, flip) in enumerate(levels):
        own = own + ((lax.axis_index(axis) // flip) % 2) * (2 ** bit)
    mine = jnp.concatenate(
        [
            lax.dynamic_slice_in_dim(shard, own * width, width, axis=1)
            for shard, width in zip(shards, widths)
        ],
        axis=1,
    )
    gathered = lax.all_gather(mine, "plane", axis=0, tiled=True)
    held = [(own, gathered if full_rows else rotate_rows(gathered, 0))]
    for bit, (axis, size, flip) in enumerate(levels):
        swap = [(i, i ^ flip) for i in range(size)]
        held = held + [
            (piece + (1 - 2 * ((piece // 2 ** bit) % 2)) * 2 ** bit, lax.ppermute(block, axis, swap))
            for piece, block in held
        ]
    results = []
    offset = 0
    for shard, width in zip(shards, widths):
        results.append(
            (
                shard,
                [(piece, block[:, offset : offset + width]) for piece, block in held],
                width,
                full_rows,
            )
        )
        offset += width
    return results


def project(inputs, pieces):
    shard, held, width, full_rows = pieces
    rows = shard.shape[0]
    out = jnp.zeros((inputs.shape[0], shard.shape[1]), jnp.float32)
    remote_inputs = inputs if full_rows else rotate_rows(inputs, 1)
    for piece, block in held:
        part = jnp.dot(remote_inputs, block, preferred_element_type=jnp.float32)
        out = lax.dynamic_update_slice_in_dim(out, part, piece * width, axis=1)
    if full_rows:
        return out
    local_inputs = lax.dynamic_slice_in_dim(inputs, lax.axis_index("plane") * rows, rows, axis=1)
    return jnp.dot(local_inputs, shard, preferred_element_type=jnp.float32) + out


def assemble(pieces):
    shard, held, width, full_rows = pieces
    remote = jnp.zeros((held[0][1].shape[0], width * len(held)), shard.dtype)
    for piece, block in held:
        remote = lax.dynamic_update_slice_in_dim(remote, block, piece * width, axis=1)
    return shard, remote, full_rows


def project_whole(inputs, weights):
    shard, remote, full_rows = weights
    if full_rows:
        return jnp.dot(inputs, remote, preferred_element_type=jnp.float32)
    rows = shard.shape[0]
    local_inputs = lax.dynamic_slice_in_dim(inputs, lax.axis_index("plane") * rows, rows, axis=1)
    local = jnp.dot(local_inputs, shard, preferred_element_type=jnp.float32)
    return local + jnp.dot(rotate_rows(inputs, 1), remote, preferred_element_type=jnp.float32)


def attend_items(pieces):
    packed_all, flags_all = pieces
    seq_len = packed_all.shape[2]
    block_len = 512
    score_scale = 1.0 / math.sqrt(HEAD_DIM)
    key_index = jnp.arange(seq_len, dtype=jnp.int32)

    def one_item(item_pair):
        packed, key_flag = item_pair
        key_rows = packed[:, HEAD_DIM : 2 * HEAD_DIM]
        value_rows = packed[:, 2 * HEAD_DIM :]
        key_alive = key_flag > 0.5
        query_blocks = packed[:, :HEAD_DIM].reshape(seq_len // block_len, block_len, HEAD_DIM)
        block_starts = jnp.arange(seq_len // block_len, dtype=jnp.int32) * block_len

        def one_block(block_pair):
            query_rows, offset = block_pair
            scores = (
                jnp.einsum("qd,kd->qk", query_rows, key_rows, preferred_element_type=jnp.float32)
                * score_scale
            )
            own_index = offset + jnp.arange(block_len, dtype=jnp.int32)
            allowed = key_alive[None, :] | (key_index[None, :] == own_index[:, None])
            attention = masked_softmax(scores, allowed)
            return jnp.dot(attention, value_rows, preferred_element_type=jnp.float32).astype(
                jnp.bfloat16
            )

        return lax.map(one_block, (query_blocks, block_starts)).reshape(seq_len, HEAD_DIM)

    return lax.map(one_item, (packed_all[0], flags_all[0]))[None]


def attend_by_section(projected, counts, plane_count):
    sec_block, tok_block = projected.shape[0], projected.shape[1]
    share = HEADS // plane_count
    seq_len = plane_count * tok_block
    score_scale = 1.0 / math.sqrt(HEAD_DIM)
    key_index = jnp.arange(seq_len, dtype=jnp.int32)
    contexts = []
    for local in range(sec_block):
        section = lax.axis_index("sec") * sec_block + local
        key_alive = key_index < lax.dynamic_index_in_dim(counts, section, keepdims=False)
        outgoing = jnp.transpose(
            projected[local].reshape(tok_block, 3, plane_count, share, HEAD_DIM), (2, 3, 0, 1, 4)
        ).reshape(plane_count, share, tok_block, 3 * HEAD_DIM)
        packed = lax.all_to_all(outgoing, "plane", split_axis=0, concat_axis=2, tiled=True)[0]
        queries = packed[:, :, :HEAD_DIM]
        keys = packed[:, :, HEAD_DIM : 2 * HEAD_DIM]
        values = packed[:, :, 2 * HEAD_DIM :]
        scores = (
            jnp.einsum("nqd,nkd->nqk", queries, keys, preferred_element_type=jnp.float32)
            * score_scale
        )
        allowed = key_alive[None, None, :] | (key_index[None, None, :] == key_index[None, :, None])
        attention = masked_softmax(scores, allowed)
        context = jnp.einsum(
            "nqk,nkd->nqd", attention, values, preferred_element_type=jnp.float32
        ).astype(jnp.bfloat16)
        homeward = jnp.transpose(
            context.reshape(share, plane_count, tok_block, HEAD_DIM), (1, 0, 2, 3)
        )
        returned = lax.all_to_all(homeward, "plane", split_axis=0, concat_axis=1, tiled=True)[0]
        contexts.append(jnp.transpose(returned, (1, 0, 2)).reshape(tok_block, HEADS * HEAD_DIM))
    return contexts


def body(tokens, counts, region_ids, norm_gains, cross_qkv, cross_out, plane_qkv, plane_out):
    sec_block, tok_block, model_width = tokens.shape
    plane_count = lax.axis_size("plane")
    regions = 2 * lax.axis_size("sec") * plane_count
    positions = lax.axis_index("plane") * tok_block + jnp.arange(tok_block, dtype=jnp.int32)
    padded_counts = jnp.concatenate(
        [jnp.zeros((1,), jnp.int32), counts, jnp.zeros((1,), jnp.int32)]
    )
    near_counts = lax.dynamic_slice_in_dim(
        padded_counts, lax.axis_index("sec") * sec_block, sec_block + 2
    )
    near_valid = positions[None, :] < near_counts[:, None]
    own_valid = near_valid[1 : sec_block + 1]
    score_scale = 1.0 / math.sqrt(HEAD_DIM)
    cross_qkv_pieces, cross_out_pieces = gather_pieces([cross_qkv, cross_out])
    plane_qkv_pieces, plane_out_pieces = gather_pieces(
        [plane_qkv, plane_out], skip_middle=True, full_rows=True
    )
    cross_out_pieces = assemble(cross_out_pieces)
    plane_out_pieces = assemble(plane_out_pieces)
    normed = rms_norm(tokens, norm_gains[0])
    inputs = normed.reshape(-1, model_width)
    result = project(inputs, cross_qkv_pieces)
    projected = result.astype(jnp.bfloat16).reshape(sec_block, tok_block, 3 * model_width)
    own_kv = projected[:, :, model_width:]
    from_below = shifted_2(own_kv[sec_block - 1], "sec", 1)
    from_above = shifted_2(own_kv[0], "sec", -1)
    near_kv = jnp.concatenate([from_below[None], own_kv, from_above[None]], axis=0)
    queries = projected[:, :, :model_width]
    windows = tok_block // WINDOW
    query_win = queries.reshape(sec_block, windows, WINDOW, HEADS, HEAD_DIM)
    pair_win = near_kv.reshape(sec_block + 2, windows, WINDOW, 2, HEADS, HEAD_DIM)
    stacked = jnp.concatenate(
        [pair_win[0:sec_block], pair_win[1 : sec_block + 1], pair_win[2 : sec_block + 2]], axis=2
    )
    valid_win = near_valid.reshape(sec_block + 2, windows, WINDOW)
    valid_three = jnp.concatenate(
        [valid_win[0:sec_block], valid_win[1 : sec_block + 1], valid_win[2 : sec_block + 2]], axis=2
    )
    itself = jnp.arange(3 * WINDOW)[None, :] == jnp.arange(WINDOW)[:, None] + WINDOW
    scores = (
        jnp.einsum(
            "snqhd,snkhd->snhqk", query_win, stacked[:, :, :, 0], preferred_element_type=jnp.float32
        )
        * score_scale
    )
    allowed = valid_three[:, :, None, None, :] | itself[None, None, None]
    attention = masked_softmax(scores, allowed)
    context = jnp.einsum(
        "snhqk,snkhd->snqhd", attention, stacked[:, :, :, 1], preferred_element_type=jnp.float32
    )
    context = context.astype(jnp.bfloat16).reshape(-1, model_width)
    result = project_whole(context, cross_out_pieces)
    after_cross = (tokens.reshape(-1, model_width).astype(jnp.float32) + result).astype(
        jnp.bfloat16
    )
    normed = rms_norm(after_cross, norm_gains[1])
    result = project(normed, plane_qkv_pieces)
    projected = result.astype(jnp.bfloat16).reshape(sec_block, tok_block, 3, HEADS, HEAD_DIM)
    if HEADS % plane_count == 0:
        contexts = attend_by_section(projected, counts, plane_count)
    else:
        per_device = sec_block * HEADS // plane_count
        heads_first = jnp.transpose(projected, (0, 3, 1, 2, 4)).reshape(
            plane_count, per_device, tok_block, 3 * HEAD_DIM
        )
        key_flags = jnp.broadcast_to(own_valid[:, None, :], (sec_block, HEADS, tok_block)).astype(
            jnp.bfloat16
        )
        key_flags = key_flags.reshape(plane_count, per_device, tok_block)
        attended = attend_items(
            (
                lax.all_to_all(heads_first, "plane", split_axis=0, concat_axis=2, tiled=True),
                lax.all_to_all(key_flags, "plane", split_axis=0, concat_axis=2, tiled=True),
            )
        )
        returned = lax.all_to_all(attended, "plane", split_axis=2, concat_axis=0, tiled=True)
        contexts = [
            jnp.transpose(
                returned.reshape(sec_block, HEADS, tok_block, HEAD_DIM), (0, 2, 1, 3)
            ).reshape(-1, model_width)
        ]
    labels = region_ids.reshape(-1)
    member = (jnp.arange(regions, dtype=jnp.int32)[:, None] == labels[None, :]) & own_valid.reshape(
        -1
    )[None, :]
    member = member.astype(jnp.bfloat16)
    pieces_out = []
    partial = None
    row = 0
    for context in contexts:
        span = context.shape[0]
        result = project_whole(context, plane_out_pieces)
        piece = (after_cross[row : row + span].astype(jnp.float32) + result).astype(jnp.bfloat16)
        pieces_out.append(piece)
        extended = jnp.concatenate([piece, jnp.ones((span, 128), jnp.bfloat16)], axis=1)
        term = jnp.dot(member[:, row : row + span], extended, preferred_element_type=jnp.float32)
        partial = term if partial is None else partial + term
        row += span
    encoded = jnp.concatenate(pieces_out, axis=0)
    sections = lax.axis_size("sec")
    width = partial.shape[1]
    partial = partial.reshape(sections, plane_count, 2, width)
    me_plane = lax.axis_index("plane")
    gathered = lax.dynamic_index_in_dim(partial, me_plane, axis=1, keepdims=False)
    for step in range(1, plane_count):
        moved = [(i, (i + step) % plane_count) for i in range(plane_count)]
        target = lax.rem(me_plane + step, plane_count)
        block = lax.dynamic_index_in_dim(partial, target, axis=1, keepdims=False)
        gathered = gathered + lax.ppermute(block, "plane", moved)
    me_sec = lax.axis_index("sec")
    totals = lax.dynamic_index_in_dim(gathered, me_sec, axis=0, keepdims=False)
    for step in range(1, sections):
        moved = [(i, (i + step) % sections) for i in range(sections)]
        target = lax.rem(me_sec + step, sections)
        block = lax.dynamic_index_in_dim(gathered, target, axis=0, keepdims=False)
        totals = totals + lax.ppermute(block, "sec", moved)
    counted = totals[:, model_width]
    pooled = totals[:, :model_width] / jnp.maximum(counted, 1.0)[:, None]
    return (encoded.reshape(sec_block, tok_block, model_width), pooled)


def solution(mesh):
    in_specs = (
        P(("groups", "sec"), "plane", None),
        P("groups"),
        P(("groups", "sec"), "plane"),
        P(),
        P("plane", None),
        P("plane", None),
        P("plane", None),
        P("plane", None),
    )
    out_specs = (P(("groups", "sec"), "plane", None), P(("groups", "sec", "plane"), None))
    return jax.shard_map(body, mesh=mesh, in_specs=in_specs, out_specs=out_specs, check_vma=False)
```

```python
import math

import jax
import jax.numpy as jnp
from jax import lax
from jax.sharding import PartitionSpec as P

HEADS = 16
HEAD_DIM = 64
WINDOW = 128


negative_big = -1e30


def shifted_2(value, axis, by):
    peers = lax.axis_size(axis)
    pairs = [(i, i + by) for i in range(peers) if 0 <= i + by < peers]
    return lax.ppermute(value, axis, pairs)


def rms_norm(values, gain):
    wide = values.astype(jnp.float32)
    scaled = wide * lax.rsqrt(jnp.mean(wide * wide, axis=-1, keepdims=True) + 1e-06) * gain
    return scaled.astype(jnp.bfloat16)


def masked_softmax(scores, allowed):
    shifted = jnp.where(allowed, scores, negative_big)
    top = jnp.max(shifted, axis=-1, keepdims=True)
    expo = jnp.where(allowed, jnp.exp(shifted - top), 0.0)
    return (expo / jnp.sum(expo, axis=-1, keepdims=True)).astype(jnp.bfloat16)


def fold_product(inputs, weight_piece):
    return jnp.dot(inputs, weight_piece, preferred_element_type=jnp.float32)


def replica_levels():
    levels = []
    if lax.axis_size("groups") % 2 == 0:
        levels.append(("groups", lax.axis_size("groups"), 1))
    if lax.axis_size("sec") % 4 == 0:
        levels.append(("sec", lax.axis_size("sec"), 2))
    if lax.axis_size("sec") % 2 == 0:
        levels.append(("sec", lax.axis_size("sec"), 1))
    return levels


def rotate_rows(values, axis):
    plane_count = lax.axis_size("plane")
    block = values.shape[axis] // plane_count
    start = (lax.axis_index("plane") + 1) * block
    doubled = jnp.concatenate([values, values], axis=axis)
    return lax.dynamic_slice_in_dim(doubled, start, (plane_count - 1) * block, axis=axis)


def gather_pieces(shards, swap_first=False, skip_middle=False, full_rows=False):
    levels = replica_levels()
    if skip_middle and len(levels) == 3:
        levels = [levels[0], levels[2]]
    elif swap_first and len(levels) == 3:
        levels = [levels[1], levels[0], levels[2]]
    count = 2 ** len(levels)
    widths = [shard.shape[1] // count for shard in shards]
    own = 0
    for bit, (axis, _, flip) in enumerate(levels):
        own = own + ((lax.axis_index(axis) // flip) % 2) * (2 ** bit)
    mine = jnp.concatenate(
        [
            lax.dynamic_slice_in_dim(shard, own * width, width, axis=1)
            for shard, width in zip(shards, widths)
        ],
        axis=1,
    )
    gathered = lax.all_gather(mine, "plane", axis=0, tiled=True)
    held = [(own, gathered if full_rows else rotate_rows(gathered, 0))]
    for bit, (axis, size, flip) in enumerate(levels):
        swap = [(i, i ^ flip) for i in range(size)]
        held = held + [
            (piece + (1 - 2 * ((piece // 2 ** bit) % 2)) * 2 ** bit, lax.ppermute(block, axis, swap))
            for piece, block in held
        ]
    results = []
    offset = 0
    for shard, width in zip(shards, widths):
        results.append(
            (
                shard,
                [(piece, block[:, offset : offset + width]) for piece, block in held],
                width,
                full_rows,
            )
        )
        offset += width
    return results


def project(inputs, pieces):
    shard, held, width, full_rows = pieces
    rows = shard.shape[0]
    out = jnp.zeros((inputs.shape[0], shard.shape[1]), jnp.float32)
    remote_inputs = inputs if full_rows else rotate_rows(inputs, 1)
    for piece, block in held:
        part = jnp.dot(remote_inputs, block, preferred_element_type=jnp.float32)
        out = lax.dynamic_update_slice_in_dim(out, part, piece * width, axis=1)
    if full_rows:
        return out
    local_inputs = lax.dynamic_slice_in_dim(inputs, lax.axis_index("plane") * rows, rows, axis=1)
    return jnp.dot(local_inputs, shard, preferred_element_type=jnp.float32) + out


def assemble(pieces):
    shard, held, width, full_rows = pieces
    remote = jnp.zeros((held[0][1].shape[0], width * len(held)), shard.dtype)
    for piece, block in held:
        remote = lax.dynamic_update_slice_in_dim(remote, block, piece * width, axis=1)
    return shard, remote, full_rows


def project_whole(inputs, weights):
    shard, remote, full_rows = weights
    if full_rows:
        return jnp.dot(inputs, remote, preferred_element_type=jnp.float32)
    rows = shard.shape[0]
    local_inputs = lax.dynamic_slice_in_dim(inputs, lax.axis_index("plane") * rows, rows, axis=1)
    local = jnp.dot(local_inputs, shard, preferred_element_type=jnp.float32)
    return local + jnp.dot(rotate_rows(inputs, 1), remote, preferred_element_type=jnp.float32)


def attend_items(pieces):
    packed_all, flags_all = pieces
    seq_len = packed_all.shape[2]
    block_len = 512
    score_scale = 1.0 / math.sqrt(HEAD_DIM)
    key_index = jnp.arange(seq_len, dtype=jnp.int32)

    def one_item(item_pair):
        packed, key_flag = item_pair
        key_rows = packed[:, HEAD_DIM : 2 * HEAD_DIM]
        value_rows = packed[:, 2 * HEAD_DIM :]
        key_alive = key_flag > 0.5
        query_blocks = packed[:, :HEAD_DIM].reshape(seq_len // block_len, block_len, HEAD_DIM)
        block_starts = jnp.arange(seq_len // block_len, dtype=jnp.int32) * block_len

        def one_block(block_pair):
            query_rows, offset = block_pair
            scores = (
                jnp.einsum("qd,kd->qk", query_rows, key_rows, preferred_element_type=jnp.float32)
                * score_scale
            )
            own_index = offset + jnp.arange(block_len, dtype=jnp.int32)
            allowed = key_alive[None, :] | (key_index[None, :] == own_index[:, None])
            attention = masked_softmax(scores, allowed)
            return jnp.dot(attention, value_rows, preferred_element_type=jnp.float32).astype(
                jnp.bfloat16
            )

        return lax.map(one_block, (query_blocks, block_starts)).reshape(seq_len, HEAD_DIM)

    return lax.map(one_item, (packed_all[0], flags_all[0]))[None]


def attend_by_section(projected, counts, plane_count):
    sec_block, tok_block = projected.shape[0], projected.shape[1]
    share = HEADS // plane_count
    seq_len = plane_count * tok_block
    score_scale = 1.0 / math.sqrt(HEAD_DIM)
    key_index = jnp.arange(seq_len, dtype=jnp.int32)
    contexts = []
    for local in range(sec_block):
        section = lax.axis_index("sec") * sec_block + local
        key_alive = key_index < lax.dynamic_index_in_dim(counts, section, keepdims=False)
        outgoing = jnp.transpose(
            projected[local].reshape(tok_block, 3, plane_count, share, HEAD_DIM), (2, 3, 0, 1, 4)
        ).reshape(plane_count, share, tok_block, 3 * HEAD_DIM)
        packed = lax.all_to_all(outgoing, "plane", split_axis=0, concat_axis=2, tiled=True)[0]
        queries = packed[:, :, :HEAD_DIM]
        keys = packed[:, :, HEAD_DIM : 2 * HEAD_DIM]
        values = packed[:, :, 2 * HEAD_DIM :]
        scores = (
            jnp.einsum("nqd,nkd->nqk", queries, keys, preferred_element_type=jnp.float32)
            * score_scale
        )
        allowed = key_alive[None, None, :] | (key_index[None, None, :] == key_index[None, :, None])
        attention = masked_softmax(scores, allowed)
        context = jnp.einsum(
            "nqk,nkd->nqd", attention, values, preferred_element_type=jnp.float32
        ).astype(jnp.bfloat16)
        homeward = jnp.transpose(
            context.reshape(share, plane_count, tok_block, HEAD_DIM), (1, 0, 2, 3)
        )
        returned = lax.all_to_all(homeward, "plane", split_axis=0, concat_axis=1, tiled=True)[0]
        contexts.append(jnp.transpose(returned, (1, 0, 2)).reshape(tok_block, HEADS * HEAD_DIM))
    return contexts


def body(tokens, counts, region_ids, norm_gains, cross_qkv, cross_out, plane_qkv, plane_out):
    sec_block, tok_block, model_width = tokens.shape
    plane_count = lax.axis_size("plane")
    regions = 2 * lax.axis_size("sec") * plane_count
    positions = lax.axis_index("plane") * tok_block + jnp.arange(tok_block, dtype=jnp.int32)
    padded_counts = jnp.concatenate(
        [jnp.zeros((1,), jnp.int32), counts, jnp.zeros((1,), jnp.int32)]
    )
    near_counts = lax.dynamic_slice_in_dim(
        padded_counts, lax.axis_index("sec") * sec_block, sec_block + 2
    )
    near_valid = positions[None, :] < near_counts[:, None]
    own_valid = near_valid[1 : sec_block + 1]
    score_scale = 1.0 / math.sqrt(HEAD_DIM)
    cross_qkv_pieces, cross_out_pieces = gather_pieces([cross_qkv, cross_out], full_rows=True)
    plane_qkv_pieces, plane_out_pieces = gather_pieces(
        [plane_qkv, plane_out], skip_middle=True, full_rows=True
    )
    cross_out_pieces = assemble(cross_out_pieces)
    plane_out_pieces = assemble(plane_out_pieces)
    normed = rms_norm(tokens, norm_gains[0])
    inputs = normed.reshape(-1, model_width)
    result = project(inputs, cross_qkv_pieces)
    projected = result.astype(jnp.bfloat16).reshape(sec_block, tok_block, 3 * model_width)
    own_kv = projected[:, :, model_width:]
    from_below = shifted_2(own_kv[sec_block - 1], "sec", 1)
    from_above = shifted_2(own_kv[0], "sec", -1)
    near_kv = jnp.concatenate([from_below[None], own_kv, from_above[None]], axis=0)
    queries = projected[:, :, :model_width]
    windows = tok_block // WINDOW
    query_win = queries.reshape(sec_block, windows, WINDOW, HEADS, HEAD_DIM)
    pair_win = near_kv.reshape(sec_block + 2, windows, WINDOW, 2, HEADS, HEAD_DIM)
    stacked = jnp.concatenate(
        [pair_win[0:sec_block], pair_win[1 : sec_block + 1], pair_win[2 : sec_block + 2]], axis=2
    )
    valid_win = near_valid.reshape(sec_block + 2, windows, WINDOW)
    valid_three = jnp.concatenate(
        [valid_win[0:sec_block], valid_win[1 : sec_block + 1], valid_win[2 : sec_block + 2]], axis=2
    )
    itself = jnp.arange(3 * WINDOW)[None, :] == jnp.arange(WINDOW)[:, None] + WINDOW
    scores = (
        jnp.einsum(
            "snqhd,snkhd->snhqk", query_win, stacked[:, :, :, 0], preferred_element_type=jnp.float32
        )
        * score_scale
    )
    allowed = valid_three[:, :, None, None, :] | itself[None, None, None]
    attention = masked_softmax(scores, allowed)
    context = jnp.einsum(
        "snhqk,snkhd->snqhd", attention, stacked[:, :, :, 1], preferred_element_type=jnp.float32
    )
    context = context.astype(jnp.bfloat16).reshape(-1, model_width)
    result = project_whole(context, cross_out_pieces)
    after_cross = (tokens.reshape(-1, model_width).astype(jnp.float32) + result).astype(
        jnp.bfloat16
    )
    normed = rms_norm(after_cross, norm_gains[1])
    result = project(normed, plane_qkv_pieces)
    projected = result.astype(jnp.bfloat16).reshape(sec_block, tok_block, 3, HEADS, HEAD_DIM)
    if HEADS % plane_count == 0:
        contexts = attend_by_section(projected, counts, plane_count)
    else:
        per_device = sec_block * HEADS // plane_count
        heads_first = jnp.transpose(projected, (0, 3, 1, 2, 4)).reshape(
            plane_count, per_device, tok_block, 3 * HEAD_DIM
        )
        key_flags = jnp.broadcast_to(own_valid[:, None, :], (sec_block, HEADS, tok_block)).astype(
            jnp.bfloat16
        )
        key_flags = key_flags.reshape(plane_count, per_device, tok_block)
        attended = attend_items(
            (
                lax.all_to_all(heads_first, "plane", split_axis=0, concat_axis=2, tiled=True),
                lax.all_to_all(key_flags, "plane", split_axis=0, concat_axis=2, tiled=True),
            )
        )
        returned = lax.all_to_all(attended, "plane", split_axis=2, concat_axis=0, tiled=True)
        contexts = [
            jnp.transpose(
                returned.reshape(sec_block, HEADS, tok_block, HEAD_DIM), (0, 2, 1, 3)
            ).reshape(-1, model_width)
        ]
    labels = region_ids.reshape(-1)
    member = (jnp.arange(regions, dtype=jnp.int32)[:, None] == labels[None, :]) & own_valid.reshape(
        -1
    )[None, :]
    member = member.astype(jnp.bfloat16)
    pieces_out = []
    partial = None
    row = 0
    for context in contexts:
        span = context.shape[0]
        result = project_whole(context, plane_out_pieces)
        piece = (after_cross[row : row + span].astype(jnp.float32) + result).astype(jnp.bfloat16)
        pieces_out.append(piece)
        extended = jnp.concatenate([piece, jnp.ones((span, 128), jnp.bfloat16)], axis=1)
        term = jnp.dot(member[:, row : row + span], extended, preferred_element_type=jnp.float32)
        partial = term if partial is None else partial + term
        row += span
    encoded = jnp.concatenate(pieces_out, axis=0)
    sections = lax.axis_size("sec")
    width = partial.shape[1]
    partial = partial.reshape(sections, plane_count, 2, width)
    me_plane = lax.axis_index("plane")
    gathered = lax.dynamic_index_in_dim(partial, me_plane, axis=1, keepdims=False)
    for step in range(1, plane_count):
        moved = [(i, (i + step) % plane_count) for i in range(plane_count)]
        target = lax.rem(me_plane + step, plane_count)
        block = lax.dynamic_index_in_dim(partial, target, axis=1, keepdims=False)
        gathered = gathered + lax.ppermute(block, "plane", moved)
    me_sec = lax.axis_index("sec")
    totals = lax.dynamic_index_in_dim(gathered, me_sec, axis=0, keepdims=False)
    for step in range(1, sections):
        moved = [(i, (i + step) % sections) for i in range(sections)]
        target = lax.rem(me_sec + step, sections)
        block = lax.dynamic_index_in_dim(gathered, target, axis=0, keepdims=False)
        totals = totals + lax.ppermute(block, "sec", moved)
    counted = totals[:, model_width]
    pooled = totals[:, :model_width] / jnp.maximum(counted, 1.0)[:, None]
    return (encoded.reshape(sec_block, tok_block, model_width), pooled)


def solution(mesh):
    in_specs = (
        P(("groups", "sec"), "plane", None),
        P("groups"),
        P(("groups", "sec"), "plane"),
        P(),
        P("plane", None),
        P("plane", None),
        P("plane", None),
        P("plane", None),
    )
    out_specs = (P(("groups", "sec"), "plane", None), P(("groups", "sec", "plane"), None))
    return jax.shard_map(body, mesh=mesh, in_specs=in_specs, out_specs=out_specs, check_vma=False)
```

```python
import math

import jax
import jax.numpy as jnp
from jax import lax
from jax.sharding import PartitionSpec as P

HEADS = 16
HEAD_DIM = 64
WINDOW = 128


negative_big = -1e30


def shifted_2(value, axis, by):
    peers = lax.axis_size(axis)
    pairs = [(i, i + by) for i in range(peers) if 0 <= i + by < peers]
    return lax.ppermute(value, axis, pairs)


def rms_norm(values, gain):
    wide = values.astype(jnp.float32)
    scaled = wide * lax.rsqrt(jnp.mean(wide * wide, axis=-1, keepdims=True) + 1e-06) * gain
    return scaled.astype(jnp.bfloat16)


def masked_softmax(scores, allowed):
    shifted = jnp.where(allowed, scores, negative_big)
    top = jnp.max(shifted, axis=-1, keepdims=True)
    expo = jnp.where(allowed, jnp.exp(shifted - top), 0.0)
    return (expo / jnp.sum(expo, axis=-1, keepdims=True)).astype(jnp.bfloat16)


def fold_product(inputs, weight_piece):
    return jnp.dot(inputs, weight_piece, preferred_element_type=jnp.float32)


def replica_levels():
    levels = []
    if lax.axis_size("groups") % 2 == 0:
        levels.append(("groups", lax.axis_size("groups"), 1))
    if lax.axis_size("sec") % 4 == 0:
        levels.append(("sec", lax.axis_size("sec"), 2))
    if lax.axis_size("sec") % 2 == 0:
        levels.append(("sec", lax.axis_size("sec"), 1))
    return levels


def rotate_rows(values, axis):
    plane_count = lax.axis_size("plane")
    block = values.shape[axis] // plane_count
    start = (lax.axis_index("plane") + 1) * block
    doubled = jnp.concatenate([values, values], axis=axis)
    return lax.dynamic_slice_in_dim(doubled, start, (plane_count - 1) * block, axis=axis)


def gather_pieces(shards, swap_first=False, skip_middle=False, full_rows=False):
    levels = replica_levels()
    if skip_middle and len(levels) == 3:
        levels = [levels[0], levels[2]]
    elif swap_first and len(levels) == 3:
        levels = [levels[1], levels[0], levels[2]]
    count = 2 ** len(levels)
    widths = [shard.shape[1] // count for shard in shards]
    own = 0
    for bit, (axis, _, flip) in enumerate(levels):
        own = own + ((lax.axis_index(axis) // flip) % 2) * (2 ** bit)
    mine = jnp.concatenate(
        [
            lax.dynamic_slice_in_dim(shard, own * width, width, axis=1)
            for shard, width in zip(shards, widths)
        ],
        axis=1,
    )
    gathered = lax.all_gather(mine, "plane", axis=0, tiled=True)
    held = [(own, gathered if full_rows else rotate_rows(gathered, 0))]
    for bit, (axis, size, flip) in enumerate(levels):
        swap = [(i, i ^ flip) for i in range(size)]
        held = held + [
            (piece + (1 - 2 * ((piece // 2 ** bit) % 2)) * 2 ** bit, lax.ppermute(block, axis, swap))
            for piece, block in held
        ]
    results = []
    offset = 0
    for shard, width in zip(shards, widths):
        results.append(
            (
                shard,
                [(piece, block[:, offset : offset + width]) for piece, block in held],
                width,
                full_rows,
            )
        )
        offset += width
    return results


def project(inputs, pieces):
    shard, held, width, full_rows = pieces
    rows = shard.shape[0]
    out = jnp.zeros((inputs.shape[0], shard.shape[1]), jnp.float32)
    remote_inputs = inputs if full_rows else rotate_rows(inputs, 1)
    for piece, block in held:
        part = jnp.dot(remote_inputs, block, preferred_element_type=jnp.float32)
        out = lax.dynamic_update_slice_in_dim(out, part, piece * width, axis=1)
    if full_rows:
        return out
    local_inputs = lax.dynamic_slice_in_dim(inputs, lax.axis_index("plane") * rows, rows, axis=1)
    return jnp.dot(local_inputs, shard, preferred_element_type=jnp.float32) + out


def assemble(pieces):
    shard, held, width, full_rows = pieces
    remote = jnp.zeros((held[0][1].shape[0], width * len(held)), shard.dtype)
    for piece, block in held:
        remote = lax.dynamic_update_slice_in_dim(remote, block, piece * width, axis=1)
    return shard, remote, full_rows


def project_whole(inputs, weights):
    shard, remote, full_rows = weights
    if full_rows:
        return jnp.dot(inputs, remote, preferred_element_type=jnp.float32)
    rows = shard.shape[0]
    local_inputs = lax.dynamic_slice_in_dim(inputs, lax.axis_index("plane") * rows, rows, axis=1)
    local = jnp.dot(local_inputs, shard, preferred_element_type=jnp.float32)
    return local + jnp.dot(rotate_rows(inputs, 1), remote, preferred_element_type=jnp.float32)


def attend_items(pieces):
    packed_all, flags_all = pieces
    seq_len = packed_all.shape[2]
    block_len = 512
    score_scale = 1.0 / math.sqrt(HEAD_DIM)
    key_index = jnp.arange(seq_len, dtype=jnp.int32)

    def one_item(item_pair):
        packed, key_flag = item_pair
        key_rows = packed[:, HEAD_DIM : 2 * HEAD_DIM]
        value_rows = packed[:, 2 * HEAD_DIM :]
        key_alive = key_flag > 0.5
        query_blocks = packed[:, :HEAD_DIM].reshape(seq_len // block_len, block_len, HEAD_DIM)
        block_starts = jnp.arange(seq_len // block_len, dtype=jnp.int32) * block_len

        def one_block(block_pair):
            query_rows, offset = block_pair
            scores = (
                jnp.einsum("qd,kd->qk", query_rows, key_rows, preferred_element_type=jnp.float32)
                * score_scale
            )
            own_index = offset + jnp.arange(block_len, dtype=jnp.int32)
            allowed = key_alive[None, :] | (key_index[None, :] == own_index[:, None])
            attention = masked_softmax(scores, allowed)
            return jnp.dot(attention, value_rows, preferred_element_type=jnp.float32).astype(
                jnp.bfloat16
            )

        return lax.map(one_block, (query_blocks, block_starts)).reshape(seq_len, HEAD_DIM)

    return lax.map(one_item, (packed_all[0], flags_all[0]))[None]


def attend_by_section(projected, counts, plane_count):
    sec_block, tok_block = projected.shape[0], projected.shape[1]
    share = HEADS // plane_count
    seq_len = plane_count * tok_block
    score_scale = 1.0 / math.sqrt(HEAD_DIM)
    key_index = jnp.arange(seq_len, dtype=jnp.int32)
    contexts = []
    for local in range(sec_block):
        section = lax.axis_index("sec") * sec_block + local
        key_alive = key_index < lax.dynamic_index_in_dim(counts, section, keepdims=False)
        outgoing = jnp.transpose(
            projected[local].reshape(tok_block, 3, plane_count, share, HEAD_DIM), (2, 3, 0, 1, 4)
        ).reshape(plane_count, share, tok_block, 3 * HEAD_DIM)
        packed = lax.all_to_all(outgoing, "plane", split_axis=0, concat_axis=2, tiled=True)[0]
        queries = packed[:, :, :HEAD_DIM]
        keys = packed[:, :, HEAD_DIM : 2 * HEAD_DIM]
        values = packed[:, :, 2 * HEAD_DIM :]
        scores = (
            jnp.einsum("nqd,nkd->nqk", queries, keys, preferred_element_type=jnp.float32)
            * score_scale
        )
        allowed = key_alive[None, None, :] | (key_index[None, None, :] == key_index[None, :, None])
        attention = masked_softmax(scores, allowed)
        context = jnp.einsum(
            "nqk,nkd->nqd", attention, values, preferred_element_type=jnp.float32
        ).astype(jnp.bfloat16)
        homeward = jnp.transpose(
            context.reshape(share, plane_count, tok_block, HEAD_DIM), (1, 0, 2, 3)
        )
        returned = lax.all_to_all(homeward, "plane", split_axis=0, concat_axis=1, tiled=True)[0]
        contexts.append(jnp.transpose(returned, (1, 0, 2)).reshape(tok_block, HEADS * HEAD_DIM))
    return contexts


def body(tokens, counts, region_ids, norm_gains, cross_qkv, cross_out, plane_qkv, plane_out):
    sec_block, tok_block, model_width = tokens.shape
    plane_count = lax.axis_size("plane")
    regions = 2 * lax.axis_size("sec") * plane_count
    positions = lax.axis_index("plane") * tok_block + jnp.arange(tok_block, dtype=jnp.int32)
    padded_counts = jnp.concatenate(
        [jnp.zeros((1,), jnp.int32), counts, jnp.zeros((1,), jnp.int32)]
    )
    near_counts = lax.dynamic_slice_in_dim(
        padded_counts, lax.axis_index("sec") * sec_block, sec_block + 2
    )
    near_valid = positions[None, :] < near_counts[:, None]
    own_valid = near_valid[1 : sec_block + 1]
    score_scale = 1.0 / math.sqrt(HEAD_DIM)
    cross_qkv_pieces, cross_out_pieces = gather_pieces([cross_qkv, cross_out], full_rows=True)
    plane_qkv_pieces, plane_out_pieces = gather_pieces(
        [plane_qkv, plane_out], swap_first=True, full_rows=True
    )
    cross_out_pieces = assemble(cross_out_pieces)
    plane_out_pieces = assemble(plane_out_pieces)
    normed = rms_norm(tokens, norm_gains[0])
    inputs = normed.reshape(-1, model_width)
    result = project(inputs, cross_qkv_pieces)
    projected = result.astype(jnp.bfloat16).reshape(sec_block, tok_block, 3 * model_width)
    own_kv = projected[:, :, model_width:]
    from_below = shifted_2(own_kv[sec_block - 1], "sec", 1)
    from_above = shifted_2(own_kv[0], "sec", -1)
    near_kv = jnp.concatenate([from_below[None], own_kv, from_above[None]], axis=0)
    queries = projected[:, :, :model_width]
    windows = tok_block // WINDOW
    query_win = queries.reshape(sec_block, windows, WINDOW, HEADS, HEAD_DIM)
    pair_win = near_kv.reshape(sec_block + 2, windows, WINDOW, 2, HEADS, HEAD_DIM)
    stacked = jnp.concatenate(
        [pair_win[0:sec_block], pair_win[1 : sec_block + 1], pair_win[2 : sec_block + 2]], axis=2
    )
    valid_win = near_valid.reshape(sec_block + 2, windows, WINDOW)
    valid_three = jnp.concatenate(
        [valid_win[0:sec_block], valid_win[1 : sec_block + 1], valid_win[2 : sec_block + 2]], axis=2
    )
    itself = jnp.arange(3 * WINDOW)[None, :] == jnp.arange(WINDOW)[:, None] + WINDOW
    scores = (
        jnp.einsum(
            "snqhd,snkhd->snhqk", query_win, stacked[:, :, :, 0], preferred_element_type=jnp.float32
        )
        * score_scale
    )
    allowed = valid_three[:, :, None, None, :] | itself[None, None, None]
    attention = masked_softmax(scores, allowed)
    context = jnp.einsum(
        "snhqk,snkhd->snqhd", attention, stacked[:, :, :, 1], preferred_element_type=jnp.float32
    )
    context = context.astype(jnp.bfloat16).reshape(-1, model_width)
    result = project_whole(context, cross_out_pieces)
    after_cross = (tokens.reshape(-1, model_width).astype(jnp.float32) + result).astype(
        jnp.bfloat16
    )
    normed = rms_norm(after_cross, norm_gains[1])
    result = project(normed, plane_qkv_pieces)
    projected = result.astype(jnp.bfloat16).reshape(sec_block, tok_block, 3, HEADS, HEAD_DIM)
    if HEADS % plane_count == 0:
        contexts = attend_by_section(projected, counts, plane_count)
    else:
        per_device = sec_block * HEADS // plane_count
        heads_first = jnp.transpose(projected, (0, 3, 1, 2, 4)).reshape(
            plane_count, per_device, tok_block, 3 * HEAD_DIM
        )
        key_flags = jnp.broadcast_to(own_valid[:, None, :], (sec_block, HEADS, tok_block)).astype(
            jnp.bfloat16
        )
        key_flags = key_flags.reshape(plane_count, per_device, tok_block)
        attended = attend_items(
            (
                lax.all_to_all(heads_first, "plane", split_axis=0, concat_axis=2, tiled=True),
                lax.all_to_all(key_flags, "plane", split_axis=0, concat_axis=2, tiled=True),
            )
        )
        returned = lax.all_to_all(attended, "plane", split_axis=2, concat_axis=0, tiled=True)
        contexts = [
            jnp.transpose(
                returned.reshape(sec_block, HEADS, tok_block, HEAD_DIM), (0, 2, 1, 3)
            ).reshape(-1, model_width)
        ]
    labels = region_ids.reshape(-1)
    member = (jnp.arange(regions, dtype=jnp.int32)[:, None] == labels[None, :]) & own_valid.reshape(
        -1
    )[None, :]
    member = member.astype(jnp.bfloat16)
    pieces_out = []
    partial = None
    row = 0
    for context in contexts:
        span = context.shape[0]
        result = project_whole(context, plane_out_pieces)
        piece = (after_cross[row : row + span].astype(jnp.float32) + result).astype(jnp.bfloat16)
        pieces_out.append(piece)
        extended = jnp.concatenate([piece, jnp.ones((span, 128), jnp.bfloat16)], axis=1)
        term = jnp.dot(member[:, row : row + span], extended, preferred_element_type=jnp.float32)
        partial = term if partial is None else partial + term
        row += span
    encoded = jnp.concatenate(pieces_out, axis=0)
    sections = lax.axis_size("sec")
    width = partial.shape[1]
    partial = partial.reshape(sections, plane_count, 2, width)
    me_plane = lax.axis_index("plane")
    gathered = lax.dynamic_index_in_dim(partial, me_plane, axis=1, keepdims=False)
    for step in range(1, plane_count):
        moved = [(i, (i + step) % plane_count) for i in range(plane_count)]
        target = lax.rem(me_plane + step, plane_count)
        block = lax.dynamic_index_in_dim(partial, target, axis=1, keepdims=False)
        gathered = gathered + lax.ppermute(block, "plane", moved)
    me_sec = lax.axis_index("sec")
    totals = lax.dynamic_index_in_dim(gathered, me_sec, axis=0, keepdims=False)
    for step in range(1, sections):
        moved = [(i, (i + step) % sections) for i in range(sections)]
        target = lax.rem(me_sec + step, sections)
        block = lax.dynamic_index_in_dim(gathered, target, axis=0, keepdims=False)
        totals = totals + lax.ppermute(block, "sec", moved)
    counted = totals[:, model_width]
    pooled = totals[:, :model_width] / jnp.maximum(counted, 1.0)[:, None]
    return (encoded.reshape(sec_block, tok_block, model_width), pooled)


def solution(mesh):
    in_specs = (
        P(("groups", "sec"), "plane", None),
        P("groups"),
        P(("groups", "sec"), "plane"),
        P(),
        P("plane", None),
        P("plane", None),
        P("plane", None),
        P("plane", None),
    )
    out_specs = (P(("groups", "sec"), "plane", None), P(("groups", "sec", "plane"), None))
    return jax.shard_map(body, mesh=mesh, in_specs=in_specs, out_specs=out_specs, check_vma=False)
```
